128 devices in a mesh: req: 8 (over x, core), kv: 16 (over y, z).
Axes of the slice: x: 4, y: 4, z: 4, core: 2. Of those that a mesh axis runs over, the one named last changes fastest.
Arguments:
- x_steps: bfloat16 [4, 1024, 1536], P(None, ('req', 'kv')), may hold values from -6 to 6
- lengths: int32 [128], replicated, may hold values from 16 to 8192
- perm: int32 [128], replicated, may hold values from 0 to 127, as said below
- parents: int32 [4, 1024], replicated, may hold values from 0 to 7
- table: int32 [1024, 9], P(('req', 'kv')), may hold values from 0 to 9215, as said below
- pool: bfloat16 [9216, 128, 256], P(('req', 'kv')), may hold values from -900 to 900
- norm_attn: float32 [1536], replicated, may hold values from 0.1 to 1.9
- w_query: bfloat16 [1536, 1536], replicated, may hold values from -0.15625 to 0.15625
- w_keyval: bfloat16 [1536, 256], replicated, may hold values from -0.15625 to 0.15625
- w_out: bfloat16 [1536, 1536], replicated, may hold values from -0.15625 to 0.15625
- norm_mlp: float32 [1536], replicated, may hold values from 0.1 to 1.9
- w_gate: bfloat16 [1536, 4608], P(None, 'kv'), may hold values from -0.15625 to 0.15625
- w_up: bfloat16 [1536, 4608], P(None, 'kv'), may hold values from -0.15625 to 0.15625
- w_down: bfloat16 [4608, 1536], P('kv'), may hold values from -0.09375 to 0.09375
Outputs:
- outputs: bfloat16 [4, 1024, 1536], P(None, ('req', 'kv'))
The draws below stay inside these ranges and needn't reach their ends.
Inputs may be any that keep to these rules, and one draw needn't show every extreme that they name: perm is a permutation with perm[s] % 16 == s % 16; among the 8 slots s with one s // 16 and one s % 16 // 8, every req index occurs as perm[s] // 16 exactly once. The entries of row b lie in [(b // 8) * 72, (b // 8 + 1) * 72); no page appears twice in the table.
All inputs are finite; a program needn't handle non-finite values.
Results may differ from the reference program's by a relative error of at most 0.02.
Values may be sent and summed in bfloat16 or wider, within the bound.
No kernel may reach another device: no remote copies, remote signals or barrier semaphores. Data moves between devices by JAX's collectives and lax.ppermute only.
A program may use at most 192 MiB of HBM per device.

```python
import jax
import jax.numpy as jnp
from jax import lax

D = 1536
HEADS = 12
HEAD_DIM = 128
FF = 4608
WINDOW = 1024
PAGE = 128
BEAMS = 8
STEPS = 4
LMAX = 8192
RQH = 8
WPAGES = 9
RQ = 16
REQS = 128
ROWS = 1024
PAGES_DEV = 72
PAGES = 9216
N_REQ = 8
N_KV = 16


def draw_lengths(key, part):
    choose_key, short_key, long_key, marked_key = jax.random.split(key, 4)
    chosen = jax.random.randint(choose_key, (REQS,), 0, 2)
    short_len = jax.random.randint(short_key, (REQS,), 16, WINDOW)
    long_len = jax.random.randint(long_key, (REQS,), WINDOW, LMAX + 1)
    values = jnp.where(chosen == 1, long_len, short_len)
    marked = jax.random.randint(marked_key, (), 0, REQS)
    values = values.at[marked].set(LMAX)
    values = values.at[(marked + 1) % REQS].set(16)
    return values.astype(jnp.int32)


def draw_perm(key, part):
    halves = N_KV // BEAMS
    per_group = RQH * halves
    half_keys = jax.random.split(key, halves)
    shifts = jax.vmap(lambda one_key: jax.random.permutation(one_key, jnp.arange(RQH, dtype=jnp.int32) % N_REQ))(half_keys)
    shifts = shifts.reshape(per_group)
    groups = jnp.arange(N_REQ, dtype=jnp.int32)
    offsets = jnp.arange(per_group, dtype=jnp.int32)
    values = (groups[:, None] + shifts[None, :]) % N_REQ * per_group + offsets[None, :]
    return values.reshape(N_REQ * per_group).astype(jnp.int32)


def draw_table(key, part):
    device_count = N_REQ * N_KV
    device_keys = jax.random.split(key, device_count)
    shuffled = jax.vmap(lambda one_key: jax.random.permutation(one_key, PAGES_DEV))(device_keys)
    owner = jnp.arange(device_count, dtype=jnp.int32)[:, None] * PAGES_DEV
    return (owner + shuffled.astype(jnp.int32)).reshape(device_count * RQH, WPAGES).astype(jnp.int32)


def draw_pool(key, part):
    base_key = jax.random.fold_in(key, 0)
    values = jnp.clip(jax.random.normal(base_key, (PAGES, PAGE // 2, 2, 2 * HEAD_DIM), jnp.float32), -6.0, 6.0)
    return values.reshape(PAGES, PAGE, 2 * HEAD_DIM).astype(jnp.bfloat16)


def place_ends(drawn, key, low, largest):
    spot = [jax.random.randint(jax.random.fold_in(key, axis), (), 0, length) for axis, length in enumerate(drawn.shape)]
    widest = drawn.shape.index(max(drawn.shape))
    next_to = spot[:widest] + [(spot[widest] + 1) % drawn.shape[widest]] + spot[widest + 1:]
    return drawn.at[tuple(spot)].set(low).at[tuple(next_to)].set(largest)


def level_of(stream_key, shape, shards, least, largest):
    factor_of = 1.0
    for position, shards_of in shards:
        heights = jax.random.uniform(jax.random.fold_in(jax.random.fold_in(stream_key, 6), position), (shards_of,), jnp.float32, least / len(shards), largest / len(shards))
        factor_of = factor_of * jnp.repeat(jnp.exp(heights), shape[position] // shards_of).reshape((-1,) + (1,) * (len(shape) - 1 - position))
    return factor_of


def noise(own_key, shape, deviation, reach, pieces=(), kind=jnp.bfloat16):
    values = jax.random.normal(own_key, shape, jnp.float32) * deviation
    if len(pieces) > 0:
        values = level_of(own_key, shape, pieces, -0.22, 0.18) * values
    return jnp.clip(values, min=-reach, max=reach).astype(kind)


def setup_inputs(seed: int = 0) -> dict:
    streams_of = jax.random.split(jax.random.key(seed), 15)
    x_steps = noise(streams_of[0], (STEPS, ROWS, D), 1.0, 6.0, ((1, 128),))
    lengths = draw_lengths(jax.random.fold_in(streams_of[14], 71), 0)
    perm = draw_perm(jax.random.fold_in(streams_of[14], 71), 0)
    parents = place_ends(jax.random.randint(streams_of[3], (STEPS, ROWS), 0, BEAMS), jax.random.fold_in(streams_of[3], 1), 0, BEAMS - 1).astype(jnp.int32)
    table = draw_table(jax.random.fold_in(streams_of[14], 71), 0)
    pool = draw_pool(jax.random.fold_in(streams_of[14], 71), 0)
    norm_attn = jnp.clip(1.0 + 0.18 * jax.random.normal(streams_of[6], (D,), jnp.float32), 0.1, 1.9)
    w_query = noise(streams_of[7], (D, HEADS * HEAD_DIM), D ** -0.5, 0.15625)
    w_keyval = noise(streams_of[8], (D, 2 * HEAD_DIM), D ** -0.5, 0.15625)
    w_out = noise(streams_of[9], (HEADS * HEAD_DIM, D), (HEADS * HEAD_DIM) ** -0.5, 0.15625)
    norm_mlp = jnp.clip(1.0 + 0.18 * jax.random.normal(streams_of[10], (D,), jnp.float32), 0.1, 1.9)
    w_gate = noise(streams_of[11], (D, FF), D ** -0.5, 0.15625, ((1, 16),))
    w_up = noise(streams_of[12], (D, FF), D ** -0.5, 0.15625, ((1, 16),))
    w_down = noise(streams_of[13], (FF, D), FF ** -0.5, 0.09375, ((0, 16),))
    return {"x_steps": x_steps, "lengths": lengths, "perm": perm, "parents": parents, "table": table, "pool": pool, "norm_attn": norm_attn, "w_query": w_query, "w_keyval": w_keyval, "w_out": w_out, "norm_mlp": norm_mlp, "w_gate": w_gate, "w_up": w_up, "w_down": w_down}


EPSILON = 1e-06
NEGATIVE = -1e+30

def member_of(beam_index, half_index, halves):
    return beam_index % 2 + 2 * half_index + 2 * halves * (beam_index // 2)

def rms_round(values, gain):
    wide = values.astype(jnp.float32)
    mean_square = lax.optimization_barrier(jnp.mean(wide * wide, axis=-1, keepdims=True))
    return (wide * lax.rsqrt(mean_square + EPSILON) * gain).astype(jnp.bfloat16)

def page_partial(queries, pages, key_pos, length, step_index):
    head_dim = queries.shape[-1]
    keys = pages[:, :, :head_dim].astype(jnp.float32)
    values = pages[:, :, head_dim:].astype(jnp.float32)
    scores = jnp.einsum('rhd,rkd->rhk', queries.astype(jnp.float32), keys) * head_dim ** (-0.5)
    allowed = (key_pos < length[:, None]) & (key_pos > length[:, None] + step_index - WINDOW)
    scores = jnp.where(allowed[:, None, :], scores, NEGATIVE)
    highest = lax.optimization_barrier(jnp.max(scores, axis=-1))
    weights = jnp.exp(scores - highest[..., None]).astype(jnp.bfloat16)
    totals = lax.optimization_barrier(jnp.sum(weights.astype(jnp.float32), axis=-1))
    weighted = jnp.einsum('rhk,rkd->rhd', weights.astype(jnp.float32), values)
    return (highest, totals, weighted)

def fresh_partial(queries, entries, count):
    head_dim = queries.shape[-1]
    keys = entries[:, :count, :head_dim].astype(jnp.float32)
    values = entries[:, :count, head_dim:].astype(jnp.float32)
    scores = jnp.einsum('rhd,rkd->rhk', queries.astype(jnp.float32), keys) * head_dim ** (-0.5)
    highest = lax.optimization_barrier(jnp.max(scores, axis=-1))
    weights = jnp.exp(scores - highest[..., None]).astype(jnp.bfloat16)
    totals = lax.optimization_barrier(jnp.sum(weights.astype(jnp.float32), axis=-1))
    weighted = jnp.einsum('rhk,rkd->rhd', weights.astype(jnp.float32), values)
    return (highest, totals, weighted)

def join_parts(first, second):
    highest = jnp.maximum(first[0], second[0])
    scale_first = jnp.exp(first[0] - highest)
    scale_second = jnp.exp(second[0] - highest)
    totals = first[1] * scale_first + second[1] * scale_second
    weighted = first[2] * scale_first[..., None] + second[2] * scale_second[..., None]
    return (highest, totals, weighted)

def feed_forward(mlp_in, w_gate, w_up, w_down):
    gate = jnp.dot(mlp_in, w_gate, preferred_element_type=jnp.float32)
    upward = jnp.dot(mlp_in, w_up, preferred_element_type=jnp.float32)
    hidden = (jax.nn.gelu(gate, approximate=True) * upward).astype(jnp.bfloat16)
    return jnp.dot(hidden, w_down, preferred_element_type=jnp.float32)

def reference(x_steps, lengths, perm, parents, table, pool, norm_attn, w_query, w_keyval, w_out, norm_mlp, w_gate, w_up, w_down):
    steps, total_rows, width = x_steps.shape
    head_dim = pool.shape[2] // 2
    heads = w_query.shape[1] // head_dim
    span = table.shape[1] * PAGE
    halves = N_KV // BEAMS
    row_ids = jnp.arange(total_rows, dtype=jnp.int32)
    column = row_ids // RQH
    offset = row_ids % RQH
    member = column % N_KV
    part_of = member // 2 % halves
    beam = member % 2 + 2 * (member // (2 * halves))
    slot = (column // N_KV * halves + part_of) * RQH + offset
    request = perm[slot]
    arrival = (request // RQ * N_KV + member_of(beam, request % RQ // RQH, halves)) * RQH + request % RQH
    inputs = x_steps[:, arrival]
    length = lengths[request]
    first_page = jnp.maximum(length - WINDOW + 1, 0) // PAGE
    key_pos = first_page[:, None] * PAGE + jnp.arange(span, dtype=jnp.int32)[None, :]
    base_columns = column - member
    cache_row = row_ids
    recent = jnp.zeros((total_rows, steps, 2 * head_dim), jnp.bfloat16)
    blocks = total_rows // RQH
    results = []
    for step_index in range(steps):
        parent_rows = (base_columns + member_of(parents[step_index], part_of, halves)) * RQH + offset
        cache_row = cache_row[parent_rows]
        recent = recent[parent_rows]
        current = inputs[step_index]
        normed = rms_round(current, norm_attn)
        query = jnp.dot(normed, w_query, preferred_element_type=jnp.float32).astype(jnp.bfloat16)
        fresh = jnp.dot(normed, w_keyval, preferred_element_type=jnp.float32).astype(jnp.bfloat16)
        recent = recent.at[:, step_index].set(fresh)
        queries = query.reshape(total_rows, heads, head_dim)

        def one_block(packed, step_index=step_index):
            block_queries, block_rows, block_pos, block_length = packed
            block_pages = pool[table[block_rows]].reshape(RQH, span, 2 * head_dim)
            return page_partial(block_queries, block_pages, block_pos, block_length, step_index)
        page = lax.map(one_block, (queries.reshape(blocks, RQH, heads, head_dim), cache_row.reshape(blocks, RQH), key_pos.reshape(blocks, RQH, span), length.reshape(blocks, RQH)))
        page = tuple((part.reshape((total_rows,) + part.shape[2:]) for part in page))
        joined = join_parts(page, fresh_partial(queries, recent, step_index + 1))
        attended = (joined[2] / joined[1][..., None]).astype(jnp.bfloat16).reshape(total_rows, heads * head_dim)
        residual = (current.astype(jnp.float32) + jnp.dot(attended, w_out, preferred_element_type=jnp.float32)).astype(jnp.bfloat16)
        summed = feed_forward(rms_round(residual, norm_mlp), w_gate, w_up, w_down)
        results.append((residual.astype(jnp.float32) + summed).astype(jnp.bfloat16))
    stacked = jnp.stack(results)
    return jnp.zeros_like(stacked).at[:, arrival].set(stacked)
```

```python
import jax
import jax.numpy as jnp
from jax import lax
from jax.sharding import PartitionSpec as P

WINDOW = 1024
PAGE = 128
BEAMS = 8


EPSILON = 1e-06
NEGATIVE = -1e30


def member_of(beam_index, half_index, halves):
    return beam_index % 2 + 2 * half_index + 2 * halves * (beam_index // 2)


def rms_round(values, gain):
    wide = values.astype(jnp.float32)
    mean_square = jnp.mean(wide * wide, axis=-1, keepdims=True)
    return (wide * lax.rsqrt(mean_square + EPSILON) * gain).astype(jnp.bfloat16)


def rank_within(labels, offsets):
    earlier = (labels[None, :] == labels[:, None]) & (offsets[None, :] < offsets[:, None])
    return jnp.sum(earlier.astype(jnp.int32), axis=1)


def follow(index, table):
    picks = index[:, None, :] == jnp.arange(BEAMS, dtype=jnp.int32)[None, :, None]
    return jnp.sum(jnp.where(picks, table[None, :, :], 0), axis=1)


def pick_rows(index, table):
    picks = index[:, None, :] == jnp.arange(BEAMS, dtype=jnp.int32)[None, :, None]
    return jnp.sum(jnp.where(picks[..., None], table[None, :, :, :], 0), axis=1).astype(table.dtype)


def on_device(
    x_steps,
    lengths,
    perm,
    parents,
    table,
    pool,
    norm_attn,
    w_query,
    w_keyval,
    w_out,
    norm_mlp,
    w_gate,
    w_up,
    w_down,
):
    steps, rows, width = x_steps.shape
    head_dim = pool.shape[2] // 2
    heads = w_query.shape[1] // head_dim
    qwidth = heads * head_dim
    span = table.shape[1] * pool.shape[1]
    req_count = lax.axis_size("req")
    kv_count = lax.axis_size("kv")
    group = lax.axis_index("req")
    member = lax.axis_index("kv")
    halves = kv_count // BEAMS
    half = member // 2 % halves
    beam = member % 2 + 2 * (member // (2 * halves))
    per_group = halves * rows
    group_rows = kv_count * rows
    quota = rows // req_count

    offsets = jnp.arange(rows, dtype=jnp.int32)
    slot_ids = group * per_group + half * rows + offsets
    placed = lax.dynamic_slice_in_dim(perm.reshape(req_count, per_group), half * rows, rows, 1)
    serving = lax.dynamic_index_in_dim(placed, group, 0, keepdims=False)
    target = jnp.sum(
        jnp.where(placed == slot_ids[None, :], jnp.arange(req_count, dtype=jnp.int32)[:, None], 0),
        axis=0,
    )
    anchor = serving // per_group
    send_order = jnp.argsort(target * rows + offsets)
    outgoing = x_steps[:, send_order].reshape(steps, req_count, quota, width)
    arrived = lax.all_to_all(outgoing, "req", split_axis=1, concat_axis=1, tiled=True).reshape(
        steps, rows, width
    )
    inputs = arrived[:, anchor * quota + rank_within(anchor, offsets)]

    normed = rms_round(inputs.reshape(steps * rows, width), norm_attn)
    query = jnp.dot(normed, w_query, preferred_element_type=jnp.float32).astype(jnp.bfloat16)
    fresh = jnp.dot(normed, w_keyval, preferred_element_type=jnp.float32).astype(jnp.bfloat16)
    packed = jnp.concatenate([query, fresh], axis=-1).reshape(steps, rows, qwidth + 2 * head_dim)
    gathered = lax.all_gather(packed, "kv", axis=0)
    mine = gathered.reshape((BEAMS // 2, halves, 2) + packed.shape)
    mine = lax.dynamic_index_in_dim(mine, half, 1, keepdims=False).reshape((BEAMS,) + packed.shape)
    queries = mine[..., :qwidth].reshape(BEAMS, steps, rows, heads, head_dim)
    entries = mine[..., qwidth:]

    family = lax.dynamic_slice_in_dim(parents, group * group_rows, group_rows, 1).reshape(
        (steps, BEAMS // 2, halves, 2, rows)
    )
    family = lax.dynamic_index_in_dim(family, half, 2, keepdims=False).reshape(steps, BEAMS, rows)
    own = jnp.broadcast_to(jnp.arange(BEAMS, dtype=jnp.int32)[:, None], (BEAMS, rows))
    cache_beam = own
    sources = []
    cache_beams = []
    listed = []
    for step_index in range(steps):
        cache_beam = follow(family[step_index], cache_beam)
        sources = [follow(family[step_index], source) for source in sources] + [own]
        cache_beams.append(cache_beam)
        picked = [pick_rows(source, entries[:, s]) for s, source in enumerate(sources)]
        picked += [jnp.zeros_like(picked[0])] * (steps - 1 - step_index)
        listed.append(jnp.stack(picked))
    held = jnp.stack(cache_beams, axis=1) == beam
    listed = jnp.stack(listed)

    length = lengths[serving]
    first_page = jnp.maximum(length - WINDOW + 1, 0) // PAGE
    key_pos = first_page[:, None] * PAGE + jnp.arange(span, dtype=jnp.int32)[None, :]
    device = group * kv_count + member
    pages = pool[table - device * pool.shape[0]].reshape(rows, span, 2 * head_dim)
    keys = pages[:, :, :head_dim]
    values = pages[:, :, head_dim:]
    scale = head_dim ** (-0.5)
    scores = jnp.einsum(
        "jtrhd,rkd->jtrhk", queries, keys, preferred_element_type=jnp.float32
    ) * scale
    step_ids = jnp.arange(steps, dtype=jnp.int32)
    allowed = (key_pos[None, :, :] < length[None, :, None]) & (
        key_pos[None, :, :] > length[None, :, None] + step_ids[:, None, None] - WINDOW
    )
    scores = jnp.where(allowed[None, :, :, None, :], scores, NEGATIVE)
    high_c = jnp.max(scores, axis=-1)
    weights = jnp.exp(scores - high_c[..., None]).astype(jnp.bfloat16)
    total_c = jnp.sum(weights.astype(jnp.float32), axis=-1)
    sum_c = jnp.einsum("jtrhk,rkd->jtrhd", weights, values, preferred_element_type=jnp.float32)

    new_keys = listed[..., :head_dim]
    new_values = listed[..., head_dim:]
    fresh_scores = jnp.einsum(
        "jtrhd,tsjrd->jtrhs", queries, new_keys, preferred_element_type=jnp.float32
    ) * scale
    counted = step_ids[None, :] <= step_ids[:, None]
    fresh_scores = jnp.where(counted[None, :, None, None, :], fresh_scores, NEGATIVE)
    high_n = jnp.max(fresh_scores, axis=-1)
    fresh_weights = jnp.exp(fresh_scores - high_n[..., None]).astype(jnp.bfloat16)
    fresh_weights = jnp.where(counted[None, :, None, None, :], fresh_weights, 0)
    total_n = jnp.sum(fresh_weights.astype(jnp.float32), axis=-1)
    sum_n = jnp.einsum(
        "jtrhs,tsjrd->jtrhd", fresh_weights, new_values, preferred_element_type=jnp.float32
    )

    highest = jnp.maximum(high_c, high_n)
    scale_c = jnp.exp(high_c - highest)
    scale_n = jnp.exp(high_n - highest)
    totals = total_c * scale_c + total_n * scale_n
    weighted = sum_c * scale_c[..., None] + sum_n * scale_n[..., None]
    attended = (weighted / totals[..., None]).astype(jnp.bfloat16).reshape(
        BEAMS, steps, rows, qwidth
    )
    attended = jnp.where(held[..., None], attended, jnp.zeros_like(attended))

    spread = attended.reshape(BEAMS // 2, 1, 2, steps, rows, qwidth)
    in_half = (jnp.arange(halves, dtype=jnp.int32) == half)[None, :, None, None, None, None]
    outgoing_att = jnp.where(in_half, spread, jnp.zeros_like(spread)).reshape(
        kv_count, steps, rows, qwidth
    )
    received = lax.all_to_all(outgoing_att, "kv", split_axis=0, concat_axis=0, tiled=True)
    attended_own = jnp.sum(received.astype(jnp.float32), axis=0).astype(jnp.bfloat16)

    current = inputs.reshape(steps * rows, width)
    residual = (
        current.astype(jnp.float32)
        + jnp.dot(attended_own.reshape(steps * rows, qwidth), w_out, preferred_element_type=jnp.float32)
    ).astype(jnp.bfloat16)
    mlp_in = lax.all_gather(rms_round(residual, norm_mlp), "kv", axis=0, tiled=True)
    gate = jnp.dot(mlp_in, w_gate, preferred_element_type=jnp.float32)
    upward = jnp.dot(mlp_in, w_up, preferred_element_type=jnp.float32)
    hidden = (jax.nn.gelu(gate, approximate=True) * upward).astype(jnp.bfloat16)
    terms = jnp.dot(hidden, w_down, preferred_element_type=jnp.float32).astype(jnp.bfloat16)
    terms = terms.reshape(kv_count, steps * rows, width)
    partial = lax.all_to_all(terms, "kv", split_axis=0, concat_axis=0, tiled=True)
    summed = jnp.sum(partial.astype(jnp.float32), axis=0)
    finished = (residual.astype(jnp.float32) + summed).astype(jnp.bfloat16).reshape(
        steps, rows, width
    )

    back_order = jnp.argsort(anchor * rows + offsets)
    leaving = finished[:, back_order].reshape(steps, req_count, quota, width)
    returned = lax.all_to_all(leaving, "req", split_axis=1, concat_axis=1, tiled=True).reshape(
        steps, rows, width
    )
    return returned[:, target * quota + rank_within(target, offsets)]


def solution(mesh):
    in_specs = (
        P(None, ("req", "kv"), None),
        P(),
        P(),
        P(),
        P(("req", "kv"), None),
        P(("req", "kv"), None, None),
        P(),
        P(),
        P(),
        P(),
        P(),
        P(None, "kv"),
        P(None, "kv"),
        P("kv", None),
    )
    out_specs = P(None, ("req", "kv"), None)
    return jax.shard_map(
        on_device, mesh=mesh, in_specs=in_specs, out_specs=out_specs, check_vma=False
    )
```

```python
import jax
import jax.numpy as jnp
from jax import lax
from jax.sharding import PartitionSpec as P

WINDOW = 1024
PAGE = 128
BEAMS = 8


EPSILON = 1e-06
NEGATIVE = -1e30


def member_of(beam_index, half_index, halves):
    return beam_index % 2 + 2 * half_index + 2 * halves * (beam_index // 2)


def rms_round(values, gain):
    wide = values.astype(jnp.float32)
    mean_square = jnp.mean(wide * wide, axis=-1, keepdims=True)
    return (wide * lax.rsqrt(mean_square + EPSILON) * gain).astype(jnp.bfloat16)


def rank_within(labels, offsets):
    earlier = (labels[None, :] == labels[:, None]) & (offsets[None, :] < offsets[:, None])
    return jnp.sum(earlier.astype(jnp.int32), axis=1)


def follow(index, table):
    picks = index[:, None, :] == jnp.arange(BEAMS, dtype=jnp.int32)[None, :, None]
    return jnp.sum(jnp.where(picks, table[None, :, :], 0), axis=1)


def pick_rows(index, table):
    picks = index[:, None, :] == jnp.arange(BEAMS, dtype=jnp.int32)[None, :, None]
    return jnp.sum(jnp.where(picks[..., None], table[None, :, :, :], 0), axis=1).astype(table.dtype)


def on_device(
    x_steps,
    lengths,
    perm,
    parents,
    table,
    pool,
    norm_attn,
    w_query,
    w_keyval,
    w_out,
    norm_mlp,
    w_gate,
    w_up,
    w_down,
):
    steps, rows, width = x_steps.shape
    head_dim = pool.shape[2] // 2
    heads = w_query.shape[1] // head_dim
    qwidth = heads * head_dim
    span = table.shape[1] * pool.shape[1]
    req_count = lax.axis_size("req")
    kv_count = lax.axis_size("kv")
    group = lax.axis_index("req")
    member = lax.axis_index("kv")
    halves = kv_count // BEAMS
    half = member // 2 % halves
    beam = member % 2 + 2 * (member // (2 * halves))
    per_group = halves * rows
    group_rows = kv_count * rows
    quota = rows // req_count

    offsets = jnp.arange(rows, dtype=jnp.int32)
    slot_ids = group * per_group + half * rows + offsets
    placed = lax.dynamic_slice_in_dim(perm.reshape(req_count, per_group), half * rows, rows, 1)
    serving = lax.dynamic_index_in_dim(placed, group, 0, keepdims=False)
    target = jnp.sum(
        jnp.where(placed == slot_ids[None, :], jnp.arange(req_count, dtype=jnp.int32)[:, None], 0),
        axis=0,
    )
    anchor = serving // per_group
    send_order = jnp.argsort(target * rows + offsets)
    outgoing = x_steps[:, send_order].reshape(steps, req_count, quota, width)
    arrived = lax.all_to_all(outgoing, "req", split_axis=1, concat_axis=1, tiled=True).reshape(
        steps, rows, width
    )
    inputs = arrived[:, anchor * quota + rank_within(anchor, offsets)]

    normed = rms_round(inputs.reshape(steps * rows, width), norm_attn)
    query = jnp.dot(normed, w_query, preferred_element_type=jnp.float32).astype(jnp.bfloat16)
    fresh = jnp.dot(normed, w_keyval, preferred_element_type=jnp.float32).astype(jnp.bfloat16)
    packed = jnp.concatenate([query, fresh], axis=-1).reshape(steps, rows, qwidth + 2 * head_dim)
    gathered = lax.all_to_all(
        jnp.broadcast_to(packed[None], (kv_count,) + packed.shape), "kv", 0, 0, tiled=True
    )
    mine = gathered.reshape((BEAMS // 2, halves, 2) + packed.shape)
    mine = lax.dynamic_index_in_dim(mine, half, 1, keepdims=False).reshape((BEAMS,) + packed.shape)
    queries = mine[..., :qwidth].reshape(BEAMS, steps, rows, heads, head_dim)
    entries = mine[..., qwidth:]

    family = lax.dynamic_slice_in_dim(parents, group * group_rows, group_rows, 1).reshape(
        (steps, BEAMS // 2, halves, 2, rows)
    )
    family = lax.dynamic_index_in_dim(family, half, 2, keepdims=False).reshape(steps, BEAMS, rows)
    own = jnp.broadcast_to(jnp.arange(BEAMS, dtype=jnp.int32)[:, None], (BEAMS, rows))
    cache_beam = own
    sources = []
    cache_beams = []
    listed = []
    for step_index in range(steps):
        cache_beam = follow(family[step_index], cache_beam)
        sources = [follow(family[step_index], source) for source in sources] + [own]
        cache_beams.append(cache_beam)
        picked = [pick_rows(source, entries[:, s]) for s, source in enumerate(sources)]
        picked += [jnp.zeros_like(picked[0])] * (steps - 1 - step_index)
        listed.append(jnp.stack(picked))
    held = jnp.stack(cache_beams, axis=1) == beam
    listed = jnp.stack(listed)

    length = lengths[serving]
    first_page = jnp.maximum(length - WINDOW + 1, 0) // PAGE
    key_pos = first_page[:, None] * PAGE + jnp.arange(span, dtype=jnp.int32)[None, :]
    device = group * kv_count + member
    pages = pool[table - device * pool.shape[0]].reshape(rows, span, 2 * head_dim)
    keys = pages[:, :, :head_dim]
    values = pages[:, :, head_dim:]
    scale = head_dim ** (-0.5)
    scores = jnp.einsum(
        "jtrhd,rkd->jtrhk", queries, keys, preferred_element_type=jnp.float32
    ) * scale
    step_ids = jnp.arange(steps, dtype=jnp.int32)
    allowed = (key_pos[None, :, :] < length[None, :, None]) & (
        key_pos[None, :, :] > length[None, :, None] + step_ids[:, None, None] - WINDOW
    )
    scores = jnp.where(allowed[None, :, :, None, :], scores, NEGATIVE)
    high_c = jnp.max(scores, axis=-1)
    weights = jnp.exp(scores - high_c[..., None]).astype(jnp.bfloat16)
    total_c = jnp.sum(weights.astype(jnp.float32), axis=-1)
    sum_c = jnp.einsum("jtrhk,rkd->jtrhd", weights, values, preferred_element_type=jnp.float32)

    new_keys = listed[..., :head_dim]
    new_values = listed[..., head_dim:]
    fresh_scores = jnp.einsum(
        "jtrhd,tsjrd->jtrhs", queries, new_keys, preferred_element_type=jnp.float32
    ) * scale
    counted = step_ids[None, :] <= step_ids[:, None]
    fresh_scores = jnp.where(counted[None, :, None, None, :], fresh_scores, NEGATIVE)
    high_n = jnp.max(fresh_scores, axis=-1)
    fresh_weights = jnp.exp(fresh_scores - high_n[..., None]).astype(jnp.bfloat16)
    fresh_weights = jnp.where(counted[None, :, None, None, :], fresh_weights, 0)
    total_n = jnp.sum(fresh_weights.astype(jnp.float32), axis=-1)
    sum_n = jnp.einsum(
        "jtrhs,tsjrd->jtrhd", fresh_weights, new_values, preferred_element_type=jnp.float32
    )

    highest = jnp.maximum(high_c, high_n)
    scale_c = jnp.exp(high_c - highest)
    scale_n = jnp.exp(high_n - highest)
    totals = total_c * scale_c + total_n * scale_n
    weighted = sum_c * scale_c[..., None] + sum_n * scale_n[..., None]
    attended = (weighted / totals[..., None]).astype(jnp.bfloat16).reshape(
        BEAMS, steps, rows, qwidth
    )
    attended = jnp.where(held[..., None], attended, jnp.zeros_like(attended))

    spread = attended.reshape(BEAMS // 2, 1, 2, steps, rows, qwidth)
    in_half = (jnp.arange(halves, dtype=jnp.int32) == half)[None, :, None, None, None, None]
    outgoing_att = jnp.where(in_half, spread, jnp.zeros_like(spread)).reshape(
        kv_count, steps, rows, qwidth
    )
    received = lax.all_to_all(outgoing_att, "kv", split_axis=0, concat_axis=0, tiled=True)
    attended_own = jnp.sum(received.astype(jnp.float32), axis=0).astype(jnp.bfloat16)

    current = inputs.reshape(steps * rows, width)
    residual = (
        current.astype(jnp.float32)
        + jnp.dot(attended_own.reshape(steps * rows, qwidth), w_out, preferred_element_type=jnp.float32)
    ).astype(jnp.bfloat16)
    mlp_own = rms_round(residual, norm_mlp)
    mlp_in = lax.all_to_all(
        jnp.broadcast_to(mlp_own[None], (kv_count,) + mlp_own.shape), "kv", 0, 0, tiled=True
    ).reshape(kv_count * steps * rows, width)
    gate = jnp.dot(mlp_in, w_gate, preferred_element_type=jnp.float32)
    upward = jnp.dot(mlp_in, w_up, preferred_element_type=jnp.float32)
    hidden = (jax.nn.gelu(gate, approximate=True) * upward).astype(jnp.bfloat16)
    terms = jnp.dot(hidden, w_down, preferred_element_type=jnp.float32)
    terms = terms.reshape(kv_count, steps, rows, width)
    is_own = (jnp.arange(kv_count, dtype=jnp.int32) == member)[:, None, None, None]
    terms = terms + jnp.where(is_own, residual.astype(jnp.float32).reshape(steps, rows, width)[None], 0.0)
    terms = terms.astype(jnp.bfloat16)

    slot_req = perm.reshape(req_count, halves, rows) // (halves * rows)
    mine_req = lax.dynamic_index_in_dim(slot_req, group, 0, keepdims=False)
    member_half = jnp.arange(kv_count, dtype=jnp.int32) // 2 % halves
    req_ids = jnp.arange(req_count, dtype=jnp.int32)
    row_of = mine_req[member_half]
    choose = row_of[:, None, :] == req_ids[None, :, None]
    leaving = jnp.sum(
        jnp.where(choose[:, :, None, :, None], terms[:, None].astype(jnp.float32), 0.0), axis=3
    ).astype(jnp.bfloat16)
    leaving = jnp.swapaxes(leaving, 0, 1).reshape(req_count * kv_count, steps, width)
    arrived_sums = lax.all_to_all(leaving, ("req", "kv"), 0, 0, tiled=True).reshape(
        req_count, kv_count, steps, width
    )
    per_group_sum = jnp.sum(arrived_sums.astype(jnp.float32), axis=1)
    served_by = slot_req[:, half, :] == group
    finished = jnp.sum(
        jnp.where(served_by[:, None, :, None], per_group_sum[:, :, None, :], 0.0), axis=0
    )
    return finished.astype(jnp.bfloat16)


def solution(mesh):
    in_specs = (
        P(None, ("req", "kv"), None),
        P(),
        P(),
        P(),
        P(("req", "kv"), None),
        P(("req", "kv"), None, None),
        P(),
        P(),
        P(),
        P(),
        P(),
        P(None, "kv"),
        P(None, "kv"),
        P("kv", None),
    )
    out_specs = P(None, ("req", "kv"), None)
    return jax.shard_map(
        on_device, mesh=mesh, in_specs=in_specs, out_specs=out_specs, check_vma=False
    )
```

```python
import jax
import jax.numpy as jnp
from jax import lax
from jax.sharding import PartitionSpec as P

WINDOW = 1024
PAGE = 128
BEAMS = 8


EPSILON = 1e-06
NEGATIVE = -1e30


def member_of(beam_index, half_index, halves):
    return beam_index % 2 + 2 * half_index + 2 * halves * (beam_index // 2)


def rms_round(values, gain):
    wide = values.astype(jnp.float32)
    mean_square = jnp.mean(wide * wide, axis=-1, keepdims=True)
    return (wide * lax.rsqrt(mean_square + EPSILON) * gain).astype(jnp.bfloat16)


def rank_within(labels, offsets):
    earlier = (labels[None, :] == labels[:, None]) & (offsets[None, :] < offsets[:, None])
    return jnp.sum(earlier.astype(jnp.int32), axis=1)


def follow(index, table):
    picks = index[:, None, :] == jnp.arange(BEAMS, dtype=jnp.int32)[None, :, None]
    return jnp.sum(jnp.where(picks, table[None, :, :], 0), axis=1)


def pick_rows(index, table):
    picks = index[:, None, :] == jnp.arange(BEAMS, dtype=jnp.int32)[None, :, None]
    return jnp.sum(jnp.where(picks[..., None], table[None, :, :, :], 0), axis=1).astype(table.dtype)


def on_device(
    x_steps,
    lengths,
    perm,
    parents,
    table,
    pool,
    norm_attn,
    w_query,
    w_keyval,
    w_out,
    norm_mlp,
    w_gate,
    w_up,
    w_down,
):
    steps, rows, width = x_steps.shape
    head_dim = pool.shape[2] // 2
    heads = w_query.shape[1] // head_dim
    qwidth = heads * head_dim
    span = table.shape[1] * pool.shape[1]
    req_count = lax.axis_size("req")
    kv_count = lax.axis_size("kv")
    group = lax.axis_index("req")
    member = lax.axis_index("kv")
    halves = kv_count // BEAMS
    half = member // 2 % halves
    beam = member % 2 + 2 * (member // (2 * halves))
    per_group = halves * rows
    group_rows = kv_count * rows
    quota = rows // req_count

    offsets = jnp.arange(rows, dtype=jnp.int32)
    slot_ids = group * per_group + half * rows + offsets
    placed = lax.dynamic_slice_in_dim(perm.reshape(req_count, per_group), half * rows, rows, 1)
    serving = lax.dynamic_index_in_dim(placed, group, 0, keepdims=False)
    target = jnp.sum(
        jnp.where(placed == slot_ids[None, :], jnp.arange(req_count, dtype=jnp.int32)[:, None], 0),
        axis=0,
    )
    anchor = serving // per_group
    send_order = jnp.argsort(target * rows + offsets)
    outgoing = x_steps[:, send_order].reshape(steps, req_count, quota, width)
    arrived = lax.all_to_all(outgoing, "req", split_axis=1, concat_axis=1, tiled=True).reshape(
        steps, rows, width
    )
    slot_req = perm.reshape(req_count, halves, rows) // (halves * rows)
    mine_req = slot_req[:, half, :][group]
    offset_of = jnp.sum(
        jnp.where(mine_req[None, :] == offsets[:, None], offsets[None, :], 0), axis=1
    )
    inputs = arrived

    normed = rms_round(inputs.reshape(steps * rows, width), norm_attn)
    query = jnp.dot(normed, w_query, preferred_element_type=jnp.float32).astype(jnp.bfloat16)
    fresh = jnp.dot(normed, w_keyval, preferred_element_type=jnp.float32).astype(jnp.bfloat16)
    packed = jnp.concatenate([query, fresh], axis=-1).reshape(steps, rows, qwidth + 2 * head_dim)
    gathered = lax.all_to_all(
        jnp.broadcast_to(packed[None], (kv_count,) + packed.shape), "kv", 0, 0, tiled=True
    )
    mine = gathered.reshape((BEAMS // 2, halves, 2) + packed.shape)
    mine = lax.dynamic_index_in_dim(mine, half, 1, keepdims=False).reshape((BEAMS,) + packed.shape)
    queries = mine[..., :qwidth].reshape(BEAMS, steps, rows, heads, head_dim)
    entries = mine[..., qwidth:]

    family = lax.dynamic_slice_in_dim(parents, group * group_rows, group_rows, 1).reshape(
        (steps, BEAMS // 2, halves, 2, rows)
    )
    family = lax.dynamic_index_in_dim(family, half, 2, keepdims=False).reshape(steps, BEAMS, rows)
    family = family[:, :, offset_of]
    own = jnp.broadcast_to(jnp.arange(BEAMS, dtype=jnp.int32)[:, None], (BEAMS, rows))
    cache_beam = own
    sources = []
    cache_beams = []
    listed = []
    for step_index in range(steps):
        cache_beam = follow(family[step_index], cache_beam)
        sources = [follow(family[step_index], source) for source in sources] + [own]
        cache_beams.append(cache_beam)
        picked = [pick_rows(source, entries[:, s]) for s, source in enumerate(sources)]
        picked += [jnp.zeros_like(picked[0])] * (steps - 1 - step_index)
        listed.append(jnp.stack(picked))
    held = jnp.stack(cache_beams, axis=1) == beam
    listed = jnp.stack(listed)

    length = lengths[serving[offset_of]]
    first_page = jnp.maximum(length - WINDOW + 1, 0) // PAGE
    key_pos = first_page[:, None] * PAGE + jnp.arange(span, dtype=jnp.int32)[None, :]
    device = group * kv_count + member
    pages = pool[table[offset_of] - device * pool.shape[0]].reshape(rows, span, 2 * head_dim)
    keys = pages[:, :, :head_dim]
    values = pages[:, :, head_dim:]
    scale = head_dim ** (-0.5)
    scores = jnp.einsum(
        "jtrhd,rkd->jtrhk", queries, keys, preferred_element_type=jnp.float32
    ) * scale
    step_ids = jnp.arange(steps, dtype=jnp.int32)
    allowed = (key_pos[None, :, :] < length[None, :, None]) & (
        key_pos[None, :, :] > length[None, :, None] + step_ids[:, None, None] - WINDOW
    )
    scores = jnp.where(allowed[None, :, :, None, :], scores, NEGATIVE)
    high_c = jnp.max(scores, axis=-1)
    weights = jnp.exp(scores - high_c[..., None]).astype(jnp.bfloat16)
    total_c = jnp.sum(weights.astype(jnp.float32), axis=-1)
    sum_c = jnp.einsum("jtrhk,rkd->jtrhd", weights, values, preferred_element_type=jnp.float32)

    new_keys = listed[..., :head_dim]
    new_values = listed[..., head_dim:]
    fresh_scores = jnp.einsum(
        "jtrhd,tsjrd->jtrhs", queries, new_keys, preferred_element_type=jnp.float32
    ) * scale
    counted = step_ids[None, :] <= step_ids[:, None]
    fresh_scores = jnp.where(counted[None, :, None, None, :], fresh_scores, NEGATIVE)
    high_n = jnp.max(fresh_scores, axis=-1)
    fresh_weights = jnp.exp(fresh_scores - high_n[..., None]).astype(jnp.bfloat16)
    fresh_weights = jnp.where(counted[None, :, None, None, :], fresh_weights, 0)
    total_n = jnp.sum(fresh_weights.astype(jnp.float32), axis=-1)
    sum_n = jnp.einsum(
        "jtrhs,tsjrd->jtrhd", fresh_weights, new_values, preferred_element_type=jnp.float32
    )

    highest = jnp.maximum(high_c, high_n)
    scale_c = jnp.exp(high_c - highest)
    scale_n = jnp.exp(high_n - highest)
    totals = total_c * scale_c + total_n * scale_n
    weighted = sum_c * scale_c[..., None] + sum_n * scale_n[..., None]
    attended = (weighted / totals[..., None]).astype(jnp.bfloat16).reshape(
        BEAMS, steps, rows, qwidth
    )
    attended = jnp.where(held[..., None], attended, jnp.zeros_like(attended))

    spread = attended.reshape(BEAMS // 2, 1, 2, steps, rows, qwidth)
    in_half = (jnp.arange(halves, dtype=jnp.int32) == half)[None, :, None, None, None, None]
    outgoing_att = jnp.where(in_half, spread, jnp.zeros_like(spread)).reshape(
        kv_count, steps, rows, qwidth
    )
    received = lax.all_to_all(outgoing_att, "kv", split_axis=0, concat_axis=0, tiled=True)
    attended_own = jnp.sum(received.astype(jnp.float32), axis=0).astype(jnp.bfloat16)

    current = inputs.reshape(steps * rows, width)
    residual = (
        current.astype(jnp.float32)
        + jnp.dot(attended_own.reshape(steps * rows, qwidth), w_out, preferred_element_type=jnp.float32)
    ).astype(jnp.bfloat16)
    mlp_own = rms_round(residual, norm_mlp)
    mlp_in = lax.all_to_all(
        jnp.broadcast_to(mlp_own[None], (kv_count,) + mlp_own.shape), "kv", 0, 0, tiled=True
    ).reshape(kv_count * steps * rows, width)
    gate = jnp.dot(mlp_in, w_gate, preferred_element_type=jnp.float32)
    upward = jnp.dot(mlp_in, w_up, preferred_element_type=jnp.float32)
    hidden = (jax.nn.gelu(gate, approximate=True) * upward).astype(jnp.bfloat16)
    terms = jnp.dot(hidden, w_down, preferred_element_type=jnp.float32)
    terms = terms.reshape(kv_count, steps, rows, width)
    is_own = (jnp.arange(kv_count, dtype=jnp.int32) == member)[:, None, None, None]
    terms = terms + jnp.where(is_own, residual.astype(jnp.float32).reshape(steps, rows, width)[None], 0.0)
    terms = terms.astype(jnp.bfloat16)

    leaving = jnp.transpose(terms, (2, 0, 1, 3)).reshape(req_count * kv_count, steps, width)
    arrived_sums = lax.all_to_all(leaving, ("req", "kv"), 0, 0, tiled=True).reshape(
        req_count, kv_count, steps, width
    )
    per_group_sum = jnp.sum(arrived_sums.astype(jnp.float32), axis=1)
    served_by = slot_req[:, half, :] == group
    finished = jnp.sum(
        jnp.where(served_by[:, None, :, None], per_group_sum[:, :, None, :], 0.0), axis=0
    )
    return finished.astype(jnp.bfloat16)


def solution(mesh):
    in_specs = (
        P(None, ("req", "kv"), None),
        P(),
        P(),
        P(),
        P(("req", "kv"), None),
        P(("req", "kv"), None, None),
        P(),
        P(),
        P(),
        P(),
        P(),
        P(None, "kv"),
        P(None, "kv"),
        P("kv", None),
    )
    out_specs = P(None, ("req", "kv"), None)
    return jax.shard_map(
        on_device, mesh=mesh, in_specs=in_specs, out_specs=out_specs, check_vma=False
    )
```

```python
import jax
import jax.numpy as jnp
from jax import lax
from jax.sharding import PartitionSpec as P
from jax.experimental import pallas as pl
from jax.experimental.pallas import tpu as pltpu

WINDOW = 1024
PAGE = 128
BEAMS = 8


EPSILON = 1e-06
NEGATIVE = -1e30


def member_of(beam_index, half_index, halves):
    return beam_index % 2 + 2 * half_index + 2 * halves * (beam_index // 2)


def rms_round(values, gain):
    wide = values.astype(jnp.float32)
    mean_square = jnp.mean(wide * wide, axis=-1, keepdims=True)
    return (wide * lax.rsqrt(mean_square + EPSILON) * gain).astype(jnp.bfloat16)


def rank_within(labels, offsets):
    earlier = (labels[None, :] == labels[:, None]) & (offsets[None, :] < offsets[:, None])
    return jnp.sum(earlier.astype(jnp.int32), axis=1)


def follow(index, table):
    picks = index[:, None, :] == jnp.arange(BEAMS, dtype=jnp.int32)[None, :, None]
    return jnp.sum(jnp.where(picks, table[None, :, :], 0), axis=1)


def pick_rows(index, table):
    picks = index[:, None, :] == jnp.arange(BEAMS, dtype=jnp.int32)[None, :, None]
    return jnp.sum(jnp.where(picks[..., None], table[None, :, :, :], 0), axis=1).astype(table.dtype)


def cache_kernel(bounds_ref, q_ref, kv_ref, high_ref, total_ref, sum_ref):
    r = pl.program_id(0)
    steps = q_ref.shape[1]
    head_dim = q_ref.shape[3]
    keys = kv_ref[0, :, :head_dim]
    values = kv_ref[0, :, head_dim:]
    pos = lax.broadcasted_iota(jnp.int32, (1, kv_ref.shape[1]), 1)
    for t in range(steps):
        lo = bounds_ref[(r * steps + t) * 2]
        hi = bounds_ref[(r * steps + t) * 2 + 1]
        scores = lax.dot_general(
            q_ref[0, t], keys, (((1,), (1,)), ((), ())), preferred_element_type=jnp.float32
        ) * (head_dim ** (-0.5))
        allowed = (pos > lo) & (pos < hi)
        scores = jnp.where(allowed, scores, NEGATIVE)
        high = jnp.max(scores, axis=1, keepdims=True)
        weights = jnp.exp(scores - high).astype(jnp.bfloat16)
        high_ref[0, t] = high
        total_ref[0, t] = jnp.sum(weights.astype(jnp.float32), axis=1, keepdims=True)
        sum_ref[0, t] = jnp.dot(weights, values, preferred_element_type=jnp.float32)


def cache_part(bounds, queries, pages):
    rows, steps, count, head_dim = queries.shape
    span = pages.shape[1]
    flops = 4 * rows * steps * count * span * head_dim
    return pl.pallas_call(
        cache_kernel,
        grid_spec=pltpu.PrefetchScalarGridSpec(
            num_scalar_prefetch=1,
            grid=(rows,),
            in_specs=[
                pl.BlockSpec((1, steps, count, head_dim), lambda r, b: (r, 0, 0, 0)),
                pl.BlockSpec((1, span, pages.shape[2]), lambda r, b: (r, 0, 0)),
            ],
            out_specs=[
                pl.BlockSpec((1, steps, count, 1), lambda r, b: (r, 0, 0, 0)),
                pl.BlockSpec((1, steps, count, 1), lambda r, b: (r, 0, 0, 0)),
                pl.BlockSpec((1, steps, count, head_dim), lambda r, b: (r, 0, 0, 0)),
            ],
        ),
        out_shape=[
            jax.ShapeDtypeStruct((rows, steps, count, 1), jnp.float32),
            jax.ShapeDtypeStruct((rows, steps, count, 1), jnp.float32),
            jax.ShapeDtypeStruct((rows, steps, count, head_dim), jnp.float32),
        ],
        cost_estimate=pl.CostEstimate(
            flops=flops,
            transcendentals=rows * steps * count * span,
            bytes_accessed=pages.size * 2 + queries.size * 2 + rows * steps * count * (head_dim + 2) * 4,
        ),
    )(bounds, queries, pages)


def on_device(
    x_steps,
    lengths,
    perm,
    parents,
    table,
    pool,
    norm_attn,
    w_query,
    w_keyval,
    w_out,
    norm_mlp,
    w_gate,
    w_up,
    w_down,
):
    steps, rows, width = x_steps.shape
    head_dim = pool.shape[2] // 2
    heads = w_query.shape[1] // head_dim
    qwidth = heads * head_dim
    span = table.shape[1] * pool.shape[1]
    req_count = lax.axis_size("req")
    kv_count = lax.axis_size("kv")
    group = lax.axis_index("req")
    member = lax.axis_index("kv")
    halves = kv_count // BEAMS
    half = member // 2 % halves
    beam = member % 2 + 2 * (member // (2 * halves))
    per_group = halves * rows
    group_rows = kv_count * rows
    quota = rows // req_count

    offsets = jnp.arange(rows, dtype=jnp.int32)
    slot_ids = group * per_group + half * rows + offsets
    placed = lax.dynamic_slice_in_dim(perm.reshape(req_count, per_group), half * rows, rows, 1)
    serving = lax.dynamic_index_in_dim(placed, group, 0, keepdims=False)
    target = jnp.sum(
        jnp.where(placed == slot_ids[None, :], jnp.arange(req_count, dtype=jnp.int32)[:, None], 0),
        axis=0,
    )
    anchor = serving // per_group
    send_order = jnp.argsort(target * rows + offsets)
    outgoing = x_steps[:, send_order].reshape(steps, req_count, quota, width)
    arrived = lax.all_to_all(outgoing, "req", split_axis=1, concat_axis=1, tiled=True).reshape(
        steps, rows, width
    )
    slot_req = perm.reshape(req_count, halves, rows) // (halves * rows)
    mine_req = slot_req[:, half, :][group]
    offset_of = jnp.sum(
        jnp.where(mine_req[None, :] == offsets[:, None], offsets[None, :], 0), axis=1
    )
    inputs = arrived

    normed = rms_round(inputs.reshape(steps * rows, width), norm_attn)
    query = jnp.dot(normed, w_query, preferred_element_type=jnp.float32).astype(jnp.bfloat16)
    fresh = jnp.dot(normed, w_keyval, preferred_element_type=jnp.float32).astype(jnp.bfloat16)
    packed = jnp.concatenate([query, fresh], axis=-1).reshape(steps, rows, qwidth + 2 * head_dim)
    gathered = lax.all_to_all(
        jnp.broadcast_to(packed[None], (kv_count,) + packed.shape), "kv", 0, 0, tiled=True
    )
    mine = gathered.reshape((BEAMS // 2, halves, 2) + packed.shape)
    mine = lax.dynamic_index_in_dim(mine, half, 1, keepdims=False).reshape((BEAMS,) + packed.shape)
    queries = mine[..., :qwidth].reshape(BEAMS, steps, rows, heads, head_dim)
    entries = mine[..., qwidth:]

    family = lax.dynamic_slice_in_dim(parents, group * group_rows, group_rows, 1).reshape(
        (steps, BEAMS // 2, halves, 2, rows)
    )
    family = lax.dynamic_index_in_dim(family, half, 2, keepdims=False).reshape(steps, BEAMS, rows)
    family = family[:, :, offset_of]
    own = jnp.broadcast_to(jnp.arange(BEAMS, dtype=jnp.int32)[:, None], (BEAMS, rows))
    cache_beam = own
    sources = []
    cache_beams = []
    listed = []
    for step_index in range(steps):
        cache_beam = follow(family[step_index], cache_beam)
        sources = [follow(family[step_index], source) for source in sources] + [own]
        cache_beams.append(cache_beam)
        picked = [pick_rows(source, entries[:, s]) for s, source in enumerate(sources)]
        picked += [jnp.zeros_like(picked[0])] * (steps - 1 - step_index)
        listed.append(jnp.stack(picked))
    held = jnp.stack(cache_beams, axis=1) == beam
    listed = jnp.stack(listed)

    length = lengths[serving[offset_of]]
    first_page = jnp.maximum(length - WINDOW + 1, 0) // PAGE
    device = group * kv_count + member
    pages = pool[table[offset_of] - device * pool.shape[0]].reshape(rows, span, 2 * head_dim)
    scale = head_dim ** (-0.5)
    step_ids = jnp.arange(steps, dtype=jnp.int32)
    base = first_page * PAGE
    lo = length[:, None] + step_ids[None, :] - WINDOW - base[:, None]
    hi = jnp.broadcast_to((length - base)[:, None], (rows, steps))
    bounds = jnp.stack([lo, hi], axis=-1).reshape(rows * steps * 2)
    by_row = jnp.transpose(queries, (2, 1, 0, 3, 4)).reshape(rows, steps, BEAMS * heads, head_dim)
    high_c, total_c, sum_c = cache_part(bounds, by_row, pages)
    high_c = jnp.transpose(high_c.reshape(rows, steps, BEAMS, heads), (2, 1, 0, 3))
    total_c = jnp.transpose(total_c.reshape(rows, steps, BEAMS, heads), (2, 1, 0, 3))
    sum_c = jnp.transpose(sum_c.reshape(rows, steps, BEAMS, heads, head_dim), (2, 1, 0, 3, 4))

    new_keys = listed[..., :head_dim]
    new_values = listed[..., head_dim:]
    fresh_scores = jnp.einsum(
        "jtrhd,tsjrd->jtrhs", queries, new_keys, preferred_element_type=jnp.float32
    ) * scale
    counted = step_ids[None, :] <= step_ids[:, None]
    fresh_scores = jnp.where(counted[None, :, None, None, :], fresh_scores, NEGATIVE)
    high_n = jnp.max(fresh_scores, axis=-1)
    fresh_weights = jnp.exp(fresh_scores - high_n[..., None]).astype(jnp.bfloat16)
    fresh_weights = jnp.where(counted[None, :, None, None, :], fresh_weights, 0)
    total_n = jnp.sum(fresh_weights.astype(jnp.float32), axis=-1)
    sum_n = jnp.einsum(
        "jtrhs,tsjrd->jtrhd", fresh_weights, new_values, preferred_element_type=jnp.float32
    )

    highest = jnp.maximum(high_c, high_n)
    scale_c = jnp.exp(high_c - highest)
    scale_n = jnp.exp(high_n - highest)
    totals = total_c * scale_c + total_n * scale_n
    weighted = sum_c * scale_c[..., None] + sum_n * scale_n[..., None]
    attended = (weighted / totals[..., None]).astype(jnp.bfloat16).reshape(
        BEAMS, steps, rows, qwidth
    )
    attended = jnp.where(held[..., None], attended, jnp.zeros_like(attended))

    spread = attended.reshape(BEAMS // 2, 1, 2, steps, rows, qwidth)
    in_half = (jnp.arange(halves, dtype=jnp.int32) == half)[None, :, None, None, None, None]
    outgoing_att = jnp.where(in_half, spread, jnp.zeros_like(spread)).reshape(
        kv_count, steps, rows, qwidth
    )
    received = lax.all_to_all(outgoing_att, "kv", split_axis=0, concat_axis=0, tiled=True)
    attended_own = jnp.sum(received.astype(jnp.float32), axis=0).astype(jnp.bfloat16)

    current = inputs.reshape(steps * rows, width)
    residual = (
        current.astype(jnp.float32)
        + jnp.dot(attended_own.reshape(steps * rows, qwidth), w_out, preferred_element_type=jnp.float32)
    ).astype(jnp.bfloat16)
    mlp_own = rms_round(residual, norm_mlp)
    mlp_in = lax.all_to_all(
        jnp.broadcast_to(mlp_own[None], (kv_count,) + mlp_own.shape), "kv", 0, 0, tiled=True
    ).reshape(kv_count * steps * rows, width)
    gate = jnp.dot(mlp_in, w_gate, preferred_element_type=jnp.float32)
    upward = jnp.dot(mlp_in, w_up, preferred_element_type=jnp.float32)
    hidden = (jax.nn.gelu(gate, approximate=True) * upward).astype(jnp.bfloat16)
    terms = jnp.dot(hidden, w_down, preferred_element_type=jnp.float32)
    terms = terms.reshape(kv_count, steps, rows, width)
    is_own = (jnp.arange(kv_count, dtype=jnp.int32) == member)[:, None, None, None]
    terms = terms + jnp.where(is_own, residual.astype(jnp.float32).reshape(steps, rows, width)[None], 0.0)
    terms = terms.astype(jnp.bfloat16)

    leaving = jnp.transpose(terms, (2, 0, 1, 3)).reshape(req_count * kv_count, steps, width)
    arrived_sums = lax.all_to_all(leaving, ("req", "kv"), 0, 0, tiled=True).reshape(
        req_count, kv_count, steps, width
    )
    per_group_sum = jnp.sum(arrived_sums.astype(jnp.float32), axis=1)
    served_by = slot_req[:, half, :] == group
    finished = jnp.sum(
        jnp.where(served_by[:, None, :, None], per_group_sum[:, :, None, :], 0.0), axis=0
    )
    return finished.astype(jnp.bfloat16)


def solution(mesh):
    in_specs = (
        P(None, ("req", "kv"), None),
        P(),
        P(),
        P(),
        P(("req", "kv"), None),
        P(("req", "kv"), None, None),
        P(),
        P(),
        P(),
        P(),
        P(),
        P(None, "kv"),
        P(None, "kv"),
        P("kv", None),
    )
    out_specs = P(None, ("req", "kv"), None)
    return jax.shard_map(
        on_device, mesh=mesh, in_specs=in_specs, out_specs=out_specs, check_vma=False
    )
```

```python
import jax
import jax.numpy as jnp
from jax import lax
from jax.sharding import PartitionSpec as P
from jax.experimental import pallas as pl
from jax.experimental.pallas import tpu as pltpu

WINDOW = 1024
PAGE = 128
BEAMS = 8


EPSILON = 1e-06
NEGATIVE = -1e30


def member_of(beam_index, half_index, halves):
    return beam_index % 2 + 2 * half_index + 2 * halves * (beam_index // 2)


def rms_round(values, gain):
    wide = values.astype(jnp.float32)
    mean_square = jnp.mean(wide * wide, axis=-1, keepdims=True)
    return (wide * lax.rsqrt(mean_square + EPSILON) * gain).astype(jnp.bfloat16)


def rank_within(labels, offsets):
    earlier = (labels[None, :] == labels[:, None]) & (offsets[None, :] < offsets[:, None])
    return jnp.sum(earlier.astype(jnp.int32), axis=1)


def follow(index, table):
    picks = index[:, None, :] == jnp.arange(BEAMS, dtype=jnp.int32)[None, :, None]
    return jnp.sum(jnp.where(picks, table[None, :, :], 0), axis=1)


def pick_rows(index, table):
    picks = index[:, None, :] == jnp.arange(BEAMS, dtype=jnp.int32)[None, :, None]
    return jnp.sum(jnp.where(picks[..., None], table[None, :, :, :], 0), axis=1).astype(table.dtype)


def attend_kernel(bounds_ref, held_ref, q_ref, kv_ref, new_ref, out_ref):
    r = pl.program_id(0)
    steps = q_ref.shape[1]
    beams = q_ref.shape[2]
    head_dim = q_ref.shape[4]
    scale = head_dim ** (-0.5)
    keys = kv_ref[0, :, :head_dim]
    values = kv_ref[0, :, head_dim:]
    pos = lax.broadcasted_iota(jnp.int32, (1, kv_ref.shape[1]), 1)
    for t in range(steps):
        lo = bounds_ref[(r * steps + t) * 2]
        hi = bounds_ref[(r * steps + t) * 2 + 1]
        allowed = (pos > lo) & (pos < hi)

        def one_beam(j, carry, t=t, allowed=allowed):
            flag = held_ref[(r * steps + t) * beams + j]

            @pl.when(flag != 0)
            def _():
                query = q_ref[0, t, j]
                scores = lax.dot_general(
                    query, keys, (((1,), (1,)), ((), ())), preferred_element_type=jnp.float32
                ) * scale
                scores = jnp.where(allowed, scores, NEGATIVE)
                high_c = jnp.max(scores, axis=1, keepdims=True)
                weights = jnp.exp(scores - high_c).astype(jnp.bfloat16)
                total_c = jnp.sum(weights.astype(jnp.float32), axis=1, keepdims=True)
                sum_c = jnp.dot(weights, values, preferred_element_type=jnp.float32)
                wide = query.astype(jnp.float32)
                entries = new_ref[0, t, j].astype(jnp.float32)
                fresh = [
                    jnp.sum(wide * entries[s : s + 1, :head_dim], axis=1, keepdims=True) * scale
                    for s in range(t + 1)
                ]
                high_n = fresh[0]
                for one in fresh[1:]:
                    high_n = jnp.maximum(high_n, one)
                fresh_w = [jnp.exp(one - high_n).astype(jnp.bfloat16).astype(jnp.float32) for one in fresh]
                total_n = fresh_w[0]
                sum_n = fresh_w[0] * entries[0:1, head_dim:]
                for s in range(1, t + 1):
                    total_n = total_n + fresh_w[s]
                    sum_n = sum_n + fresh_w[s] * entries[s : s + 1, head_dim:]
                highest = jnp.maximum(high_c, high_n)
                scale_c = jnp.exp(high_c - highest)
                scale_n = jnp.exp(high_n - highest)
                totals = total_c * scale_c + total_n * scale_n
                weighted = sum_c * scale_c + sum_n * scale_n
                out_ref[0, t, j] = (weighted / totals).astype(out_ref.dtype)

            @pl.when(flag == 0)
            def _():
                out_ref[0, t, j] = jnp.zeros(out_ref.shape[3:], out_ref.dtype)

            return carry

        lax.fori_loop(0, beams, one_beam, 0)


def attend(bounds, held, queries, pages, listed):
    rows, steps, beams, padded, head_dim = queries.shape
    span = pages.shape[1]
    flops = 4 * rows * steps * padded * span * head_dim
    return pl.pallas_call(
        attend_kernel,
        grid_spec=pltpu.PrefetchScalarGridSpec(
            num_scalar_prefetch=2,
            grid=(rows,),
            in_specs=[
                pl.BlockSpec((1, steps, beams, padded, head_dim), lambda r, b, h: (r, 0, 0, 0, 0)),
                pl.BlockSpec((1, span, pages.shape[2]), lambda r, b, h: (r, 0, 0)),
                pl.BlockSpec((1,) + listed.shape[1:], lambda r, b, h: (r, 0, 0, 0, 0)),
            ],
            out_specs=pl.BlockSpec((1, steps, beams, padded, head_dim), lambda r, b, h: (r, 0, 0, 0, 0)),
        ),
        out_shape=jax.ShapeDtypeStruct(queries.shape, jnp.bfloat16),
        cost_estimate=pl.CostEstimate(
            flops=flops,
            transcendentals=rows * steps * padded * span,
            bytes_accessed=pages.size * 2 + queries.size * 4 + listed.size * 2,
        ),
    )(bounds, held, queries, pages, listed)


def on_device(
    x_steps,
    lengths,
    perm,
    parents,
    table,
    pool,
    norm_attn,
    w_query,
    w_keyval,
    w_out,
    norm_mlp,
    w_gate,
    w_up,
    w_down,
):
    steps, rows, width = x_steps.shape
    head_dim = pool.shape[2] // 2
    heads = w_query.shape[1] // head_dim
    qwidth = heads * head_dim
    span = table.shape[1] * pool.shape[1]
    req_count = lax.axis_size("req")
    kv_count = lax.axis_size("kv")
    group = lax.axis_index("req")
    member = lax.axis_index("kv")
    halves = kv_count // BEAMS
    half = member // 2 % halves
    beam = member % 2 + 2 * (member // (2 * halves))
    per_group = halves * rows
    group_rows = kv_count * rows
    quota = rows // req_count

    offsets = jnp.arange(rows, dtype=jnp.int32)
    slot_ids = group * per_group + half * rows + offsets
    placed = lax.dynamic_slice_in_dim(perm.reshape(req_count, per_group), half * rows, rows, 1)
    serving = lax.dynamic_index_in_dim(placed, group, 0, keepdims=False)
    target = jnp.sum(
        jnp.where(placed == slot_ids[None, :], jnp.arange(req_count, dtype=jnp.int32)[:, None], 0),
        axis=0,
    )
    anchor = serving // per_group
    send_order = jnp.argsort(target * rows + offsets)
    outgoing = x_steps[:, send_order].reshape(steps, req_count, quota, width)
    arrived = lax.all_to_all(outgoing, "req", split_axis=1, concat_axis=1, tiled=True).reshape(
        steps, rows, width
    )
    slot_req = perm.reshape(req_count, halves, rows) // (halves * rows)
    mine_req = slot_req[:, half, :][group]
    offset_of = jnp.sum(
        jnp.where(mine_req[None, :] == offsets[:, None], offsets[None, :], 0), axis=1
    )
    inputs = arrived

    normed = rms_round(inputs.reshape(steps * rows, width), norm_attn)
    query = jnp.dot(normed, w_query, preferred_element_type=jnp.float32).astype(jnp.bfloat16)
    fresh = jnp.dot(normed, w_keyval, preferred_element_type=jnp.float32).astype(jnp.bfloat16)
    packed = jnp.concatenate([query, fresh], axis=-1).reshape(steps, rows, qwidth + 2 * head_dim)
    gathered = lax.all_to_all(
        jnp.broadcast_to(packed[None], (kv_count,) + packed.shape), "kv", 0, 0, tiled=True
    )
    mine = gathered.reshape((BEAMS // 2, halves, 2) + packed.shape)
    mine = lax.dynamic_index_in_dim(mine, half, 1, keepdims=False).reshape((BEAMS,) + packed.shape)
    queries = mine[..., :qwidth].reshape(BEAMS, steps, rows, heads, head_dim)
    entries = mine[..., qwidth:]

    family = lax.dynamic_slice_in_dim(parents, group * group_rows, group_rows, 1).reshape(
        (steps, BEAMS // 2, halves, 2, rows)
    )
    family = lax.dynamic_index_in_dim(family, half, 2, keepdims=False).reshape(steps, BEAMS, rows)
    family = family[:, :, offset_of]
    own = jnp.broadcast_to(jnp.arange(BEAMS, dtype=jnp.int32)[:, None], (BEAMS, rows))
    cache_beam = own
    sources = []
    cache_beams = []
    listed = []
    for step_index in range(steps):
        cache_beam = follow(family[step_index], cache_beam)
        sources = [follow(family[step_index], source) for source in sources] + [own]
        cache_beams.append(cache_beam)
        picked = [pick_rows(source, entries[:, s]) for s, source in enumerate(sources)]
        picked += [jnp.zeros_like(picked[0])] * (steps - 1 - step_index)
        listed.append(jnp.stack(picked))
    held = jnp.stack(cache_beams, axis=1) == beam
    listed = jnp.stack(listed)

    length = lengths[serving[offset_of]]
    first_page = jnp.maximum(length - WINDOW + 1, 0) // PAGE
    device = group * kv_count + member
    pages = pool[table[offset_of] - device * pool.shape[0]].reshape(rows, span, 2 * head_dim)
    scale = head_dim ** (-0.5)
    step_ids = jnp.arange(steps, dtype=jnp.int32)
    base = first_page * PAGE
    lo = length[:, None] + step_ids[None, :] - WINDOW - base[:, None]
    hi = jnp.broadcast_to((length - base)[:, None], (rows, steps))
    bounds = jnp.stack([lo, hi], axis=-1).reshape(rows * steps * 2)
    padded = jnp.pad(queries, ((0, 0), (0, 0), (0, 0), (0, 16 - heads), (0, 0)))
    by_row = jnp.transpose(padded, (2, 1, 0, 3, 4))
    held_flags = jnp.transpose(held, (2, 1, 0)).astype(jnp.int32).reshape(rows * steps * BEAMS)
    listed_by_row = jnp.transpose(listed, (3, 0, 2, 1, 4))
    attended = attend(bounds, held_flags, by_row, pages, listed_by_row)[:, :, :, :heads]
    attended = jnp.transpose(attended, (2, 1, 0, 3, 4)).reshape(BEAMS, steps, rows, qwidth)

    spread = attended.reshape(BEAMS // 2, 1, 2, steps, rows, qwidth)
    in_half = (jnp.arange(halves, dtype=jnp.int32) == half)[None, :, None, None, None, None]
    outgoing_att = jnp.where(in_half, spread, jnp.zeros_like(spread)).reshape(
        kv_count, steps, rows, qwidth
    )
    received = lax.all_to_all(outgoing_att, "kv", split_axis=0, concat_axis=0, tiled=True)
    attended_own = jnp.sum(received.astype(jnp.float32), axis=0).astype(jnp.bfloat16)

    current = inputs.reshape(steps * rows, width)
    residual = (
        current.astype(jnp.float32)
        + jnp.dot(attended_own.reshape(steps * rows, qwidth), w_out, preferred_element_type=jnp.float32)
    ).astype(jnp.bfloat16)
    mlp_own = rms_round(residual, norm_mlp)
    mlp_in = lax.all_to_all(
        jnp.broadcast_to(mlp_own[None], (kv_count,) + mlp_own.shape), "kv", 0, 0, tiled=True
    ).reshape(kv_count * steps * rows, width)
    gate = jnp.dot(mlp_in, w_gate, preferred_element_type=jnp.float32)
    upward = jnp.dot(mlp_in, w_up, preferred_element_type=jnp.float32)
    hidden = (jax.nn.gelu(gate, approximate=True) * upward).astype(jnp.bfloat16)
    terms = jnp.dot(hidden, w_down, preferred_element_type=jnp.float32)
    terms = terms.reshape(kv_count, steps, rows, width)
    is_own = (jnp.arange(kv_count, dtype=jnp.int32) == member)[:, None, None, None]
    terms = terms + jnp.where(is_own, residual.astype(jnp.float32).reshape(steps, rows, width)[None], 0.0)
    terms = terms.astype(jnp.bfloat16)

    leaving = jnp.transpose(terms, (2, 0, 1, 3)).reshape(req_count * kv_count, steps, width)
    arrived_sums = lax.all_to_all(leaving, ("req", "kv"), 0, 0, tiled=True).reshape(
        req_count, kv_count, steps, width
    )
    per_group_sum = jnp.sum(arrived_sums.astype(jnp.float32), axis=1)
    served_by = slot_req[:, half, :] == group
    finished = jnp.sum(
        jnp.where(served_by[:, None, :, None], per_group_sum[:, :, None, :], 0.0), axis=0
    )
    return finished.astype(jnp.bfloat16)


def solution(mesh):
    in_specs = (
        P(None, ("req", "kv"), None),
        P(),
        P(),
        P(),
        P(("req", "kv"), None),
        P(("req", "kv"), None, None),
        P(),
        P(),
        P(),
        P(),
        P(),
        P(None, "kv"),
        P(None, "kv"),
        P("kv", None),
    )
    out_specs = P(None, ("req", "kv"), None)
    return jax.shard_map(
        on_device, mesh=mesh, in_specs=in_specs, out_specs=out_specs, check_vma=False
    )
```

```python
import jax
import jax.numpy as jnp
from jax import lax
from jax.sharding import Mesh, PartitionSpec as P
from jax.experimental import pallas as pl
from jax.experimental.pallas import tpu as pltpu

WINDOW = 1024
PAGE = 128
BEAMS = 8


EPSILON = 1e-06
KV = ("y", "zhi", "zlo")
HALF = ("y", "zlo")
NEGATIVE = -1e30


def member_of(beam_index, half_index, halves):
    return beam_index % 2 + 2 * half_index + 2 * halves * (beam_index // 2)


def rms_round(values, gain):
    wide = values.astype(jnp.float32)
    mean_square = jnp.mean(wide * wide, axis=-1, keepdims=True)
    return (wide * lax.rsqrt(mean_square + EPSILON) * gain).astype(jnp.bfloat16)


def rank_within(labels, offsets):
    earlier = (labels[None, :] == labels[:, None]) & (offsets[None, :] < offsets[:, None])
    return jnp.sum(earlier.astype(jnp.int32), axis=1)


def follow(index, table):
    picks = index[:, None, :] == jnp.arange(BEAMS, dtype=jnp.int32)[None, :, None]
    return jnp.sum(jnp.where(picks, table[None, :, :], 0), axis=1)


def pick_rows(index, table):
    picks = index[:, None, :] == jnp.arange(BEAMS, dtype=jnp.int32)[None, :, None]
    return jnp.sum(jnp.where(picks[..., None], table[None, :, :, :], 0), axis=1).astype(table.dtype)


def cache_kernel(bounds_ref, q_ref, kv_ref, high_ref, total_ref, sum_ref):
    r = pl.program_id(0)
    steps = q_ref.shape[1]
    head_dim = q_ref.shape[3]
    keys = kv_ref[0, :, :head_dim]
    values = kv_ref[0, :, head_dim:]
    pos = lax.broadcasted_iota(jnp.int32, (1, kv_ref.shape[1]), 1)
    for t in range(steps):
        lo = bounds_ref[(r * steps + t) * 2]
        hi = bounds_ref[(r * steps + t) * 2 + 1]
        scores = lax.dot_general(
            q_ref[0, t], keys, (((1,), (1,)), ((), ())), preferred_element_type=jnp.float32
        ) * (head_dim ** (-0.5))
        allowed = (pos > lo) & (pos < hi)
        scores = jnp.where(allowed, scores, NEGATIVE)
        high = jnp.max(scores, axis=1, keepdims=True)
        weights = jnp.exp(scores - high).astype(jnp.bfloat16)
        high_ref[0, t] = high
        total_ref[0, t] = jnp.sum(weights.astype(jnp.float32), axis=1, keepdims=True)
        sum_ref[0, t] = jnp.dot(weights, values, preferred_element_type=jnp.float32)


def cache_part(bounds, queries, pages):
    rows, steps, count, head_dim = queries.shape
    span = pages.shape[1]
    flops = 4 * rows * steps * count * span * head_dim
    return pl.pallas_call(
        cache_kernel,
        grid_spec=pltpu.PrefetchScalarGridSpec(
            num_scalar_prefetch=1,
            grid=(rows,),
            in_specs=[
                pl.BlockSpec((1, steps, count, head_dim), lambda r, b: (r, 0, 0, 0)),
                pl.BlockSpec((1, span, pages.shape[2]), lambda r, b: (r, 0, 0)),
            ],
            out_specs=[
                pl.BlockSpec((1, steps, count, 1), lambda r, b: (r, 0, 0, 0)),
                pl.BlockSpec((1, steps, count, 1), lambda r, b: (r, 0, 0, 0)),
                pl.BlockSpec((1, steps, count, head_dim), lambda r, b: (r, 0, 0, 0)),
            ],
        ),
        out_shape=[
            jax.ShapeDtypeStruct((rows, steps, count, 1), jnp.float32),
            jax.ShapeDtypeStruct((rows, steps, count, 1), jnp.float32),
            jax.ShapeDtypeStruct((rows, steps, count, head_dim), jnp.float32),
        ],
        cost_estimate=pl.CostEstimate(
            flops=flops,
            transcendentals=rows * steps * count * span,
            bytes_accessed=pages.size * 2 + queries.size * 2 + rows * steps * count * (head_dim + 2) * 4,
        ),
    )(bounds, queries, pages)


def on_device(
    x_steps,
    lengths,
    perm,
    parents,
    table,
    pool,
    norm_attn,
    w_query,
    w_keyval,
    w_out,
    norm_mlp,
    w_gate,
    w_up,
    w_down,
):
    steps, rows, width = x_steps.shape
    head_dim = pool.shape[2] // 2
    heads = w_query.shape[1] // head_dim
    qwidth = heads * head_dim
    span = table.shape[1] * pool.shape[1]
    req_count = lax.axis_size("req")
    kv_count = lax.axis_size(KV)
    group = lax.axis_index("req")
    halves = lax.axis_size("zhi")
    half = lax.axis_index("zhi")
    beam = lax.axis_index("y") * 2 + lax.axis_index("zlo")
    member = member_of(beam, half, halves)
    per_group = halves * rows
    group_rows = kv_count * rows
    quota = rows // req_count

    offsets = jnp.arange(rows, dtype=jnp.int32)
    slot_ids = group * per_group + half * rows + offsets
    placed = lax.dynamic_slice_in_dim(perm.reshape(req_count, per_group), half * rows, rows, 1)
    serving = lax.dynamic_index_in_dim(placed, group, 0, keepdims=False)
    target = jnp.sum(
        jnp.where(placed == slot_ids[None, :], jnp.arange(req_count, dtype=jnp.int32)[:, None], 0),
        axis=0,
    )
    anchor = serving // per_group
    send_order = jnp.argsort(target * rows + offsets)
    outgoing = x_steps[:, send_order].reshape(steps, req_count, quota, width)
    arrived = lax.all_to_all(outgoing, "req", split_axis=1, concat_axis=1, tiled=True).reshape(
        steps, rows, width
    )
    slot_req = perm.reshape(req_count, halves, rows) // (halves * rows)
    mine_req = slot_req[:, half, :][group]
    offset_of = jnp.sum(
        jnp.where(mine_req[None, :] == offsets[:, None], offsets[None, :], 0), axis=1
    )
    inputs = arrived

    normed = rms_round(inputs.reshape(steps * rows, width), norm_attn)
    query = jnp.dot(normed, w_query, preferred_element_type=jnp.float32).astype(jnp.bfloat16)
    fresh = jnp.dot(normed, w_keyval, preferred_element_type=jnp.float32).astype(jnp.bfloat16)
    packed = jnp.concatenate([query, fresh], axis=-1).reshape(steps, rows, qwidth + 2 * head_dim)
    mine = lax.all_to_all(
        jnp.broadcast_to(packed[None], (BEAMS,) + packed.shape), HALF, 0, 0, tiled=True
    )
    queries = mine[..., :qwidth].reshape(BEAMS, steps, rows, heads, head_dim)
    entries = mine[..., qwidth:]

    family = lax.dynamic_slice_in_dim(parents, group * group_rows, group_rows, 1).reshape(
        (steps, BEAMS // 2, halves, 2, rows)
    )
    family = lax.dynamic_index_in_dim(family, half, 2, keepdims=False).reshape(steps, BEAMS, rows)
    family = family[:, :, offset_of]
    own = jnp.broadcast_to(jnp.arange(BEAMS, dtype=jnp.int32)[:, None], (BEAMS, rows))
    cache_beam = own
    sources = []
    cache_beams = []
    listed = []
    for step_index in range(steps):
        cache_beam = follow(family[step_index], cache_beam)
        sources = [follow(family[step_index], source) for source in sources] + [own]
        cache_beams.append(cache_beam)
        picked = [pick_rows(source, entries[:, s]) for s, source in enumerate(sources)]
        picked += [jnp.zeros_like(picked[0])] * (steps - 1 - step_index)
        listed.append(jnp.stack(picked))
    held = jnp.stack(cache_beams, axis=1) == beam
    listed = jnp.stack(listed)

    length = lengths[serving[offset_of]]
    first_page = jnp.maximum(length - WINDOW + 1, 0) // PAGE
    device = group * kv_count + member
    pages = pool[table[offset_of] - device * pool.shape[0]].reshape(rows, span, 2 * head_dim)
    scale = head_dim ** (-0.5)
    step_ids = jnp.arange(steps, dtype=jnp.int32)
    base = first_page * PAGE
    lo = length[:, None] + step_ids[None, :] - WINDOW - base[:, None]
    hi = jnp.broadcast_to((length - base)[:, None], (rows, steps))
    bounds = jnp.stack([lo, hi], axis=-1).reshape(rows * steps * 2)
    by_row = jnp.transpose(queries, (2, 1, 0, 3, 4)).reshape(rows, steps, BEAMS * heads, head_dim)
    high_c, total_c, sum_c = cache_part(bounds, by_row, pages)
    high_c = jnp.transpose(high_c.reshape(rows, steps, BEAMS, heads), (2, 1, 0, 3))
    total_c = jnp.transpose(total_c.reshape(rows, steps, BEAMS, heads), (2, 1, 0, 3))
    sum_c = jnp.transpose(sum_c.reshape(rows, steps, BEAMS, heads, head_dim), (2, 1, 0, 3, 4))

    new_keys = listed[..., :head_dim]
    new_values = listed[..., head_dim:]
    fresh_scores = jnp.einsum(
        "jtrhd,tsjrd->jtrhs", queries, new_keys, preferred_element_type=jnp.float32
    ) * scale
    counted = step_ids[None, :] <= step_ids[:, None]
    fresh_scores = jnp.where(counted[None, :, None, None, :], fresh_scores, NEGATIVE)
    high_n = jnp.max(fresh_scores, axis=-1)
    fresh_weights = jnp.exp(fresh_scores - high_n[..., None]).astype(jnp.bfloat16)
    fresh_weights = jnp.where(counted[None, :, None, None, :], fresh_weights, 0)
    total_n = jnp.sum(fresh_weights.astype(jnp.float32), axis=-1)
    sum_n = jnp.einsum(
        "jtrhs,tsjrd->jtrhd", fresh_weights, new_values, preferred_element_type=jnp.float32
    )

    highest = jnp.maximum(high_c, high_n)
    scale_c = jnp.exp(high_c - highest)
    scale_n = jnp.exp(high_n - highest)
    totals = total_c * scale_c + total_n * scale_n
    weighted = sum_c * scale_c[..., None] + sum_n * scale_n[..., None]
    attended = (weighted / totals[..., None]).astype(jnp.bfloat16).reshape(
        BEAMS, steps, rows, qwidth
    )
    attended = jnp.where(held[..., None], attended, jnp.zeros_like(attended))

    received = lax.all_to_all(attended, HALF, split_axis=0, concat_axis=0, tiled=True)
    attended_own = jnp.sum(received.astype(jnp.float32), axis=0).astype(jnp.bfloat16)

    current = inputs.reshape(steps * rows, width)
    residual = (
        current.astype(jnp.float32)
        + jnp.dot(attended_own.reshape(steps * rows, qwidth), w_out, preferred_element_type=jnp.float32)
    ).astype(jnp.bfloat16)
    mlp_own = rms_round(residual, norm_mlp)
    mlp_in = lax.all_to_all(
        jnp.broadcast_to(mlp_own[None], (kv_count,) + mlp_own.shape), KV, 0, 0, tiled=True
    ).reshape(kv_count * steps * rows, width)
    gate = jnp.dot(mlp_in, w_gate, preferred_element_type=jnp.float32)
    upward = jnp.dot(mlp_in, w_up, preferred_element_type=jnp.float32)
    hidden = (jax.nn.gelu(gate, approximate=True) * upward).astype(jnp.bfloat16)
    terms = jnp.dot(hidden, w_down, preferred_element_type=jnp.float32)
    terms = terms.reshape(kv_count, steps, rows, width)
    is_own = (jnp.arange(kv_count, dtype=jnp.int32) == member)[:, None, None, None]
    terms = terms + jnp.where(is_own, residual.astype(jnp.float32).reshape(steps, rows, width)[None], 0.0)
    terms = terms.astype(jnp.bfloat16)

    leaving = jnp.transpose(terms, (2, 0, 1, 3)).reshape(req_count * kv_count, steps, width)
    arrived_sums = lax.all_to_all(leaving, ("req",) + KV, 0, 0, tiled=True).reshape(
        req_count, kv_count, steps, width
    )
    per_group_sum = jnp.sum(arrived_sums.astype(jnp.float32), axis=1)
    served_by = slot_req[:, half, :] == group
    finished = jnp.sum(
        jnp.where(served_by[:, None, :, None], per_group_sum[:, :, None, :], 0.0), axis=0
    )
    return finished.astype(jnp.bfloat16)


def solution(mesh):
    req_count, kv_count = mesh.devices.shape
    halves = kv_count // BEAMS
    split = Mesh(
        mesh.devices.reshape(req_count, BEAMS // 2, halves, 2), ("req",) + KV
    )
    mesh = split
    ROWS = ("req",) + KV
    in_specs = (
        P(None, ROWS, None),
        P(),
        P(),
        P(),
        P(ROWS, None),
        P(ROWS, None, None),
        P(),
        P(),
        P(),
        P(),
        P(),
        P(None, KV),
        P(None, KV),
        P(KV, None),
    )
    out_specs = P(None, ROWS, None)
    return jax.shard_map(
        on_device, mesh=mesh, in_specs=in_specs, out_specs=out_specs, check_vma=False
    )
```

```python
import jax
import jax.numpy as jnp
from jax import lax
from jax.sharding import Mesh, PartitionSpec as P
from jax.experimental import pallas as pl
from jax.experimental.pallas import tpu as pltpu

WINDOW = 1024
PAGE = 128
BEAMS = 8


EPSILON = 1e-06
KV = ("y", "zhi", "zlo")
HALF = ("y", "zlo")
NEGATIVE = -1e30


def member_of(beam_index, half_index, halves):
    return beam_index % 2 + 2 * half_index + 2 * halves * (beam_index // 2)


def rms_round(values, gain):
    wide = values.astype(jnp.float32)
    mean_square = jnp.mean(wide * wide, axis=-1, keepdims=True)
    return (wide * lax.rsqrt(mean_square + EPSILON) * gain).astype(jnp.bfloat16)


def rank_within(labels, offsets):
    earlier = (labels[None, :] == labels[:, None]) & (offsets[None, :] < offsets[:, None])
    return jnp.sum(earlier.astype(jnp.int32), axis=1)


def follow(index, table):
    picks = index[:, None, :] == jnp.arange(BEAMS, dtype=jnp.int32)[None, :, None]
    return jnp.sum(jnp.where(picks, table[None, :, :], 0), axis=1)


def pick_rows(index, table):
    picks = index[:, None, :] == jnp.arange(BEAMS, dtype=jnp.int32)[None, :, None]
    return jnp.sum(jnp.where(picks[..., None], table[None, :, :, :], 0), axis=1).astype(table.dtype)


def attend_kernel(bounds_ref, q_ref, kv_ref, new_ref, pick_ref, out_ref):
    r = pl.program_id(0)
    steps = q_ref.shape[1]
    head_dim = q_ref.shape[3]
    scale = head_dim ** (-0.5)
    keys = kv_ref[0, :, :head_dim]
    values = kv_ref[0, :, head_dim:]
    pos = lax.broadcasted_iota(jnp.int32, (1, kv_ref.shape[1]), 1)
    contract = (((1,), (1,)), ((), ()))
    for t in range(steps):
        lo = bounds_ref[(r * steps + t) * 2]
        hi = bounds_ref[(r * steps + t) * 2 + 1]
        query = q_ref[0, t]
        scores = lax.dot_general(query, keys, contract, preferred_element_type=jnp.float32) * scale
        allowed = (pos > lo) & (pos < hi)
        scores = jnp.where(allowed, scores, NEGATIVE)
        high_c = jnp.max(scores, axis=1, keepdims=True)
        weights = jnp.exp(scores - high_c).astype(jnp.bfloat16)
        total_c = jnp.sum(weights.astype(jnp.float32), axis=1, keepdims=True)
        sum_c = jnp.dot(weights, values, preferred_element_type=jnp.float32)
        entries = new_ref[0, t]
        fresh = lax.dot_general(
            query, entries[:, :head_dim], contract, preferred_element_type=jnp.float32
        ) * scale
        fresh = jnp.where(pick_ref[t] > 0, fresh, NEGATIVE)
        high_n = jnp.max(fresh, axis=1, keepdims=True)
        fresh_w = jnp.exp(fresh - high_n).astype(jnp.bfloat16)
        total_n = jnp.sum(fresh_w.astype(jnp.float32), axis=1, keepdims=True)
        sum_n = jnp.dot(fresh_w, entries[:, head_dim:], preferred_element_type=jnp.float32)
        highest = jnp.maximum(high_c, high_n)
        scale_c = jnp.exp(high_c - highest)
        scale_n = jnp.exp(high_n - highest)
        totals = total_c * scale_c + total_n * scale_n
        weighted = sum_c * scale_c + sum_n * scale_n
        out_ref[0, t] = (weighted / totals).astype(out_ref.dtype)


def attend(bounds, queries, pages, entries, pick):
    rows, steps, count, head_dim = queries.shape
    span = pages.shape[1]
    flops = 4 * rows * steps * count * (span + entries.shape[2]) * head_dim
    return pl.pallas_call(
        attend_kernel,
        grid_spec=pltpu.PrefetchScalarGridSpec(
            num_scalar_prefetch=1,
            grid=(rows,),
            in_specs=[
                pl.BlockSpec((1, steps, count, head_dim), lambda r, b: (r, 0, 0, 0)),
                pl.BlockSpec((1, span, pages.shape[2]), lambda r, b: (r, 0, 0)),
                pl.BlockSpec((1,) + entries.shape[1:], lambda r, b: (r, 0, 0, 0)),
                pl.BlockSpec(pick.shape, lambda r, b: (0, 0, 0)),
            ],
            out_specs=pl.BlockSpec((1, steps, count, head_dim), lambda r, b: (r, 0, 0, 0)),
        ),
        out_shape=jax.ShapeDtypeStruct(queries.shape, jnp.bfloat16),
        cost_estimate=pl.CostEstimate(
            flops=flops,
            transcendentals=rows * steps * count * span,
            bytes_accessed=pages.size * 2 + queries.size * 4 + entries.size * 2,
        ),
    )(bounds, queries, pages, entries, pick)


def on_device(
    x_steps,
    lengths,
    perm,
    parents,
    table,
    pool,
    norm_attn,
    w_query,
    w_keyval,
    w_out,
    norm_mlp,
    w_gate,
    w_up,
    w_down,
):
    steps, rows, width = x_steps.shape
    head_dim = pool.shape[2] // 2
    heads = w_query.shape[1] // head_dim
    qwidth = heads * head_dim
    span = table.shape[1] * pool.shape[1]
    req_count = lax.axis_size("req")
    kv_count = lax.axis_size(KV)
    group = lax.axis_index("req")
    halves = lax.axis_size("zhi")
    half = lax.axis_index("zhi")
    beam = lax.axis_index("y") * 2 + lax.axis_index("zlo")
    member = member_of(beam, half, halves)
    per_group = halves * rows
    group_rows = kv_count * rows
    quota = rows // req_count

    offsets = jnp.arange(rows, dtype=jnp.int32)
    slot_ids = group * per_group + half * rows + offsets
    placed = lax.dynamic_slice_in_dim(perm.reshape(req_count, per_group), half * rows, rows, 1)
    serving = lax.dynamic_index_in_dim(placed, group, 0, keepdims=False)
    target = jnp.sum(
        jnp.where(placed == slot_ids[None, :], jnp.arange(req_count, dtype=jnp.int32)[:, None], 0),
        axis=0,
    )
    anchor = serving // per_group
    send_order = jnp.argsort(target * rows + offsets)
    outgoing = x_steps[:, send_order].reshape(steps, req_count, quota, width)
    arrived = lax.all_to_all(outgoing, "req", split_axis=1, concat_axis=1, tiled=True).reshape(
        steps, rows, width
    )
    slot_req = perm.reshape(req_count, halves, rows) // (halves * rows)
    mine_req = slot_req[:, half, :][group]
    offset_of = jnp.sum(
        jnp.where(mine_req[None, :] == offsets[:, None], offsets[None, :], 0), axis=1
    )
    inputs = arrived

    normed = rms_round(inputs.reshape(steps * rows, width), norm_attn)
    query = jnp.dot(normed, w_query, preferred_element_type=jnp.float32).astype(jnp.bfloat16)
    fresh = jnp.dot(normed, w_keyval, preferred_element_type=jnp.float32).astype(jnp.bfloat16)
    packed = jnp.concatenate([query, fresh], axis=-1).reshape(steps, rows, qwidth + 2 * head_dim)
    mine = lax.all_to_all(
        jnp.broadcast_to(packed[None], (BEAMS,) + packed.shape), HALF, 0, 0, tiled=True
    )
    queries = mine[..., :qwidth].reshape(BEAMS, steps, rows, heads, head_dim)
    entries = mine[..., qwidth:]

    family = lax.dynamic_slice_in_dim(parents, group * group_rows, group_rows, 1).reshape(
        (steps, BEAMS // 2, halves, 2, rows)
    )
    family = lax.dynamic_index_in_dim(family, half, 2, keepdims=False).reshape(steps, BEAMS, rows)
    family = family[:, :, offset_of]
    own = jnp.broadcast_to(jnp.arange(BEAMS, dtype=jnp.int32)[:, None], (BEAMS, rows))
    cache_beam = own
    sources = []
    cache_beams = []
    listed = []
    for step_index in range(steps):
        cache_beam = follow(family[step_index], cache_beam)
        sources = [follow(family[step_index], source) for source in sources] + [own]
        cache_beams.append(cache_beam)
        picked = [pick_rows(source, entries[:, s]) for s, source in enumerate(sources)]
        picked += [jnp.zeros_like(picked[0])] * (steps - 1 - step_index)
        listed.append(jnp.stack(picked))
    held = jnp.stack(cache_beams, axis=1) == beam
    listed = jnp.stack(listed)

    length = lengths[serving[offset_of]]
    first_page = jnp.maximum(length - WINDOW + 1, 0) // PAGE
    device = group * kv_count + member
    pages = pool[table[offset_of] - device * pool.shape[0]].reshape(rows, span, 2 * head_dim)
    scale = head_dim ** (-0.5)
    step_ids = jnp.arange(steps, dtype=jnp.int32)
    base = first_page * PAGE
    lo = length[:, None] + step_ids[None, :] - WINDOW - base[:, None]
    hi = jnp.broadcast_to((length - base)[:, None], (rows, steps))
    bounds = jnp.stack([lo, hi], axis=-1).reshape(rows * steps * 2)
    by_row = jnp.transpose(queries, (2, 1, 0, 3, 4)).reshape(rows, steps, BEAMS * heads, head_dim)
    entries_by_row = jnp.transpose(listed, (3, 0, 1, 2, 4)).reshape(
        rows, steps, steps * BEAMS, 2 * head_dim
    )
    row_beam = jnp.arange(BEAMS * heads, dtype=jnp.int32) // heads
    column = jnp.arange(steps * BEAMS, dtype=jnp.int32)
    pick = (
        (column[None, None, :] % BEAMS == row_beam[None, :, None])
        & (column[None, None, :] // BEAMS <= step_ids[:, None, None])
    ).astype(jnp.float32)
    attended = attend(bounds, by_row, pages, entries_by_row, pick)
    attended = jnp.transpose(attended.reshape(rows, steps, BEAMS, qwidth), (2, 1, 0, 3))
    attended = jnp.where(held[..., None], attended, jnp.zeros_like(attended))

    received = lax.all_to_all(attended, HALF, split_axis=0, concat_axis=0, tiled=True)
    attended_own = jnp.sum(received.astype(jnp.float32), axis=0).astype(jnp.bfloat16)

    current = inputs.reshape(steps * rows, width)
    residual = (
        current.astype(jnp.float32)
        + jnp.dot(attended_own.reshape(steps * rows, qwidth), w_out, preferred_element_type=jnp.float32)
    ).astype(jnp.bfloat16)
    mlp_own = jnp.swapaxes(rms_round(residual, norm_mlp).reshape(steps, rows, width), 0, 1)
    mlp_in = lax.all_to_all(
        jnp.broadcast_to(mlp_own[None], (kv_count,) + mlp_own.shape), KV, 0, 0, tiled=True
    ).reshape(kv_count * steps * rows, width)
    gate = jnp.dot(mlp_in, w_gate, preferred_element_type=jnp.float32)
    upward = jnp.dot(mlp_in, w_up, preferred_element_type=jnp.float32)
    hidden = (jax.nn.gelu(gate, approximate=True) * upward).astype(jnp.bfloat16)
    terms = jnp.dot(hidden, w_down, preferred_element_type=jnp.float32)
    terms = terms.reshape(kv_count, rows, steps, width)
    own_rows = jnp.swapaxes(residual.astype(jnp.float32).reshape(steps, rows, width), 0, 1)
    own_rows = lax.dynamic_index_in_dim(terms, member, 0, keepdims=False) + own_rows
    terms = lax.dynamic_update_index_in_dim(terms, own_rows, member, 0).astype(jnp.bfloat16)

    leaving = terms.reshape(kv_count * req_count, steps, width)
    arrived_sums = lax.all_to_all(leaving, KV + ("req",), 0, 0, tiled=True).reshape(
        kv_count, req_count, steps, width
    )
    per_group_sum = jnp.sum(arrived_sums.astype(jnp.float32), axis=0)
    served_by = slot_req[:, half, :] == group
    finished = jnp.sum(
        jnp.where(served_by[:, None, :, None], per_group_sum[:, :, None, :], 0.0), axis=0
    )
    return finished.astype(jnp.bfloat16)


def solution(mesh):
    req_count, kv_count = mesh.devices.shape
    halves = kv_count // BEAMS
    split = Mesh(
        mesh.devices.reshape(req_count, BEAMS // 2, halves, 2), ("req",) + KV
    )
    mesh = split
    ROWS = ("req",) + KV
    in_specs = (
        P(None, ROWS, None),
        P(),
        P(),
        P(),
        P(ROWS, None),
        P(ROWS, None, None),
        P(),
        P(),
        P(),
        P(),
        P(),
        P(None, KV),
        P(None, KV),
        P(KV, None),
    )
    out_specs = P(None, ROWS, None)
    return jax.shard_map(
        on_device, mesh=mesh, in_specs=in_specs, out_specs=out_specs, check_vma=False
    )
```

```python
import jax
import jax.numpy as jnp
from jax import lax
from jax.sharding import Mesh, PartitionSpec as P
from jax.experimental import pallas as pl
from jax.experimental.pallas import tpu as pltpu

WINDOW = 1024
PAGE = 128
BEAMS = 8


EPSILON = 1e-06
KV = ("y", "zhi", "zlo")
HALF = ("y", "zlo")
NEGATIVE = -1e30


def member_of(beam_index, half_index, halves):
    return beam_index % 2 + 2 * half_index + 2 * halves * (beam_index // 2)


def rms_round(values, gain):
    wide = values.astype(jnp.float32)
    mean_square = jnp.mean(wide * wide, axis=-1, keepdims=True)
    return (wide * lax.rsqrt(mean_square + EPSILON) * gain).astype(jnp.bfloat16)


def rank_within(labels, offsets):
    earlier = (labels[None, :] == labels[:, None]) & (offsets[None, :] < offsets[:, None])
    return jnp.sum(earlier.astype(jnp.int32), axis=1)


def follow(index, table):
    picks = index[:, None, :] == jnp.arange(BEAMS, dtype=jnp.int32)[None, :, None]
    return jnp.sum(jnp.where(picks, table[None, :, :], 0), axis=1)


def pick_rows(index, table):
    picks = index[:, None, :] == jnp.arange(BEAMS, dtype=jnp.int32)[None, :, None]
    return jnp.sum(jnp.where(picks[..., None], table[None, :, :, :], 0), axis=1).astype(table.dtype)


def attend_kernel(bounds_ref, q_ref, kv_ref, new_ref, pick_ref, out_ref):
    r = pl.program_id(0)
    steps = q_ref.shape[1]
    head_dim = q_ref.shape[3]
    scale = head_dim ** (-0.5)
    keys = kv_ref[0, :, :head_dim]
    values = kv_ref[0, :, head_dim:]
    pos = lax.broadcasted_iota(jnp.int32, (1, kv_ref.shape[1]), 1)
    contract = (((1,), (1,)), ((), ()))
    for t in range(steps):
        lo = bounds_ref[(r * steps + t) * 2]
        hi = bounds_ref[(r * steps + t) * 2 + 1]
        query = q_ref[0, t]
        scores = lax.dot_general(query, keys, contract, preferred_element_type=jnp.float32) * scale
        allowed = (pos > lo) & (pos < hi)
        scores = jnp.where(allowed, scores, NEGATIVE)
        high_c = jnp.max(scores, axis=1, keepdims=True)
        weights = jnp.exp(scores - high_c).astype(jnp.bfloat16)
        total_c = jnp.sum(weights.astype(jnp.float32), axis=1, keepdims=True)
        sum_c = jnp.dot(weights, values, preferred_element_type=jnp.float32)
        entries = new_ref[0, t]
        fresh = lax.dot_general(
            query, entries[:, :head_dim], contract, preferred_element_type=jnp.float32
        ) * scale
        fresh = jnp.where(pick_ref[t] > 0, fresh, NEGATIVE)
        high_n = jnp.max(fresh, axis=1, keepdims=True)
        fresh_w = jnp.exp(fresh - high_n).astype(jnp.bfloat16)
        total_n = jnp.sum(fresh_w.astype(jnp.float32), axis=1, keepdims=True)
        sum_n = jnp.dot(fresh_w, entries[:, head_dim:], preferred_element_type=jnp.float32)
        highest = jnp.maximum(high_c, high_n)
        scale_c = jnp.exp(high_c - highest)
        scale_n = jnp.exp(high_n - highest)
        totals = total_c * scale_c + total_n * scale_n
        weighted = sum_c * scale_c + sum_n * scale_n
        out_ref[0, t] = (weighted / totals).astype(out_ref.dtype)


def attend(bounds, queries, pages, entries, pick):
    rows, steps, count, head_dim = queries.shape
    span = pages.shape[1]
    flops = 4 * rows * steps * count * (span + entries.shape[2]) * head_dim
    return pl.pallas_call(
        attend_kernel,
        grid_spec=pltpu.PrefetchScalarGridSpec(
            num_scalar_prefetch=1,
            grid=(rows,),
            in_specs=[
                pl.BlockSpec((1, steps, count, head_dim), lambda r, b: (r, 0, 0, 0)),
                pl.BlockSpec((1, span, pages.shape[2]), lambda r, b: (r, 0, 0)),
                pl.BlockSpec((1,) + entries.shape[1:], lambda r, b: (r, 0, 0, 0)),
                pl.BlockSpec(pick.shape, lambda r, b: (0, 0, 0)),
            ],
            out_specs=pl.BlockSpec((1, steps, count, head_dim), lambda r, b: (r, 0, 0, 0)),
        ),
        out_shape=jax.ShapeDtypeStruct(queries.shape, jnp.bfloat16),
        cost_estimate=pl.CostEstimate(
            flops=flops,
            transcendentals=rows * steps * count * span,
            bytes_accessed=pages.size * 2 + queries.size * 4 + entries.size * 2,
        ),
    )(bounds, queries, pages, entries, pick)


def on_device(
    x_steps,
    lengths,
    perm,
    parents,
    table,
    pool,
    norm_attn,
    w_query,
    w_keyval,
    w_out,
    norm_mlp,
    w_gate,
    w_up,
    w_down,
):
    steps, rows, width = x_steps.shape
    head_dim = pool.shape[2] // 2
    heads = w_query.shape[1] // head_dim
    qwidth = heads * head_dim
    span = table.shape[1] * pool.shape[1]
    req_count = lax.axis_size("req")
    kv_count = lax.axis_size(KV)
    group = lax.axis_index("req")
    halves = lax.axis_size("zhi")
    half = lax.axis_index("zhi")
    beam = lax.axis_index("y") * 2 + lax.axis_index("zlo")
    member = member_of(beam, half, halves)
    per_group = halves * rows
    group_rows = kv_count * rows
    quota = rows // req_count

    offsets = jnp.arange(rows, dtype=jnp.int32)
    slot_ids = group * per_group + half * rows + offsets
    placed = lax.dynamic_slice_in_dim(perm.reshape(req_count, per_group), half * rows, rows, 1)
    serving = lax.dynamic_index_in_dim(placed, group, 0, keepdims=False)
    target = jnp.sum(
        jnp.where(placed == slot_ids[None, :], jnp.arange(req_count, dtype=jnp.int32)[:, None], 0),
        axis=0,
    )
    anchor = serving // per_group
    send_order = jnp.argsort(target * rows + offsets)
    outgoing = x_steps[:, send_order].reshape(steps, req_count, quota, width)
    arrived = lax.all_to_all(outgoing, "req", split_axis=1, concat_axis=1, tiled=True).reshape(
        steps, rows, width
    )
    slot_req = perm.reshape(req_count, halves, rows) // (halves * rows)
    mine_req = slot_req[:, half, :][group]
    offset_of = jnp.sum(
        jnp.where(mine_req[None, :] == offsets[:, None], offsets[None, :], 0), axis=1
    )
    inputs = arrived

    normed = rms_round(inputs.reshape(steps * rows, width), norm_attn)
    query = jnp.dot(normed, w_query, preferred_element_type=jnp.float32).astype(jnp.bfloat16)
    fresh = jnp.dot(normed, w_keyval, preferred_element_type=jnp.float32).astype(jnp.bfloat16)
    packed = jnp.concatenate([query, fresh], axis=-1).reshape(steps, rows, qwidth + 2 * head_dim)
    mine = lax.all_to_all(
        jnp.broadcast_to(packed[None], (BEAMS,) + packed.shape), HALF, 0, 0, tiled=True
    )
    queries = mine[..., :qwidth].reshape(BEAMS, steps, rows, heads, head_dim)
    entries = mine[..., qwidth:]

    family = lax.dynamic_slice_in_dim(parents, group * group_rows, group_rows, 1).reshape(
        (steps, BEAMS // 2, halves, 2, rows)
    )
    family = lax.dynamic_index_in_dim(family, half, 2, keepdims=False).reshape(steps, BEAMS, rows)
    family = family[:, :, offset_of]
    own = jnp.broadcast_to(jnp.arange(BEAMS, dtype=jnp.int32)[:, None], (BEAMS, rows))
    cache_beam = own
    sources = []
    cache_beams = []
    listed = []
    for step_index in range(steps):
        cache_beam = follow(family[step_index], cache_beam)
        sources = [follow(family[step_index], source) for source in sources] + [own]
        cache_beams.append(cache_beam)
        picked = [pick_rows(source, entries[:, s]) for s, source in enumerate(sources)]
        picked += [jnp.zeros_like(picked[0])] * (steps - 1 - step_index)
        listed.append(jnp.stack(picked))
    held = jnp.stack(cache_beams, axis=1) == beam
    listed = jnp.stack(listed)

    length = lengths[serving[offset_of]]
    first_page = jnp.maximum(length - WINDOW + 1, 0) // PAGE
    device = group * kv_count + member
    pages = pool[table[offset_of] - device * pool.shape[0]].reshape(rows, span, 2 * head_dim)
    scale = head_dim ** (-0.5)
    step_ids = jnp.arange(steps, dtype=jnp.int32)
    base = first_page * PAGE
    lo = length[:, None] + step_ids[None, :] - WINDOW - base[:, None]
    hi = jnp.broadcast_to((length - base)[:, None], (rows, steps))
    bounds = jnp.stack([lo, hi], axis=-1).reshape(rows * steps * 2)
    by_row = jnp.transpose(queries, (2, 1, 0, 3, 4)).reshape(rows, steps, BEAMS * heads, head_dim)
    entries_by_row = jnp.transpose(listed, (3, 0, 1, 2, 4)).reshape(
        rows, steps, steps * BEAMS, 2 * head_dim
    )
    row_beam = jnp.arange(BEAMS * heads, dtype=jnp.int32) // heads
    column = jnp.arange(steps * BEAMS, dtype=jnp.int32)
    pick = (
        (column[None, None, :] % BEAMS == row_beam[None, :, None])
        & (column[None, None, :] // BEAMS <= step_ids[:, None, None])
    ).astype(jnp.float32)
    attended = attend(bounds, by_row, pages, entries_by_row, pick)
    attended = jnp.transpose(attended.reshape(rows, steps, BEAMS, qwidth), (2, 1, 0, 3))
    attended = jnp.where(held[..., None], attended, jnp.zeros_like(attended))

    received = lax.all_to_all(attended, HALF, split_axis=0, concat_axis=0, tiled=True)
    attended_own = jnp.sum(received.astype(jnp.float32), axis=0).astype(jnp.bfloat16)

    current = inputs.reshape(steps * rows, width)
    residual = (
        current.astype(jnp.float32)
        + jnp.dot(attended_own.reshape(steps * rows, qwidth), w_out, preferred_element_type=jnp.float32)
    ).astype(jnp.bfloat16)
    by_req = jnp.swapaxes(residual.reshape(steps, rows, width), 0, 1).reshape(rows * steps, width)
    mlp_own = rms_round(by_req, norm_mlp)
    mlp_in = lax.all_to_all(
        jnp.broadcast_to(mlp_own[None], (kv_count,) + mlp_own.shape), KV, 0, 0, tiled=True
    ).reshape(kv_count * rows * steps, width)
    gate = jnp.dot(mlp_in, w_gate, preferred_element_type=jnp.float32)
    upward = jnp.dot(mlp_in, w_up, preferred_element_type=jnp.float32)
    hidden = (jax.nn.gelu(gate, approximate=True) * upward).astype(jnp.bfloat16)
    own_row = jnp.arange(kv_count * rows * steps, dtype=jnp.int32)
    select = (
        (own_row[:, None] // (rows * steps) == member)
        & (own_row[:, None] % (rows * steps) == jnp.arange(rows * steps, dtype=jnp.int32)[None, :])
    ).astype(jnp.bfloat16)
    terms = jnp.dot(
        jnp.concatenate([hidden, select], axis=1),
        jnp.concatenate([w_down, by_req], axis=0),
        preferred_element_type=jnp.float32,
    ).astype(jnp.bfloat16)

    leaving = terms
    arrived_sums = lax.all_to_all(leaving, KV + ("req",), 0, 0, tiled=True).reshape(
        kv_count, req_count, steps, width
    )
    per_group_sum = jnp.sum(arrived_sums.astype(jnp.float32), axis=0)
    served_by = slot_req[:, half, :] == group
    finished = jnp.sum(
        jnp.where(served_by[:, None, :, None], per_group_sum[:, :, None, :], 0.0), axis=0
    )
    return finished.astype(jnp.bfloat16)


def solution(mesh):
    req_count, kv_count = mesh.devices.shape
    halves = kv_count // BEAMS
    split = Mesh(
        mesh.devices.reshape(req_count, BEAMS // 2, halves, 2), ("req",) + KV
    )
    mesh = split
    ROWS = ("req",) + KV
    in_specs = (
        P(None, ROWS, None),
        P(),
        P(),
        P(),
        P(ROWS, None),
        P(ROWS, None, None),
        P(),
        P(),
        P(),
        P(),
        P(),
        P(None, KV),
        P(None, KV),
        P(KV, None),
    )
    out_specs = P(None, ROWS, None)
    return jax.shard_map(
        on_device, mesh=mesh, in_specs=in_specs, out_specs=out_specs, check_vma=False
    )
```

```python
import jax
import jax.numpy as jnp
from jax import lax
from jax.sharding import Mesh, PartitionSpec as P
from jax.experimental import pallas as pl
from jax.experimental.pallas import tpu as pltpu

WINDOW = 1024
PAGE = 128
BEAMS = 8


EPSILON = 1e-06
KV = ("y", "zhi", "zlo")
HALF = ("y", "zlo")
NEGATIVE = -1e30


def member_of(beam_index, half_index, halves):
    return beam_index % 2 + 2 * half_index + 2 * halves * (beam_index // 2)


def rms_round(values, gain):
    wide = values.astype(jnp.float32)
    mean_square = jnp.mean(wide * wide, axis=-1, keepdims=True)
    return (wide * lax.rsqrt(mean_square + EPSILON) * gain).astype(jnp.bfloat16)


def rank_within(labels, offsets):
    earlier = (labels[None, :] == labels[:, None]) & (offsets[None, :] < offsets[:, None])
    return jnp.sum(earlier.astype(jnp.int32), axis=1)


def follow(index, table):
    picks = index[:, None, :] == jnp.arange(BEAMS, dtype=jnp.int32)[None, :, None]
    return jnp.sum(jnp.where(picks, table[None, :, :], 0), axis=1)


def pick_rows(index, table):
    picks = index[:, None, :] == jnp.arange(BEAMS, dtype=jnp.int32)[None, :, None]
    return jnp.sum(jnp.where(picks[..., None], table[None, :, :, :], 0), axis=1).astype(table.dtype)


def attend_kernel(bounds_ref, q_ref, kv_ref, new_ref, pick_ref, out_ref):
    r = pl.program_id(0)
    steps = q_ref.shape[1]
    head_dim = q_ref.shape[3]
    scale = head_dim ** (-0.5)
    keys = kv_ref[0, :, :head_dim]
    values = kv_ref[0, :, head_dim:]
    pos = lax.broadcasted_iota(jnp.int32, (1, kv_ref.shape[1]), 1)
    contract = (((1,), (1,)), ((), ()))
    for t in range(steps):
        lo = bounds_ref[(r * steps + t) * 2]
        hi = bounds_ref[(r * steps + t) * 2 + 1]
        query = q_ref[0, t]
        scores = lax.dot_general(query, keys, contract, preferred_element_type=jnp.float32) * scale
        allowed = (pos > lo) & (pos < hi)
        scores = jnp.where(allowed, scores, NEGATIVE)
        high_c = jnp.max(scores, axis=1, keepdims=True)
        weights = jnp.exp(scores - high_c).astype(jnp.bfloat16)
        total_c = jnp.sum(weights.astype(jnp.float32), axis=1, keepdims=True)
        sum_c = jnp.dot(weights, values, preferred_element_type=jnp.float32)
        entries = new_ref[0, t]
        fresh = lax.dot_general(
            query, entries[:, :head_dim], contract, preferred_element_type=jnp.float32
        ) * scale
        fresh = jnp.where(pick_ref[t] > 0, fresh, NEGATIVE)
        high_n = jnp.max(fresh, axis=1, keepdims=True)
        fresh_w = jnp.exp(fresh - high_n).astype(jnp.bfloat16)
        total_n = jnp.sum(fresh_w.astype(jnp.float32), axis=1, keepdims=True)
        sum_n = jnp.dot(fresh_w, entries[:, head_dim:], preferred_element_type=jnp.float32)
        highest = jnp.maximum(high_c, high_n)
        scale_c = jnp.exp(high_c - highest)
        scale_n = jnp.exp(high_n - highest)
        totals = total_c * scale_c + total_n * scale_n
        weighted = sum_c * scale_c + sum_n * scale_n
        out_ref[0, t] = (weighted / totals).astype(out_ref.dtype)


def attend(bounds, queries, pages, entries, pick):
    rows, steps, count, head_dim = queries.shape
    span = pages.shape[1]
    flops = 4 * rows * steps * count * (span + entries.shape[2]) * head_dim
    return pl.pallas_call(
        attend_kernel,
        grid_spec=pltpu.PrefetchScalarGridSpec(
            num_scalar_prefetch=1,
            grid=(rows,),
            in_specs=[
                pl.BlockSpec((1, steps, count, head_dim), lambda r, b: (r, 0, 0, 0)),
                pl.BlockSpec((1, span, pages.shape[2]), lambda r, b: (r, 0, 0)),
                pl.BlockSpec((1,) + entries.shape[1:], lambda r, b: (r, 0, 0, 0)),
                pl.BlockSpec(pick.shape, lambda r, b: (0, 0, 0)),
            ],
            out_specs=pl.BlockSpec((1, steps, count, head_dim), lambda r, b: (r, 0, 0, 0)),
        ),
        out_shape=jax.ShapeDtypeStruct(queries.shape, jnp.bfloat16),
        cost_estimate=pl.CostEstimate(
            flops=flops,
            transcendentals=rows * steps * count * span,
            bytes_accessed=pages.size * 2 + queries.size * 4 + entries.size * 2,
        ),
    )(bounds, queries, pages, entries, pick)


def on_device(
    x_steps,
    lengths,
    perm,
    parents,
    table,
    pool,
    norm_attn,
    w_query,
    w_keyval,
    w_out,
    norm_mlp,
    w_gate,
    w_up,
    w_down,
):
    steps, rows, width = x_steps.shape
    head_dim = pool.shape[2] // 2
    heads = w_query.shape[1] // head_dim
    qwidth = heads * head_dim
    span = table.shape[1] * pool.shape[1]
    req_count = lax.axis_size("req")
    kv_count = lax.axis_size(KV)
    group = lax.axis_index("req")
    halves = lax.axis_size("zhi")
    half = lax.axis_index("zhi")
    beam = lax.axis_index("y") * 2 + lax.axis_index("zlo")
    member = member_of(beam, half, halves)
    per_group = halves * rows
    group_rows = kv_count * rows
    quota = rows // req_count
    swap = [(0, 1), (1, 0)]
    gate_w = jnp.concatenate([w_gate, lax.ppermute(w_gate, "zhi", swap)], axis=1)
    up_w = jnp.concatenate([w_up, lax.ppermute(w_up, "zhi", swap)], axis=1)
    down_w = jnp.concatenate([w_down, lax.ppermute(w_down, "zhi", swap)], axis=0)

    offsets = jnp.arange(rows, dtype=jnp.int32)
    slot_ids = group * per_group + half * rows + offsets
    placed = lax.dynamic_slice_in_dim(perm.reshape(req_count, per_group), half * rows, rows, 1)
    serving = lax.dynamic_index_in_dim(placed, group, 0, keepdims=False)
    target = jnp.sum(
        jnp.where(placed == slot_ids[None, :], jnp.arange(req_count, dtype=jnp.int32)[:, None], 0),
        axis=0,
    )
    anchor = serving // per_group
    send_order = jnp.argsort(target * rows + offsets)
    outgoing = x_steps[:, send_order].reshape(steps, req_count, quota, width)
    arrived = lax.all_to_all(outgoing, "req", split_axis=1, concat_axis=1, tiled=True).reshape(
        steps, rows, width
    )
    slot_req = perm.reshape(req_count, halves, rows) // (halves * rows)
    mine_req = slot_req[:, half, :][group]
    offset_of = jnp.sum(
        jnp.where(mine_req[None, :] == offsets[:, None], offsets[None, :], 0), axis=1
    )
    inputs = arrived

    normed = rms_round(inputs.reshape(steps * rows, width), norm_attn)
    query = jnp.dot(normed, w_query, preferred_element_type=jnp.float32).astype(jnp.bfloat16)
    fresh = jnp.dot(normed, w_keyval, preferred_element_type=jnp.float32).astype(jnp.bfloat16)
    packed = jnp.concatenate([query, fresh], axis=-1).reshape(steps, rows, qwidth + 2 * head_dim)
    mine = lax.all_to_all(
        jnp.broadcast_to(packed[None], (BEAMS,) + packed.shape), HALF, 0, 0, tiled=True
    )
    queries = mine[..., :qwidth].reshape(BEAMS, steps, rows, heads, head_dim)
    entries = mine[..., qwidth:]

    family = lax.dynamic_slice_in_dim(parents, group * group_rows, group_rows, 1).reshape(
        (steps, BEAMS // 2, halves, 2, rows)
    )
    family = lax.dynamic_index_in_dim(family, half, 2, keepdims=False).reshape(steps, BEAMS, rows)
    family = family[:, :, offset_of]
    own = jnp.broadcast_to(jnp.arange(BEAMS, dtype=jnp.int32)[:, None], (BEAMS, rows))
    cache_beam = own
    sources = []
    cache_beams = []
    listed = []
    for step_index in range(steps):
        cache_beam = follow(family[step_index], cache_beam)
        sources = [follow(family[step_index], source) for source in sources] + [own]
        cache_beams.append(cache_beam)
        picked = [pick_rows(source, entries[:, s]) for s, source in enumerate(sources)]
        picked += [jnp.zeros_like(picked[0])] * (steps - 1 - step_index)
        listed.append(jnp.stack(picked))
    held = jnp.stack(cache_beams, axis=1) == beam
    listed = jnp.stack(listed)

    length = lengths[serving[offset_of]]
    first_page = jnp.maximum(length - WINDOW + 1, 0) // PAGE
    device = group * kv_count + member
    pages = pool[table[offset_of] - device * pool.shape[0]].reshape(rows, span, 2 * head_dim)
    scale = head_dim ** (-0.5)
    step_ids = jnp.arange(steps, dtype=jnp.int32)
    base = first_page * PAGE
    lo = length[:, None] + step_ids[None, :] - WINDOW - base[:, None]
    hi = jnp.broadcast_to((length - base)[:, None], (rows, steps))
    bounds = jnp.stack([lo, hi], axis=-1).reshape(rows * steps * 2)
    by_row = jnp.transpose(queries, (2, 1, 0, 3, 4)).reshape(rows, steps, BEAMS * heads, head_dim)
    entries_by_row = jnp.transpose(listed, (3, 0, 1, 2, 4)).reshape(
        rows, steps, steps * BEAMS, 2 * head_dim
    )
    row_beam = jnp.arange(BEAMS * heads, dtype=jnp.int32) // heads
    column = jnp.arange(steps * BEAMS, dtype=jnp.int32)
    pick = (
        (column[None, None, :] % BEAMS == row_beam[None, :, None])
        & (column[None, None, :] // BEAMS <= step_ids[:, None, None])
    ).astype(jnp.float32)
    attended = attend(bounds, by_row, pages, entries_by_row, pick)
    attended = jnp.transpose(attended.reshape(rows, steps, BEAMS, qwidth), (2, 1, 0, 3))
    attended = jnp.where(held[..., None], attended, jnp.zeros_like(attended))

    received = lax.all_to_all(attended, HALF, split_axis=0, concat_axis=0, tiled=True)
    attended_own = jnp.sum(received.astype(jnp.float32), axis=0).astype(jnp.bfloat16)

    current = inputs.reshape(steps * rows, width)
    residual = (
        current.astype(jnp.float32)
        + jnp.dot(attended_own.reshape(steps * rows, qwidth), w_out, preferred_element_type=jnp.float32)
    ).astype(jnp.bfloat16)
    by_req = jnp.swapaxes(residual.reshape(steps, rows, width), 0, 1).reshape(rows * steps, width)
    mlp_own = rms_round(by_req, norm_mlp)
    mlp_in = lax.all_to_all(
        jnp.broadcast_to(mlp_own[None], (BEAMS,) + mlp_own.shape), HALF, 0, 0, tiled=True
    ).reshape(BEAMS * rows * steps, width)
    gate = jnp.dot(mlp_in, gate_w, preferred_element_type=jnp.float32)
    upward = jnp.dot(mlp_in, up_w, preferred_element_type=jnp.float32)
    hidden = (jax.nn.gelu(gate, approximate=True) * upward).astype(jnp.bfloat16)
    own_row = jnp.arange(BEAMS * rows * steps, dtype=jnp.int32)
    select = (
        (own_row[:, None] // (rows * steps) == beam)
        & (own_row[:, None] % (rows * steps) == jnp.arange(rows * steps, dtype=jnp.int32)[None, :])
    ).astype(jnp.bfloat16)
    terms = jnp.dot(
        jnp.concatenate([hidden, select], axis=1),
        jnp.concatenate([down_w, by_req], axis=0),
        preferred_element_type=jnp.float32,
    ).astype(jnp.bfloat16)

    arrived_sums = lax.all_to_all(terms, HALF + ("req",), 0, 0, tiled=True).reshape(
        BEAMS, req_count, steps, width
    )
    per_group_sum = jnp.sum(arrived_sums.astype(jnp.float32), axis=0)
    served_by = slot_req[:, half, :] == group
    finished = jnp.sum(
        jnp.where(served_by[:, None, :, None], per_group_sum[:, :, None, :], 0.0), axis=0
    )
    return finished.astype(jnp.bfloat16)


def solution(mesh):
    req_count, kv_count = mesh.devices.shape
    halves = kv_count // BEAMS
    split = Mesh(
        mesh.devices.reshape(req_count, BEAMS // 2, halves, 2), ("req",) + KV
    )
    mesh = split
    ROWS = ("req",) + KV
    in_specs = (
        P(None, ROWS, None),
        P(),
        P(),
        P(),
        P(ROWS, None),
        P(ROWS, None, None),
        P(),
        P(),
        P(),
        P(),
        P(),
        P(None, KV),
        P(None, KV),
        P(KV, None),
    )
    out_specs = P(None, ROWS, None)
    return jax.shard_map(
        on_device, mesh=mesh, in_specs=in_specs, out_specs=out_specs, check_vma=False
    )
```

```python
import jax
import jax.numpy as jnp
from jax import lax
from jax.sharding import Mesh, PartitionSpec as P
from jax.experimental import pallas as pl
from jax.experimental.pallas import tpu as pltpu

WINDOW = 1024
PAGE = 128
BEAMS = 8


EPSILON = 1e-06
KV = ("y", "zhi", "zlo")
HALF = ("y", "zlo")
NEGATIVE = -1e30


def member_of(beam_index, half_index, halves):
    return beam_index % 2 + 2 * half_index + 2 * halves * (beam_index // 2)


def rms_round(values, gain):
    wide = values.astype(jnp.float32)
    mean_square = jnp.mean(wide * wide, axis=-1, keepdims=True)
    return (wide * lax.rsqrt(mean_square + EPSILON) * gain).astype(jnp.bfloat16)


def rank_within(labels, offsets):
    earlier = (labels[None, :] == labels[:, None]) & (offsets[None, :] < offsets[:, None])
    return jnp.sum(earlier.astype(jnp.int32), axis=1)


def follow(index, table):
    picks = index[:, None, :] == jnp.arange(BEAMS, dtype=jnp.int32)[None, :, None]
    return jnp.sum(jnp.where(picks, table[None, :, :], 0), axis=1)


def pick_rows(index, table):
    picks = index[:, None, :] == jnp.arange(BEAMS, dtype=jnp.int32)[None, :, None]
    return jnp.sum(jnp.where(picks[..., None], table[None, :, :, :], 0), axis=1).astype(table.dtype)


def attend_kernel(bounds_ref, q_ref, kv_ref, new_ref, pick_ref, out_ref):
    r = pl.program_id(0)
    steps = q_ref.shape[1]
    head_dim = q_ref.shape[3]
    scale = head_dim ** (-0.5)
    keys = kv_ref[0, :, :head_dim]
    values = kv_ref[0, :, head_dim:]
    pos = lax.broadcasted_iota(jnp.int32, (1, kv_ref.shape[1]), 1)
    contract = (((1,), (1,)), ((), ()))
    for t in range(steps):
        lo = bounds_ref[(r * steps + t) * 2]
        hi = bounds_ref[(r * steps + t) * 2 + 1]
        query = q_ref[0, t]
        scores = lax.dot_general(query, keys, contract, preferred_element_type=jnp.float32) * scale
        allowed = (pos > lo) & (pos < hi)
        scores = jnp.where(allowed, scores, NEGATIVE)
        high_c = jnp.max(scores, axis=1, keepdims=True)
        weights = jnp.exp(scores - high_c).astype(jnp.bfloat16)
        total_c = jnp.sum(weights.astype(jnp.float32), axis=1, keepdims=True)
        sum_c = jnp.dot(weights, values, preferred_element_type=jnp.float32)
        entries = new_ref[0, t]
        fresh = lax.dot_general(
            query, entries[:, :head_dim], contract, preferred_element_type=jnp.float32
        ) * scale
        fresh = jnp.where(pick_ref[t] > 0, fresh, NEGATIVE)
        high_n = jnp.max(fresh, axis=1, keepdims=True)
        fresh_w = jnp.exp(fresh - high_n).astype(jnp.bfloat16)
        total_n = jnp.sum(fresh_w.astype(jnp.float32), axis=1, keepdims=True)
        sum_n = jnp.dot(fresh_w, entries[:, head_dim:], preferred_element_type=jnp.float32)
        highest = jnp.maximum(high_c, high_n)
        scale_c = jnp.exp(high_c - highest)
        scale_n = jnp.exp(high_n - highest)
        totals = total_c * scale_c + total_n * scale_n
        weighted = sum_c * scale_c + sum_n * scale_n
        out_ref[0, t] = (weighted / totals).astype(out_ref.dtype)


def attend(bounds, queries, pages, entries, pick):
    rows, steps, count, head_dim = queries.shape
    span = pages.shape[1]
    flops = 4 * rows * steps * count * (span + entries.shape[2]) * head_dim
    return pl.pallas_call(
        attend_kernel,
        grid_spec=pltpu.PrefetchScalarGridSpec(
            num_scalar_prefetch=1,
            grid=(rows,),
            in_specs=[
                pl.BlockSpec((1, steps, count, head_dim), lambda r, b: (r, 0, 0, 0)),
                pl.BlockSpec((1, span, pages.shape[2]), lambda r, b: (r, 0, 0)),
                pl.BlockSpec((1,) + entries.shape[1:], lambda r, b: (r, 0, 0, 0)),
                pl.BlockSpec(pick.shape, lambda r, b: (0, 0, 0)),
            ],
            out_specs=pl.BlockSpec((1, steps, count, head_dim), lambda r, b: (r, 0, 0, 0)),
        ),
        out_shape=jax.ShapeDtypeStruct(queries.shape, jnp.bfloat16),
        cost_estimate=pl.CostEstimate(
            flops=flops,
            transcendentals=rows * steps * count * span,
            bytes_accessed=pages.size * 2 + queries.size * 4 + entries.size * 2,
        ),
    )(bounds, queries, pages, entries, pick)


def on_device(
    x_steps,
    lengths,
    perm,
    parents,
    table,
    pool,
    norm_attn,
    w_query,
    w_keyval,
    w_out,
    norm_mlp,
    w_gate,
    w_up,
    w_down,
):
    steps, rows, width = x_steps.shape
    head_dim = pool.shape[2] // 2
    heads = w_query.shape[1] // head_dim
    qwidth = heads * head_dim
    span = table.shape[1] * pool.shape[1]
    req_count = lax.axis_size("req")
    kv_count = lax.axis_size(KV)
    group = lax.axis_index("req")
    halves = lax.axis_size("zhi")
    half = lax.axis_index("zhi")
    beam = lax.axis_index("y") * 2 + lax.axis_index("zlo")
    member = member_of(beam, half, halves)
    per_group = halves * rows
    group_rows = kv_count * rows
    quota = rows // req_count
    swap = [(0, 1), (1, 0)]
    partner = [lax.ppermute(w, "zhi", swap) for w in (w_gate, w_up, w_down)]

    offsets = jnp.arange(rows, dtype=jnp.int32)
    slot_ids = group * per_group + half * rows + offsets
    placed = lax.dynamic_slice_in_dim(perm.reshape(req_count, per_group), half * rows, rows, 1)
    serving = lax.dynamic_index_in_dim(placed, group, 0, keepdims=False)
    target = jnp.sum(
        jnp.where(placed == slot_ids[None, :], jnp.arange(req_count, dtype=jnp.int32)[:, None], 0),
        axis=0,
    )
    anchor = serving // per_group
    send_order = jnp.argsort(target * rows + offsets)
    outgoing = x_steps[:, send_order].reshape(steps, req_count, quota, width)
    arrived = lax.all_to_all(outgoing, "req", split_axis=1, concat_axis=1, tiled=True).reshape(
        steps, rows, width
    )
    slot_req = perm.reshape(req_count, halves, rows) // (halves * rows)
    mine_req = slot_req[:, half, :][group]
    offset_of = jnp.sum(
        jnp.where(mine_req[None, :] == offsets[:, None], offsets[None, :], 0), axis=1
    )
    inputs = arrived

    normed = rms_round(inputs.reshape(steps * rows, width), norm_attn)
    query = jnp.dot(normed, w_query, preferred_element_type=jnp.float32).astype(jnp.bfloat16)
    fresh = jnp.dot(normed, w_keyval, preferred_element_type=jnp.float32).astype(jnp.bfloat16)
    packed = jnp.concatenate([query, fresh], axis=-1).reshape(steps, rows, qwidth + 2 * head_dim)
    mine = lax.all_to_all(
        jnp.broadcast_to(packed[None], (BEAMS,) + packed.shape), HALF, 0, 0, tiled=True
    )
    queries = mine[..., :qwidth].reshape(BEAMS, steps, rows, heads, head_dim)
    entries = mine[..., qwidth:]

    family = lax.dynamic_slice_in_dim(parents, group * group_rows, group_rows, 1).reshape(
        (steps, BEAMS // 2, halves, 2, rows)
    )
    family = lax.dynamic_index_in_dim(family, half, 2, keepdims=False).reshape(steps, BEAMS, rows)
    family = family[:, :, offset_of]
    own = jnp.broadcast_to(jnp.arange(BEAMS, dtype=jnp.int32)[:, None], (BEAMS, rows))
    cache_beam = own
    sources = []
    cache_beams = []
    listed = []
    for step_index in range(steps):
        cache_beam = follow(family[step_index], cache_beam)
        sources = [follow(family[step_index], source) for source in sources] + [own]
        cache_beams.append(cache_beam)
        picked = [pick_rows(source, entries[:, s]) for s, source in enumerate(sources)]
        picked += [jnp.zeros_like(picked[0])] * (steps - 1 - step_index)
        listed.append(jnp.stack(picked))
    held = jnp.stack(cache_beams, axis=1) == beam
    listed = jnp.stack(listed)

    length = lengths[serving[offset_of]]
    first_page = jnp.maximum(length - WINDOW + 1, 0) // PAGE
    device = group * kv_count + member
    pages = pool[table[offset_of] - device * pool.shape[0]].reshape(rows, span, 2 * head_dim)
    pages, partner = lax.optimization_barrier((pages, partner))
    gate_w = jnp.concatenate([w_gate, partner[0]], axis=1)
    up_w = jnp.concatenate([w_up, partner[1]], axis=1)
    down_w = jnp.concatenate([w_down, partner[2]], axis=0)
    scale = head_dim ** (-0.5)
    step_ids = jnp.arange(steps, dtype=jnp.int32)
    base = first_page * PAGE
    lo = length[:, None] + step_ids[None, :] - WINDOW - base[:, None]
    hi = jnp.broadcast_to((length - base)[:, None], (rows, steps))
    bounds = jnp.stack([lo, hi], axis=-1).reshape(rows * steps * 2)
    by_row = jnp.transpose(queries, (2, 1, 0, 3, 4)).reshape(rows, steps, BEAMS * heads, head_dim)
    entries_by_row = jnp.transpose(listed, (3, 0, 1, 2, 4)).reshape(
        rows, steps, steps * BEAMS, 2 * head_dim
    )
    row_beam = jnp.arange(BEAMS * heads, dtype=jnp.int32) // heads
    column = jnp.arange(steps * BEAMS, dtype=jnp.int32)
    pick = (
        (column[None, None, :] % BEAMS == row_beam[None, :, None])
        & (column[None, None, :] // BEAMS <= step_ids[:, None, None])
    ).astype(jnp.float32)
    attended = attend(bounds, by_row, pages, entries_by_row, pick)
    attended = jnp.transpose(attended.reshape(rows, steps, BEAMS, qwidth), (2, 1, 0, 3))
    attended = jnp.where(held[..., None], attended, jnp.zeros_like(attended))

    received = lax.all_to_all(attended, HALF, split_axis=0, concat_axis=0, tiled=True)
    attended_own = jnp.sum(received.astype(jnp.float32), axis=0).astype(jnp.bfloat16)

    current = inputs.reshape(steps * rows, width)
    residual = (
        current.astype(jnp.float32)
        + jnp.dot(attended_own.reshape(steps * rows, qwidth), w_out, preferred_element_type=jnp.float32)
    ).astype(jnp.bfloat16)
    by_req = jnp.swapaxes(residual.reshape(steps, rows, width), 0, 1).reshape(rows * steps, width)
    mlp_own = rms_round(by_req, norm_mlp)
    mlp_in = lax.all_to_all(
        jnp.broadcast_to(mlp_own[None], (BEAMS,) + mlp_own.shape), HALF, 0, 0, tiled=True
    ).reshape(BEAMS * rows * steps, width)
    gate = jnp.dot(mlp_in, gate_w, preferred_element_type=jnp.float32)
    upward = jnp.dot(mlp_in, up_w, preferred_element_type=jnp.float32)
    hidden = (jax.nn.gelu(gate, approximate=True) * upward).astype(jnp.bfloat16)
    own_row = jnp.arange(BEAMS * rows * steps, dtype=jnp.int32)
    select = (
        (own_row[:, None] // (rows * steps) == beam)
        & (own_row[:, None] % (rows * steps) == jnp.arange(rows * steps, dtype=jnp.int32)[None, :])
    ).astype(jnp.bfloat16)
    terms = jnp.dot(
        jnp.concatenate([hidden, select], axis=1),
        jnp.concatenate([down_w, by_req], axis=0),
        preferred_element_type=jnp.float32,
    ).astype(jnp.bfloat16)

    arrived_sums = lax.all_to_all(terms, HALF + ("req",), 0, 0, tiled=True).reshape(
        BEAMS, req_count, steps, width
    )
    per_group_sum = jnp.sum(arrived_sums.astype(jnp.float32), axis=0)
    served_by = slot_req[:, half, :] == group
    finished = jnp.sum(
        jnp.where(served_by[:, None, :, None], per_group_sum[:, :, None, :], 0.0), axis=0
    )
    return finished.astype(jnp.bfloat16)


def solution(mesh):
    req_count, kv_count = mesh.devices.shape
    halves = kv_count // BEAMS
    split = Mesh(
        mesh.devices.reshape(req_count, BEAMS // 2, halves, 2), ("req",) + KV
    )
    mesh = split
    ROWS = ("req",) + KV
    in_specs = (
        P(None, ROWS, None),
        P(),
        P(),
        P(),
        P(ROWS, None),
        P(ROWS, None, None),
        P(),
        P(),
        P(),
        P(),
        P(),
        P(None, KV),
        P(None, KV),
        P(KV, None),
    )
    out_specs = P(None, ROWS, None)
    return jax.shard_map(
        on_device, mesh=mesh, in_specs=in_specs, out_specs=out_specs, check_vma=False
    )
```

```python
import jax
import jax.numpy as jnp
from jax import lax
from jax.sharding import Mesh, PartitionSpec as P
from jax.experimental import pallas as pl
from jax.experimental.pallas import tpu as pltpu

WINDOW = 1024
PAGE = 128
BEAMS = 8


EPSILON = 1e-06
KV = ("y", "zhi", "zlo")
HALF = ("y", "zlo")
NEGATIVE = -1e30


def member_of(beam_index, half_index, halves):
    return beam_index % 2 + 2 * half_index + 2 * halves * (beam_index // 2)


def rms_round(values, gain):
    wide = values.astype(jnp.float32)
    mean_square = jnp.mean(wide * wide, axis=-1, keepdims=True)
    return (wide * lax.rsqrt(mean_square + EPSILON) * gain).astype(jnp.bfloat16)


def rank_within(labels, offsets):
    earlier = (labels[None, :] == labels[:, None]) & (offsets[None, :] < offsets[:, None])
    return jnp.sum(earlier.astype(jnp.int32), axis=1)


def follow(index, table):
    picks = index[:, None, :] == jnp.arange(BEAMS, dtype=jnp.int32)[None, :, None]
    return jnp.sum(jnp.where(picks, table[None, :, :], 0), axis=1)


def pick_rows(index, table):
    picks = index[:, None, :] == jnp.arange(BEAMS, dtype=jnp.int32)[None, :, None]
    return jnp.sum(jnp.where(picks[..., None], table[None, :, :, :], 0), axis=1).astype(table.dtype)


def attend_kernel(count_ref, q_ref, lo_ref, hi_ref, kv_ref, new_ref, pick_ref, out_ref):
    r = pl.program_id(0)
    chunks = q_ref.shape[1]
    head_dim = q_ref.shape[3]
    scale = head_dim ** (-0.5)
    keys = kv_ref[0, :, :head_dim]
    values = kv_ref[0, :, head_dim:]
    pos = lax.broadcasted_iota(jnp.int32, (1, kv_ref.shape[1]), 1)
    contract = (((1,), (1,)), ((), ()))
    for c in range(chunks):

        @pl.when(c < count_ref[r])
        def _(c=c):
            query = q_ref[0, c]
            scores = lax.dot_general(query, keys, contract, preferred_element_type=jnp.float32) * scale
            allowed = (pos > lo_ref[0, c]) & (pos < hi_ref[0, c])
            scores = jnp.where(allowed, scores, NEGATIVE)
            high_c = jnp.max(scores, axis=1, keepdims=True)
            weights = jnp.exp(scores - high_c).astype(jnp.bfloat16)
            total_c = jnp.sum(weights.astype(jnp.float32), axis=1, keepdims=True)
            sum_c = jnp.dot(weights, values, preferred_element_type=jnp.float32)
            entries = new_ref[0, c]
            fresh = lax.dot_general(
                query, entries[:, :head_dim], contract, preferred_element_type=jnp.float32
            ) * scale
            fresh = jnp.where(pick_ref[0, c] > 0, fresh, NEGATIVE)
            high_n = jnp.max(fresh, axis=1, keepdims=True)
            fresh_w = jnp.exp(fresh - high_n).astype(jnp.bfloat16)
            total_n = jnp.sum(fresh_w.astype(jnp.float32), axis=1, keepdims=True)
            sum_n = jnp.dot(fresh_w, entries[:, head_dim:], preferred_element_type=jnp.float32)
            highest = jnp.maximum(high_c, high_n)
            scale_c = jnp.exp(high_c - highest)
            scale_n = jnp.exp(high_n - highest)
            totals = total_c * scale_c + total_n * scale_n
            weighted = sum_c * scale_c + sum_n * scale_n
            out_ref[0, c] = (weighted / totals).astype(out_ref.dtype)

        @pl.when(c >= count_ref[r])
        def _(c=c):
            out_ref[0, c] = jnp.zeros(out_ref.shape[2:], out_ref.dtype)


def attend(count, queries, lo, hi, pages, entries, pick):
    rows, chunks, count_rows, head_dim = queries.shape
    span = pages.shape[1]
    flops = 4 * rows * chunks * count_rows * (span + entries.shape[2]) * head_dim
    block = lambda *shape: pl.BlockSpec((1,) + shape, lambda r, n: (r,) + (0,) * len(shape))
    return pl.pallas_call(
        attend_kernel,
        grid_spec=pltpu.PrefetchScalarGridSpec(
            num_scalar_prefetch=1,
            grid=(rows,),
            in_specs=[
                block(chunks, count_rows, head_dim),
                block(chunks, count_rows, 1),
                block(chunks, count_rows, 1),
                block(span, pages.shape[2]),
                block(*entries.shape[1:]),
                block(*pick.shape[1:]),
            ],
            out_specs=block(chunks, count_rows, head_dim),
        ),
        out_shape=jax.ShapeDtypeStruct(queries.shape, jnp.bfloat16),
        cost_estimate=pl.CostEstimate(
            flops=flops // 3,
            transcendentals=rows * chunks * count_rows * span // 3,
            bytes_accessed=pages.size * 2 + queries.size * 4 + entries.size * 2 + pick.size * 4,
        ),
    )(count, queries, lo, hi, pages, entries, pick)


def on_device(
    x_steps,
    lengths,
    perm,
    parents,
    table,
    pool,
    norm_attn,
    w_query,
    w_keyval,
    w_out,
    norm_mlp,
    w_gate,
    w_up,
    w_down,
):
    steps, rows, width = x_steps.shape
    head_dim = pool.shape[2] // 2
    heads = w_query.shape[1] // head_dim
    qwidth = heads * head_dim
    span = table.shape[1] * pool.shape[1]
    req_count = lax.axis_size("req")
    kv_count = lax.axis_size(KV)
    group = lax.axis_index("req")
    halves = lax.axis_size("zhi")
    half = lax.axis_index("zhi")
    beam = lax.axis_index("y") * 2 + lax.axis_index("zlo")
    member = member_of(beam, half, halves)
    per_group = halves * rows
    group_rows = kv_count * rows
    quota = rows // req_count

    offsets = jnp.arange(rows, dtype=jnp.int32)
    slot_ids = group * per_group + half * rows + offsets
    placed = lax.dynamic_slice_in_dim(perm.reshape(req_count, per_group), half * rows, rows, 1)
    serving = lax.dynamic_index_in_dim(placed, group, 0, keepdims=False)
    target = jnp.sum(
        jnp.where(placed == slot_ids[None, :], jnp.arange(req_count, dtype=jnp.int32)[:, None], 0),
        axis=0,
    )
    anchor = serving // per_group
    send_order = jnp.argsort(target * rows + offsets)
    outgoing = x_steps[:, send_order].reshape(steps, req_count, quota, width)
    arrived = lax.all_to_all(outgoing, "req", split_axis=1, concat_axis=1, tiled=True).reshape(
        steps, rows, width
    )
    slot_req = perm.reshape(req_count, halves, rows) // (halves * rows)
    mine_req = slot_req[:, half, :][group]
    offset_of = jnp.sum(
        jnp.where(mine_req[None, :] == offsets[:, None], offsets[None, :], 0), axis=1
    )
    inputs = arrived

    normed = rms_round(inputs.reshape(steps * rows, width), norm_attn)
    query = jnp.dot(normed, w_query, preferred_element_type=jnp.float32).astype(jnp.bfloat16)
    fresh = jnp.dot(normed, w_keyval, preferred_element_type=jnp.float32).astype(jnp.bfloat16)
    packed = jnp.concatenate([query, fresh], axis=-1).reshape(steps, rows, qwidth + 2 * head_dim)
    mine = lax.all_to_all(
        jnp.broadcast_to(packed[None], (BEAMS,) + packed.shape), HALF, 0, 0, tiled=True
    )
    queries = mine[..., :qwidth].reshape(BEAMS, steps, rows, heads, head_dim)
    entries = mine[..., qwidth:]

    family = lax.dynamic_slice_in_dim(parents, group * group_rows, group_rows, 1).reshape(
        (steps, BEAMS // 2, halves, 2, rows)
    )
    family = lax.dynamic_index_in_dim(family, half, 2, keepdims=False).reshape(steps, BEAMS, rows)
    family = family[:, :, offset_of]
    own = jnp.broadcast_to(jnp.arange(BEAMS, dtype=jnp.int32)[:, None], (BEAMS, rows))
    cache_beam = own
    sources = []
    cache_beams = []
    listed = []
    for step_index in range(steps):
        cache_beam = follow(family[step_index], cache_beam)
        sources = [follow(family[step_index], source) for source in sources] + [own]
        cache_beams.append(cache_beam)
        picked = [pick_rows(source, entries[:, s]) for s, source in enumerate(sources)]
        picked += [jnp.zeros_like(picked[0])] * (steps - 1 - step_index)
        listed.append(jnp.stack(picked))
    held = jnp.stack(cache_beams, axis=1) == beam
    listed = jnp.stack(listed)

    length = lengths[serving[offset_of]]
    first_page = jnp.maximum(length - WINDOW + 1, 0) // PAGE
    device = group * kv_count + member
    pages = pool[table[offset_of] - device * pool.shape[0]].reshape(rows, span, 2 * head_dim)
    scale = head_dim ** (-0.5)
    step_ids = jnp.arange(steps, dtype=jnp.int32)
    base = first_page * PAGE
    lo = length[:, None] + step_ids[None, :] - WINDOW - base[:, None]
    hi = jnp.broadcast_to((length - base)[:, None], (rows, steps))
    pairs = steps * BEAMS
    held_by_row = jnp.transpose(held, (2, 1, 0)).reshape(rows, pairs)
    pair_ids = jnp.arange(pairs, dtype=jnp.int32)
    order = jnp.argsort(jnp.where(held_by_row, pair_ids[None, :], pair_ids[None, :] + pairs), axis=1)
    place = jnp.argsort(order, axis=1)
    count = (jnp.sum(held_by_row.astype(jnp.int32), axis=1) + BEAMS - 1) // BEAMS
    pair_step = order // BEAMS
    q_by = jnp.transpose(queries, (2, 1, 0, 3, 4)).reshape(rows, pairs, heads * head_dim)
    q_c = jnp.take_along_axis(q_by, order[:, :, None], axis=1).reshape(
        rows, steps, BEAMS * heads, head_dim
    )
    lo_c = jnp.take_along_axis(lo, pair_step, axis=1)
    hi_c = jnp.take_along_axis(hi, pair_step, axis=1)
    lo_c = jnp.broadcast_to(lo_c[:, :, None], (rows, pairs, heads)).reshape(rows, steps, BEAMS * heads, 1)
    hi_c = jnp.broadcast_to(hi_c[:, :, None], (rows, pairs, heads)).reshape(rows, steps, BEAMS * heads, 1)
    entries_by = jnp.transpose(listed, (3, 0, 2, 1, 4)).reshape(rows, pairs, steps, 2 * head_dim)
    entries_c = jnp.take_along_axis(entries_by, order[:, :, None, None], axis=1)
    entries_c = jnp.transpose(
        entries_c.reshape(rows, steps, BEAMS, steps, 2 * head_dim), (0, 1, 3, 2, 4)
    ).reshape(rows, steps, steps * BEAMS, 2 * head_dim)
    slot_in_chunk = pair_ids % BEAMS
    column = jnp.arange(steps * BEAMS, dtype=jnp.int32)
    pick = (
        (column[None, None, None, :] % BEAMS == slot_in_chunk[None, :, None, None])
        & (column[None, None, None, :] // BEAMS <= pair_step[:, :, None, None])
    )
    pick = jnp.broadcast_to(pick, (rows, pairs, heads, steps * BEAMS)).astype(jnp.float32).reshape(
        rows, steps, BEAMS * heads, steps * BEAMS
    )
    out_c = attend(count, q_c, lo_c, hi_c, pages, entries_c, pick).reshape(rows, pairs, qwidth)
    attended = jnp.take_along_axis(out_c, place[:, :, None], axis=1).reshape(
        rows, steps, BEAMS, qwidth
    )
    attended = jnp.transpose(attended, (2, 1, 0, 3))
    attended = jnp.where(held[..., None], attended, jnp.zeros_like(attended))

    received = lax.all_to_all(attended, HALF, split_axis=0, concat_axis=0, tiled=True)
    attended_own = jnp.sum(received.astype(jnp.float32), axis=0).astype(jnp.bfloat16)

    current = inputs.reshape(steps * rows, width)
    residual = (
        current.astype(jnp.float32)
        + jnp.dot(attended_own.reshape(steps * rows, qwidth), w_out, preferred_element_type=jnp.float32)
    ).astype(jnp.bfloat16)
    by_req = jnp.swapaxes(residual.reshape(steps, rows, width), 0, 1).reshape(rows * steps, width)
    mlp_own = rms_round(by_req, norm_mlp)
    mlp_in = lax.all_to_all(
        jnp.broadcast_to(mlp_own[None], (kv_count,) + mlp_own.shape), KV, 0, 0, tiled=True
    ).reshape(kv_count * rows * steps, width)
    gate = jnp.dot(mlp_in, w_gate, preferred_element_type=jnp.float32)
    upward = jnp.dot(mlp_in, w_up, preferred_element_type=jnp.float32)
    hidden = (jax.nn.gelu(gate, approximate=True) * upward).astype(jnp.bfloat16)
    own_row = jnp.arange(kv_count * rows * steps, dtype=jnp.int32)
    select = (
        (own_row[:, None] // (rows * steps) == member)
        & (own_row[:, None] % (rows * steps) == jnp.arange(rows * steps, dtype=jnp.int32)[None, :])
    ).astype(jnp.bfloat16)
    terms = jnp.dot(
        jnp.concatenate([hidden, select], axis=1),
        jnp.concatenate([w_down, by_req], axis=0),
        preferred_element_type=jnp.float32,
    ).astype(jnp.bfloat16)

    leaving = terms
    arrived_sums = lax.all_to_all(leaving, KV + ("req",), 0, 0, tiled=True).reshape(
        kv_count, req_count, steps, width
    )
    per_group_sum = jnp.sum(arrived_sums.astype(jnp.float32), axis=0)
    served_by = slot_req[:, half, :] == group
    finished = jnp.sum(
        jnp.where(served_by[:, None, :, None], per_group_sum[:, :, None, :], 0.0), axis=0
    )
    return finished.astype(jnp.bfloat16)


def solution(mesh):
    req_count, kv_count = mesh.devices.shape
    halves = kv_count // BEAMS
    split = Mesh(
        mesh.devices.reshape(req_count, BEAMS // 2, halves, 2), ("req",) + KV
    )
    mesh = split
    ROWS = ("req",) + KV
    in_specs = (
        P(None, ROWS, None),
        P(),
        P(),
        P(),
        P(ROWS, None),
        P(ROWS, None, None),
        P(),
        P(),
        P(),
        P(),
        P(),
        P(None, KV),
        P(None, KV),
        P(KV, None),
    )
    out_specs = P(None, ROWS, None)
    return jax.shard_map(
        on_device, mesh=mesh, in_specs=in_specs, out_specs=out_specs, check_vma=False
    )
```

```python
import jax
import jax.numpy as jnp
from jax import lax
from jax.sharding import Mesh, PartitionSpec as P
from jax.experimental import pallas as pl
from jax.experimental.pallas import tpu as pltpu

WINDOW = 1024
PAGE = 128
BEAMS = 8


EPSILON = 1e-06
KV = ("y", "zhi", "zlo")
HALF = ("y", "zlo")
NEGATIVE = -1e30


def member_of(beam_index, half_index, halves):
    return beam_index % 2 + 2 * half_index + 2 * halves * (beam_index // 2)


def rms_round(values, gain):
    wide = values.astype(jnp.float32)
    mean_square = jnp.mean(wide * wide, axis=-1, keepdims=True)
    return (wide * lax.rsqrt(mean_square + EPSILON) * gain).astype(jnp.bfloat16)


def rank_within(labels, offsets):
    earlier = (labels[None, :] == labels[:, None]) & (offsets[None, :] < offsets[:, None])
    return jnp.sum(earlier.astype(jnp.int32), axis=1)


def follow(index, table):
    picks = index[:, None, :] == jnp.arange(BEAMS, dtype=jnp.int32)[None, :, None]
    return jnp.sum(jnp.where(picks, table[None, :, :], 0), axis=1)


def pick_rows(index, table):
    picks = index[:, None, :] == jnp.arange(BEAMS, dtype=jnp.int32)[None, :, None]
    return jnp.sum(jnp.where(picks[..., None], table[None, :, :, :], 0), axis=1).astype(table.dtype)


def attend_kernel(bounds_ref, used_ref, q_ref, kv_ref, new_ref, pick_ref, out_ref):
    r = pl.program_id(0)
    steps = q_ref.shape[1]
    head_dim = q_ref.shape[3]
    scale = head_dim ** (-0.5)
    keys = kv_ref[0, :, :head_dim]
    values = kv_ref[0, :, head_dim:]
    pos = lax.broadcasted_iota(jnp.int32, (1, kv_ref.shape[1]), 1)
    contract = (((1,), (1,)), ((), ()))
    for t in range(steps):

        @pl.when(used_ref[r * steps + t] != 0)
        def _(t=t):
            lo = bounds_ref[(r * steps + t) * 2]
            hi = bounds_ref[(r * steps + t) * 2 + 1]
            query = q_ref[0, t]
            scores = lax.dot_general(query, keys, contract, preferred_element_type=jnp.float32) * scale
            allowed = (pos > lo) & (pos < hi)
            scores = jnp.where(allowed, scores, NEGATIVE)
            high_c = jnp.max(scores, axis=1, keepdims=True)
            weights = jnp.exp(scores - high_c).astype(jnp.bfloat16)
            total_c = jnp.sum(weights.astype(jnp.float32), axis=1, keepdims=True)
            sum_c = jnp.dot(weights, values, preferred_element_type=jnp.float32)
            entries = new_ref[0, t]
            fresh = lax.dot_general(
                query, entries[:, :head_dim], contract, preferred_element_type=jnp.float32
            ) * scale
            fresh = jnp.where(pick_ref[t] > 0, fresh, NEGATIVE)
            high_n = jnp.max(fresh, axis=1, keepdims=True)
            fresh_w = jnp.exp(fresh - high_n).astype(jnp.bfloat16)
            total_n = jnp.sum(fresh_w.astype(jnp.float32), axis=1, keepdims=True)
            sum_n = jnp.dot(fresh_w, entries[:, head_dim:], preferred_element_type=jnp.float32)
            highest = jnp.maximum(high_c, high_n)
            scale_c = jnp.exp(high_c - highest)
            scale_n = jnp.exp(high_n - highest)
            totals = total_c * scale_c + total_n * scale_n
            weighted = sum_c * scale_c + sum_n * scale_n
            out_ref[0, t] = (weighted / totals).astype(out_ref.dtype)

        @pl.when(used_ref[r * steps + t] == 0)
        def _(t=t):
            out_ref[0, t] = jnp.zeros(out_ref.shape[2:], out_ref.dtype)


def attend(bounds, used, queries, pages, entries, pick):
    rows, steps, count, head_dim = queries.shape
    span = pages.shape[1]
    flops = 4 * rows * steps * count * (span + entries.shape[2]) * head_dim
    return pl.pallas_call(
        attend_kernel,
        grid_spec=pltpu.PrefetchScalarGridSpec(
            num_scalar_prefetch=2,
            grid=(rows,),
            in_specs=[
                pl.BlockSpec((1, steps, count, head_dim), lambda r, b, u: (r, 0, 0, 0)),
                pl.BlockSpec((1, span, pages.shape[2]), lambda r, b, u: (r, 0, 0)),
                pl.BlockSpec((1,) + entries.shape[1:], lambda r, b, u: (r, 0, 0, 0)),
                pl.BlockSpec(pick.shape, lambda r, b, u: (0, 0, 0)),
            ],
            out_specs=pl.BlockSpec((1, steps, count, head_dim), lambda r, b, u: (r, 0, 0, 0)),
        ),
        out_shape=jax.ShapeDtypeStruct(queries.shape, jnp.bfloat16),
        cost_estimate=pl.CostEstimate(
            flops=flops,
            transcendentals=rows * steps * count * span,
            bytes_accessed=pages.size * 2 + queries.size * 4 + entries.size * 2,
        ),
    )(bounds, used, queries, pages, entries, pick)


def on_device(
    x_steps,
    lengths,
    perm,
    parents,
    table,
    pool,
    norm_attn,
    w_query,
    w_keyval,
    w_out,
    norm_mlp,
    w_gate,
    w_up,
    w_down,
):
    steps, rows, width = x_steps.shape
    head_dim = pool.shape[2] // 2
    heads = w_query.shape[1] // head_dim
    qwidth = heads * head_dim
    span = table.shape[1] * pool.shape[1]
    req_count = lax.axis_size("req")
    kv_count = lax.axis_size(KV)
    group = lax.axis_index("req")
    halves = lax.axis_size("zhi")
    half = lax.axis_index("zhi")
    beam = lax.axis_index("y") * 2 + lax.axis_index("zlo")
    member = member_of(beam, half, halves)
    per_group = halves * rows
    group_rows = kv_count * rows
    quota = rows // req_count

    offsets = jnp.arange(rows, dtype=jnp.int32)
    slot_ids = group * per_group + half * rows + offsets
    placed = lax.dynamic_slice_in_dim(perm.reshape(req_count, per_group), half * rows, rows, 1)
    serving = lax.dynamic_index_in_dim(placed, group, 0, keepdims=False)
    target = jnp.sum(
        jnp.where(placed == slot_ids[None, :], jnp.arange(req_count, dtype=jnp.int32)[:, None], 0),
        axis=0,
    )
    anchor = serving // per_group
    send_order = jnp.argsort(target * rows + offsets)
    outgoing = x_steps[:, send_order].reshape(steps, req_count, quota, width)
    arrived = lax.all_to_all(outgoing, "req", split_axis=1, concat_axis=1, tiled=True).reshape(
        steps, rows, width
    )
    slot_req = perm.reshape(req_count, halves, rows) // (halves * rows)
    mine_req = slot_req[:, half, :][group]
    offset_of = jnp.sum(
        jnp.where(mine_req[None, :] == offsets[:, None], offsets[None, :], 0), axis=1
    )
    inputs = arrived

    normed = rms_round(inputs.reshape(steps * rows, width), norm_attn)
    query = jnp.dot(normed, w_query, preferred_element_type=jnp.float32).astype(jnp.bfloat16)
    fresh = jnp.dot(normed, w_keyval, preferred_element_type=jnp.float32).astype(jnp.bfloat16)
    packed = jnp.concatenate([query, fresh], axis=-1).reshape(steps, rows, qwidth + 2 * head_dim)
    mine = lax.all_to_all(
        jnp.broadcast_to(packed[None], (BEAMS,) + packed.shape), HALF, 0, 0, tiled=True
    )
    queries = mine[..., :qwidth].reshape(BEAMS, steps, rows, heads, head_dim)
    entries = mine[..., qwidth:]

    family = lax.dynamic_slice_in_dim(parents, group * group_rows, group_rows, 1).reshape(
        (steps, BEAMS // 2, halves, 2, rows)
    )
    family = lax.dynamic_index_in_dim(family, half, 2, keepdims=False).reshape(steps, BEAMS, rows)
    family = family[:, :, offset_of]
    own = jnp.broadcast_to(jnp.arange(BEAMS, dtype=jnp.int32)[:, None], (BEAMS, rows))
    cache_beam = own
    sources = []
    cache_beams = []
    listed = []
    for step_index in range(steps):
        cache_beam = follow(family[step_index], cache_beam)
        sources = [follow(family[step_index], source) for source in sources] + [own]
        cache_beams.append(cache_beam)
        picked = [pick_rows(source, entries[:, s]) for s, source in enumerate(sources)]
        picked += [jnp.zeros_like(picked[0])] * (steps - 1 - step_index)
        listed.append(jnp.stack(picked))
    held = jnp.stack(cache_beams, axis=1) == beam
    listed = jnp.stack(listed)

    length = lengths[serving[offset_of]]
    first_page = jnp.maximum(length - WINDOW + 1, 0) // PAGE
    device = group * kv_count + member
    pages = pool[table[offset_of] - device * pool.shape[0]].reshape(rows, span, 2 * head_dim)
    scale = head_dim ** (-0.5)
    step_ids = jnp.arange(steps, dtype=jnp.int32)
    base = first_page * PAGE
    lo = length[:, None] + step_ids[None, :] - WINDOW - base[:, None]
    hi = jnp.broadcast_to((length - base)[:, None], (rows, steps))
    bounds = jnp.stack([lo, hi], axis=-1).reshape(rows * steps * 2)
    by_row = jnp.transpose(queries, (2, 1, 0, 3, 4)).reshape(rows, steps, BEAMS * heads, head_dim)
    entries_by_row = jnp.transpose(listed, (3, 0, 1, 2, 4)).reshape(
        rows, steps, steps * BEAMS, 2 * head_dim
    )
    row_beam = jnp.arange(BEAMS * heads, dtype=jnp.int32) // heads
    column = jnp.arange(steps * BEAMS, dtype=jnp.int32)
    pick = (
        (column[None, None, :] % BEAMS == row_beam[None, :, None])
        & (column[None, None, :] // BEAMS <= step_ids[:, None, None])
    ).astype(jnp.float32)
    used = jnp.any(held, axis=0).T.astype(jnp.int32).reshape(rows * steps)
    attended = attend(bounds, used, by_row, pages, entries_by_row, pick)
    attended = jnp.transpose(attended.reshape(rows, steps, BEAMS, qwidth), (2, 1, 0, 3))
    attended = jnp.where(held[..., None], attended, jnp.zeros_like(attended))

    received = lax.all_to_all(attended, HALF, split_axis=0, concat_axis=0, tiled=True)
    attended_own = jnp.sum(received.astype(jnp.float32), axis=0).astype(jnp.bfloat16)

    current = inputs.reshape(steps * rows, width)
    residual = (
        current.astype(jnp.float32)
        + jnp.dot(attended_own.reshape(steps * rows, qwidth), w_out, preferred_element_type=jnp.float32)
    ).astype(jnp.bfloat16)
    by_req = jnp.swapaxes(residual.reshape(steps, rows, width), 0, 1).reshape(rows * steps, width)
    mlp_own = rms_round(by_req, norm_mlp)
    mlp_in = lax.all_to_all(
        jnp.broadcast_to(mlp_own[None], (kv_count,) + mlp_own.shape), KV, 0, 0, tiled=True
    ).reshape(kv_count * rows * steps, width)
    gate = jnp.dot(mlp_in, w_gate, preferred_element_type=jnp.float32)
    upward = jnp.dot(mlp_in, w_up, preferred_element_type=jnp.float32)
    hidden = (jax.nn.gelu(gate, approximate=True) * upward).astype(jnp.bfloat16)
    own_row = jnp.arange(kv_count * rows * steps, dtype=jnp.int32)
    select = (
        (own_row[:, None] // (rows * steps) == member)
        & (own_row[:, None] % (rows * steps) == jnp.arange(rows * steps, dtype=jnp.int32)[None, :])
    ).astype(jnp.bfloat16)
    terms = jnp.dot(
        jnp.concatenate([hidden, select], axis=1),
        jnp.concatenate([w_down, by_req], axis=0),
        preferred_element_type=jnp.float32,
    ).astype(jnp.bfloat16)

    leaving = terms
    arrived_sums = lax.all_to_all(leaving, KV + ("req",), 0, 0, tiled=True).reshape(
        kv_count, req_count, steps, width
    )
    per_group_sum = jnp.sum(arrived_sums.astype(jnp.float32), axis=0)
    served_by = slot_req[:, half, :] == group
    finished = jnp.sum(
        jnp.where(served_by[:, None, :, None], per_group_sum[:, :, None, :], 0.0), axis=0
    )
    return finished.astype(jnp.bfloat16)


def solution(mesh):
    req_count, kv_count = mesh.devices.shape
    halves = kv_count // BEAMS
    split = Mesh(
        mesh.devices.reshape(req_count, BEAMS // 2, halves, 2), ("req",) + KV
    )
    mesh = split
    ROWS = ("req",) + KV
    in_specs = (
        P(None, ROWS, None),
        P(),
        P(),
        P(),
        P(ROWS, None),
        P(ROWS, None, None),
        P(),
        P(),
        P(),
        P(),
        P(),
        P(None, KV),
        P(None, KV),
        P(KV, None),
    )
    out_specs = P(None, ROWS, None)
    return jax.shard_map(
        on_device, mesh=mesh, in_specs=in_specs, out_specs=out_specs, check_vma=False
    )
```

```python
import jax
import jax.numpy as jnp
from jax import lax
from jax.sharding import Mesh, PartitionSpec as P
from jax.experimental import pallas as pl
from jax.experimental.pallas import tpu as pltpu

WINDOW = 1024
PAGE = 128
BEAMS = 8


EPSILON = 1e-06
KV = ("y", "zhi", "zlo")
HALF = ("y", "zlo")
NEGATIVE = -1e30


def member_of(beam_index, half_index, halves):
    return beam_index % 2 + 2 * half_index + 2 * halves * (beam_index // 2)


def rms_round(values, gain):
    wide = values.astype(jnp.float32)
    mean_square = jnp.mean(wide * wide, axis=-1, keepdims=True)
    return (wide * lax.rsqrt(mean_square + EPSILON) * gain).astype(jnp.bfloat16)


def rank_within(labels, offsets):
    earlier = (labels[None, :] == labels[:, None]) & (offsets[None, :] < offsets[:, None])
    return jnp.sum(earlier.astype(jnp.int32), axis=1)


def follow(index, table):
    picks = index[:, None, :] == jnp.arange(BEAMS, dtype=jnp.int32)[None, :, None]
    return jnp.sum(jnp.where(picks, table[None, :, :], 0), axis=1)


def pick_rows(index, table):
    picks = index[:, None, :] == jnp.arange(BEAMS, dtype=jnp.int32)[None, :, None]
    return jnp.sum(jnp.where(picks[..., None], table[None, :, :, :], 0), axis=1).astype(table.dtype)


def attend_kernel(bounds_ref, used_ref, q_ref, kv_ref, new_ref, pick_ref, out_ref):
    r = pl.program_id(0)
    steps = q_ref.shape[1]
    head_dim = q_ref.shape[3]
    scale = head_dim ** (-0.5)
    keys = kv_ref[0, :, :head_dim]
    values = kv_ref[0, :, head_dim:]
    pos = lax.broadcasted_iota(jnp.int32, (1, kv_ref.shape[1]), 1)
    contract = (((1,), (1,)), ((), ()))
    for t in range(steps):

        @pl.when(used_ref[r * steps + t] != 0)
        def _(t=t):
            lo = bounds_ref[(r * steps + t) * 2]
            hi = bounds_ref[(r * steps + t) * 2 + 1]
            query = q_ref[0, t]
            scores = lax.dot_general(query, keys, contract, preferred_element_type=jnp.float32) * scale
            allowed = (pos > lo) & (pos < hi)
            scores = jnp.where(allowed, scores, NEGATIVE)
            high_c = jnp.max(scores, axis=1, keepdims=True)
            weights = jnp.exp(scores - high_c).astype(jnp.bfloat16)
            total_c = jnp.sum(weights.astype(jnp.float32), axis=1, keepdims=True)
            sum_c = jnp.dot(weights, values, preferred_element_type=jnp.float32)
            entries = new_ref[0, t]
            fresh = lax.dot_general(
                query, entries[:, :head_dim], contract, preferred_element_type=jnp.float32
            ) * scale
            fresh = jnp.where(pick_ref[t] > 0, fresh, NEGATIVE)
            high_n = jnp.max(fresh, axis=1, keepdims=True)
            fresh_w = jnp.exp(fresh - high_n).astype(jnp.bfloat16)
            total_n = jnp.sum(fresh_w.astype(jnp.float32), axis=1, keepdims=True)
            sum_n = jnp.dot(fresh_w, entries[:, head_dim:], preferred_element_type=jnp.float32)
            highest = jnp.maximum(high_c, high_n)
            scale_c = jnp.exp(high_c - highest)
            scale_n = jnp.exp(high_n - highest)
            totals = total_c * scale_c + total_n * scale_n
            weighted = sum_c * scale_c + sum_n * scale_n
            out_ref[0, t] = (weighted / totals).astype(out_ref.dtype)

        @pl.when(used_ref[r * steps + t] == 0)
        def _(t=t):
            out_ref[0, t] = jnp.zeros(out_ref.shape[2:], out_ref.dtype)


def attend(bounds, used, queries, pages, entries, pick):
    rows, steps, count, head_dim = queries.shape
    span = pages.shape[1]
    flops = 4 * rows * steps * count * (span + entries.shape[2]) * head_dim
    return pl.pallas_call(
        attend_kernel,
        grid_spec=pltpu.PrefetchScalarGridSpec(
            num_scalar_prefetch=2,
            grid=(rows,),
            in_specs=[
                pl.BlockSpec((1, steps, count, head_dim), lambda r, b, u: (r, 0, 0, 0)),
                pl.BlockSpec((1, span, pages.shape[2]), lambda r, b, u: (r, 0, 0)),
                pl.BlockSpec((1,) + entries.shape[1:], lambda r, b, u: (r, 0, 0, 0)),
                pl.BlockSpec(pick.shape, lambda r, b, u: (0, 0, 0)),
            ],
            out_specs=pl.BlockSpec((1, steps, count, head_dim), lambda r, b, u: (r, 0, 0, 0)),
        ),
        out_shape=jax.ShapeDtypeStruct(queries.shape, jnp.bfloat16),
        cost_estimate=pl.CostEstimate(
            flops=flops,
            transcendentals=rows * steps * count * span,
            bytes_accessed=pages.size * 2 + queries.size * 4 + entries.size * 2,
        ),
    )(bounds, used, queries, pages, entries, pick)


def on_device(
    x_steps,
    lengths,
    perm,
    parents,
    table,
    pool,
    norm_attn,
    w_query,
    w_keyval,
    w_out,
    norm_mlp,
    w_gate,
    w_up,
    w_down,
):
    steps, rows, width = x_steps.shape
    head_dim = pool.shape[2] // 2
    heads = w_query.shape[1] // head_dim
    qwidth = heads * head_dim
    span = table.shape[1] * pool.shape[1]
    req_count = lax.axis_size("req")
    kv_count = lax.axis_size(KV)
    group = lax.axis_index("req")
    halves = lax.axis_size("zhi")
    half = lax.axis_index("zhi")
    beam = lax.axis_index("y") * 2 + lax.axis_index("zlo")
    member = member_of(beam, half, halves)
    per_group = halves * rows
    group_rows = kv_count * rows
    quota = rows // req_count

    offsets = jnp.arange(rows, dtype=jnp.int32)
    slot_ids = group * per_group + half * rows + offsets
    placed = lax.dynamic_slice_in_dim(perm.reshape(req_count, per_group), half * rows, rows, 1)
    serving = lax.dynamic_index_in_dim(placed, group, 0, keepdims=False)
    target = jnp.sum(
        jnp.where(placed == slot_ids[None, :], jnp.arange(req_count, dtype=jnp.int32)[:, None], 0),
        axis=0,
    )
    slot_req = perm.reshape(req_count, halves, rows) // (halves * rows)
    mine_req = slot_req[:, half, :][group]
    offset_of = jnp.sum(
        jnp.where(mine_req[None, :] == offsets[:, None], offsets[None, :], 0), axis=1
    )

    normed = rms_round(x_steps.reshape(steps * rows, width), norm_attn)
    query = jnp.dot(normed, w_query, preferred_element_type=jnp.float32).astype(jnp.bfloat16)
    fresh = jnp.dot(normed, w_keyval, preferred_element_type=jnp.float32).astype(jnp.bfloat16)
    packed = jnp.concatenate(
        [x_steps.reshape(steps * rows, width), query, fresh], axis=-1
    ).reshape(steps, rows, width + qwidth + 2 * head_dim)
    send_slot = jnp.sum(
        jnp.where(target[None, :] == offsets[:, None], offsets[None, :], 0), axis=1
    )
    sending = jnp.swapaxes(jnp.take(packed, send_slot, axis=1), 0, 1)
    sending = jnp.broadcast_to(sending[:, None], (req_count, BEAMS) + sending.shape[1:])
    arrived = lax.all_to_all(
        sending.reshape((req_count * BEAMS,) + sending.shape[2:]), ("req",) + HALF, 0, 0, tiled=True
    ).reshape((req_count, BEAMS) + sending.shape[2:])
    inputs = jnp.swapaxes(lax.dynamic_index_in_dim(arrived, beam, 1, keepdims=False)[..., :width], 0, 1)
    mine = jnp.transpose(arrived[..., width:], (1, 2, 0, 3))
    queries = mine[..., :qwidth].reshape(BEAMS, steps, rows, heads, head_dim)
    entries = mine[..., qwidth:]

    family = lax.dynamic_slice_in_dim(parents, group * group_rows, group_rows, 1).reshape(
        (steps, BEAMS // 2, halves, 2, rows)
    )
    family = lax.dynamic_index_in_dim(family, half, 2, keepdims=False).reshape(steps, BEAMS, rows)
    family = family[:, :, offset_of]
    own = jnp.broadcast_to(jnp.arange(BEAMS, dtype=jnp.int32)[:, None], (BEAMS, rows))
    cache_beam = own
    sources = []
    cache_beams = []
    listed = []
    for step_index in range(steps):
        cache_beam = follow(family[step_index], cache_beam)
        sources = [follow(family[step_index], source) for source in sources] + [own]
        cache_beams.append(cache_beam)
        picked = [pick_rows(source, entries[:, s]) for s, source in enumerate(sources)]
        picked += [jnp.zeros_like(picked[0])] * (steps - 1 - step_index)
        listed.append(jnp.stack(picked))
    held = jnp.stack(cache_beams, axis=1) == beam
    listed = jnp.stack(listed)

    length = lengths[serving[offset_of]]
    first_page = jnp.maximum(length - WINDOW + 1, 0) // PAGE
    device = group * kv_count + member
    pages = pool[table[offset_of] - device * pool.shape[0]].reshape(rows, span, 2 * head_dim)
    scale = head_dim ** (-0.5)
    step_ids = jnp.arange(steps, dtype=jnp.int32)
    base = first_page * PAGE
    lo = length[:, None] + step_ids[None, :] - WINDOW - base[:, None]
    hi = jnp.broadcast_to((length - base)[:, None], (rows, steps))
    bounds = jnp.stack([lo, hi], axis=-1).reshape(rows * steps * 2)
    by_row = jnp.transpose(queries, (2, 1, 0, 3, 4)).reshape(rows, steps, BEAMS * heads, head_dim)
    entries_by_row = jnp.transpose(listed, (3, 0, 1, 2, 4)).reshape(
        rows, steps, steps * BEAMS, 2 * head_dim
    )
    row_beam = jnp.arange(BEAMS * heads, dtype=jnp.int32) // heads
    column = jnp.arange(steps * BEAMS, dtype=jnp.int32)
    pick = (
        (column[None, None, :] % BEAMS == row_beam[None, :, None])
        & (column[None, None, :] // BEAMS <= step_ids[:, None, None])
    ).astype(jnp.float32)
    used = jnp.any(held, axis=0).T.astype(jnp.int32).reshape(rows * steps)
    attended = attend(bounds, used, by_row, pages, entries_by_row, pick)
    attended = jnp.transpose(attended.reshape(rows, steps, BEAMS, qwidth), (2, 1, 0, 3))
    attended = jnp.where(held[..., None], attended, jnp.zeros_like(attended))

    received = lax.all_to_all(attended, HALF, split_axis=0, concat_axis=0, tiled=True)
    attended_own = jnp.sum(received.astype(jnp.float32), axis=0).astype(jnp.bfloat16)

    current = inputs.reshape(steps * rows, width)
    residual = (
        current.astype(jnp.float32)
        + jnp.dot(attended_own.reshape(steps * rows, qwidth), w_out, preferred_element_type=jnp.float32)
    ).astype(jnp.bfloat16)
    by_req = jnp.swapaxes(residual.reshape(steps, rows, width), 0, 1).reshape(rows * steps, width)
    mlp_own = rms_round(by_req, norm_mlp)
    mlp_in = lax.all_to_all(
        jnp.broadcast_to(mlp_own[None], (kv_count,) + mlp_own.shape), KV, 0, 0, tiled=True
    ).reshape(kv_count * rows * steps, width)
    gate = jnp.dot(mlp_in, w_gate, preferred_element_type=jnp.float32)
    upward = jnp.dot(mlp_in, w_up, preferred_element_type=jnp.float32)
    hidden = (jax.nn.gelu(gate, approximate=True) * upward).astype(jnp.bfloat16)
    own_row = jnp.arange(kv_count * rows * steps, dtype=jnp.int32)
    select = (
        (own_row[:, None] // (rows * steps) == member)
        & (own_row[:, None] % (rows * steps) == jnp.arange(rows * steps, dtype=jnp.int32)[None, :])
    ).astype(jnp.bfloat16)
    terms = jnp.dot(
        jnp.concatenate([hidden, select], axis=1),
        jnp.concatenate([w_down, by_req], axis=0),
        preferred_element_type=jnp.float32,
    ).astype(jnp.bfloat16)

    leaving = terms
    arrived_sums = lax.all_to_all(leaving, KV + ("req",), 0, 0, tiled=True).reshape(
        kv_count, req_count, steps, width
    )
    per_group_sum = jnp.sum(arrived_sums.astype(jnp.float32), axis=0)
    served_by = slot_req[:, half, :] == group
    finished = jnp.sum(
        jnp.where(served_by[:, None, :, None], per_group_sum[:, :, None, :], 0.0), axis=0
    )
    return finished.astype(jnp.bfloat16)


def solution(mesh):
    req_count, kv_count = mesh.devices.shape
    halves = kv_count // BEAMS
    split = Mesh(
        mesh.devices.reshape(req_count, BEAMS // 2, halves, 2), ("req",) + KV
    )
    mesh = split
    ROWS = ("req",) + KV
    in_specs = (
        P(None, ROWS, None),
        P(),
        P(),
        P(),
        P(ROWS, None),
        P(ROWS, None, None),
        P(),
        P(),
        P(),
        P(),
        P(),
        P(None, KV),
        P(None, KV),
        P(KV, None),
    )
    out_specs = P(None, ROWS, None)
    return jax.shard_map(
        on_device, mesh=mesh, in_specs=in_specs, out_specs=out_specs, check_vma=False
    )
```

```python
import jax
import jax.numpy as jnp
from jax import lax
from jax.sharding import Mesh, PartitionSpec as P
from jax.experimental import pallas as pl
from jax.experimental.pallas import tpu as pltpu

WINDOW = 1024
PAGE = 128
BEAMS = 8


EPSILON = 1e-06
KV = ("y", "zhi", "zlo")
HALF = ("y", "zlo")
NEGATIVE = -1e30


def member_of(beam_index, half_index, halves):
    return beam_index % 2 + 2 * half_index + 2 * halves * (beam_index // 2)


def rms_round(values, gain):
    wide = values.astype(jnp.float32)
    mean_square = jnp.mean(wide * wide, axis=-1, keepdims=True)
    return (wide * lax.rsqrt(mean_square + EPSILON) * gain).astype(jnp.bfloat16)


def rank_within(labels, offsets):
    earlier = (labels[None, :] == labels[:, None]) & (offsets[None, :] < offsets[:, None])
    return jnp.sum(earlier.astype(jnp.int32), axis=1)


def follow(index, table):
    picks = index[:, None, :] == jnp.arange(BEAMS, dtype=jnp.int32)[None, :, None]
    return jnp.sum(jnp.where(picks, table[None, :, :], 0), axis=1)


def pick_rows(index, table):
    picks = index[:, None, :] == jnp.arange(BEAMS, dtype=jnp.int32)[None, :, None]
    return jnp.sum(jnp.where(picks[..., None], table[None, :, :, :], 0), axis=1).astype(table.dtype)


def attend_kernel(bounds_ref, used_ref, q_ref, kv_ref, new_ref, pick_ref, out_ref):
    r = pl.program_id(0)
    steps = q_ref.shape[1]
    head_dim = q_ref.shape[3]
    scale = head_dim ** (-0.5)
    keys = kv_ref[0, :, :head_dim]
    values = kv_ref[0, :, head_dim:]
    pos = lax.broadcasted_iota(jnp.int32, (1, kv_ref.shape[1]), 1)
    contract = (((1,), (1,)), ((), ()))
    for t in range(steps):

        @pl.when(used_ref[r * steps + t] != 0)
        def _(t=t):
            lo = bounds_ref[(r * steps + t) * 2]
            hi = bounds_ref[(r * steps + t) * 2 + 1]
            query = q_ref[0, t]
            scores = lax.dot_general(query, keys, contract, preferred_element_type=jnp.float32) * scale
            allowed = (pos > lo) & (pos < hi)
            scores = jnp.where(allowed, scores, NEGATIVE)
            high_c = jnp.max(scores, axis=1, keepdims=True)
            weights = jnp.exp(scores - high_c).astype(jnp.bfloat16)
            total_c = jnp.sum(weights.astype(jnp.float32), axis=1, keepdims=True)
            sum_c = jnp.dot(weights, values, preferred_element_type=jnp.float32)
            entries = new_ref[0, t]
            fresh = lax.dot_general(
                query, entries[:, :head_dim], contract, preferred_element_type=jnp.float32
            ) * scale
            fresh = jnp.where(pick_ref[t] > 0, fresh, NEGATIVE)
            high_n = jnp.max(fresh, axis=1, keepdims=True)
            fresh_w = jnp.exp(fresh - high_n).astype(jnp.bfloat16)
            total_n = jnp.sum(fresh_w.astype(jnp.float32), axis=1, keepdims=True)
            sum_n = jnp.dot(fresh_w, entries[:, head_dim:], preferred_element_type=jnp.float32)
            highest = jnp.maximum(high_c, high_n)
            scale_c = jnp.exp(high_c - highest)
            scale_n = jnp.exp(high_n - highest)
            totals = total_c * scale_c + total_n * scale_n
            weighted = sum_c * scale_c + sum_n * scale_n
            out_ref[0, t] = (weighted / totals).astype(out_ref.dtype)

        @pl.when(used_ref[r * steps + t] == 0)
        def _(t=t):
            out_ref[0, t] = jnp.zeros(out_ref.shape[2:], out_ref.dtype)


def attend(bounds, used, queries, pages, entries, pick):
    rows, steps, count, head_dim = queries.shape
    span = pages.shape[1]
    flops = 4 * rows * steps * count * (span + entries.shape[2]) * head_dim
    return pl.pallas_call(
        attend_kernel,
        grid_spec=pltpu.PrefetchScalarGridSpec(
            num_scalar_prefetch=2,
            grid=(rows,),
            in_specs=[
                pl.BlockSpec((1, steps, count, head_dim), lambda r, b, u: (r, 0, 0, 0)),
                pl.BlockSpec((1, span, pages.shape[2]), lambda r, b, u: (r, 0, 0)),
                pl.BlockSpec((1,) + entries.shape[1:], lambda r, b, u: (r, 0, 0, 0)),
                pl.BlockSpec(pick.shape, lambda r, b, u: (0, 0, 0)),
            ],
            out_specs=pl.BlockSpec((1, steps, count, head_dim), lambda r, b, u: (r, 0, 0, 0)),
        ),
        out_shape=jax.ShapeDtypeStruct(queries.shape, jnp.bfloat16),
        cost_estimate=pl.CostEstimate(
            flops=flops,
            transcendentals=rows * steps * count * span,
            bytes_accessed=pages.size * 2 + queries.size * 4 + entries.size * 2,
        ),
    )(bounds, used, queries, pages, entries, pick)


def on_device(
    x_steps,
    lengths,
    perm,
    parents,
    table,
    pool,
    norm_attn,
    w_query,
    w_keyval,
    w_out,
    norm_mlp,
    w_gate,
    w_up,
    w_down,
):
    steps, rows, width = x_steps.shape
    head_dim = pool.shape[2] // 2
    heads = w_query.shape[1] // head_dim
    qwidth = heads * head_dim
    span = table.shape[1] * pool.shape[1]
    req_count = lax.axis_size("req")
    kv_count = lax.axis_size(KV)
    group = lax.axis_index("req")
    halves = lax.axis_size("zhi")
    half = lax.axis_index("zhi")
    beam = lax.axis_index("y") * 2 + lax.axis_index("zlo")
    member = member_of(beam, half, halves)
    per_group = halves * rows
    group_rows = kv_count * rows
    quota = rows // req_count

    offsets = jnp.arange(rows, dtype=jnp.int32)
    slot_ids = group * per_group + half * rows + offsets
    placed = lax.dynamic_slice_in_dim(perm.reshape(req_count, per_group), half * rows, rows, 1)
    serving = lax.dynamic_index_in_dim(placed, group, 0, keepdims=False)
    target = jnp.sum(
        jnp.where(placed == slot_ids[None, :], jnp.arange(req_count, dtype=jnp.int32)[:, None], 0),
        axis=0,
    )
    slot_req = perm.reshape(req_count, halves, rows) // (halves * rows)
    mine_req = slot_req[:, half, :][group]
    offset_of = jnp.sum(
        jnp.where(mine_req[None, :] == offsets[:, None], offsets[None, :], 0), axis=1
    )

    normed = rms_round(x_steps.reshape(steps * rows, width), norm_attn)
    query = jnp.dot(normed, w_query, preferred_element_type=jnp.float32).astype(jnp.bfloat16)
    fresh = jnp.dot(normed, w_keyval, preferred_element_type=jnp.float32).astype(jnp.bfloat16)
    packed = jnp.concatenate([query, fresh], axis=-1).reshape(steps, rows, qwidth + 2 * head_dim)
    send_slot = jnp.sum(
        jnp.where(target[None, :] == offsets[:, None], offsets[None, :], 0), axis=1
    )
    inputs = lax.all_to_all(
        jnp.take(x_steps, send_slot, axis=1), "req", split_axis=1, concat_axis=1, tiled=True
    )
    inputs, packed = lax.optimization_barrier((inputs, packed))
    sending = jnp.swapaxes(jnp.take(packed, send_slot, axis=1), 0, 1)
    sending = jnp.broadcast_to(sending[:, None], (req_count, BEAMS) + sending.shape[1:])
    arrived = lax.all_to_all(
        sending.reshape((req_count * BEAMS,) + sending.shape[2:]), ("req",) + HALF, 0, 0, tiled=True
    ).reshape((req_count, BEAMS) + sending.shape[2:])
    mine = jnp.transpose(arrived, (1, 2, 0, 3))
    queries = mine[..., :qwidth].reshape(BEAMS, steps, rows, heads, head_dim)
    entries = mine[..., qwidth:]

    family = lax.dynamic_slice_in_dim(parents, group * group_rows, group_rows, 1).reshape(
        (steps, BEAMS // 2, halves, 2, rows)
    )
    family = lax.dynamic_index_in_dim(family, half, 2, keepdims=False).reshape(steps, BEAMS, rows)
    family = family[:, :, offset_of]
    own = jnp.broadcast_to(jnp.arange(BEAMS, dtype=jnp.int32)[:, None], (BEAMS, rows))
    cache_beam = own
    sources = []
    cache_beams = []
    listed = []
    for step_index in range(steps):
        cache_beam = follow(family[step_index], cache_beam)
        sources = [follow(family[step_index], source) for source in sources] + [own]
        cache_beams.append(cache_beam)
        picked = [pick_rows(source, entries[:, s]) for s, source in enumerate(sources)]
        picked += [jnp.zeros_like(picked[0])] * (steps - 1 - step_index)
        listed.append(jnp.stack(picked))
    held = jnp.stack(cache_beams, axis=1) == beam
    listed = jnp.stack(listed)

    length = lengths[serving[offset_of]]
    first_page = jnp.maximum(length - WINDOW + 1, 0) // PAGE
    device = group * kv_count + member
    pages = pool[table[offset_of] - device * pool.shape[0]].reshape(rows, span, 2 * head_dim)
    scale = head_dim ** (-0.5)
    step_ids = jnp.arange(steps, dtype=jnp.int32)
    base = first_page * PAGE
    lo = length[:, None] + step_ids[None, :] - WINDOW - base[:, None]
    hi = jnp.broadcast_to((length - base)[:, None], (rows, steps))
    bounds = jnp.stack([lo, hi], axis=-1).reshape(rows * steps * 2)
    by_row = jnp.transpose(queries, (2, 1, 0, 3, 4)).reshape(rows, steps, BEAMS * heads, head_dim)
    entries_by_row = jnp.transpose(listed, (3, 0, 1, 2, 4)).reshape(
        rows, steps, steps * BEAMS, 2 * head_dim
    )
    row_beam = jnp.arange(BEAMS * heads, dtype=jnp.int32) // heads
    column = jnp.arange(steps * BEAMS, dtype=jnp.int32)
    pick = (
        (column[None, None, :] % BEAMS == row_beam[None, :, None])
        & (column[None, None, :] // BEAMS <= step_ids[:, None, None])
    ).astype(jnp.float32)
    used = jnp.any(held, axis=0).T.astype(jnp.int32).reshape(rows * steps)
    attended = attend(bounds, used, by_row, pages, entries_by_row, pick)
    attended = jnp.transpose(attended.reshape(rows, steps, BEAMS, qwidth), (2, 1, 0, 3))
    attended = jnp.where(held[..., None], attended, jnp.zeros_like(attended))

    received = lax.all_to_all(attended, HALF, split_axis=0, concat_axis=0, tiled=True)
    attended_own = jnp.sum(received.astype(jnp.float32), axis=0).astype(jnp.bfloat16)

    current = inputs.reshape(steps * rows, width)
    residual = (
        current.astype(jnp.float32)
        + jnp.dot(attended_own.reshape(steps * rows, qwidth), w_out, preferred_element_type=jnp.float32)
    ).astype(jnp.bfloat16)
    by_req = jnp.swapaxes(residual.reshape(steps, rows, width), 0, 1).reshape(rows * steps, width)
    mlp_own = rms_round(by_req, norm_mlp)
    mlp_in = lax.all_to_all(
        jnp.broadcast_to(mlp_own[None], (kv_count,) + mlp_own.shape), KV, 0, 0, tiled=True
    ).reshape(kv_count * rows * steps, width)
    gate = jnp.dot(mlp_in, w_gate, preferred_element_type=jnp.float32)
    upward = jnp.dot(mlp_in, w_up, preferred_element_type=jnp.float32)
    hidden = (jax.nn.gelu(gate, approximate=True) * upward).astype(jnp.bfloat16)
    own_row = jnp.arange(kv_count * rows * steps, dtype=jnp.int32)
    select = (
        (own_row[:, None] // (rows * steps) == member)
        & (own_row[:, None] % (rows * steps) == jnp.arange(rows * steps, dtype=jnp.int32)[None, :])
    ).astype(jnp.bfloat16)
    terms = jnp.dot(
        jnp.concatenate([hidden, select], axis=1),
        jnp.concatenate([w_down, by_req], axis=0),
        preferred_element_type=jnp.float32,
    ).astype(jnp.bfloat16)

    leaving = terms
    arrived_sums = lax.all_to_all(leaving, KV + ("req",), 0, 0, tiled=True).reshape(
        kv_count, req_count, steps, width
    )
    per_group_sum = jnp.sum(arrived_sums.astype(jnp.float32), axis=0)
    served_by = slot_req[:, half, :] == group
    finished = jnp.sum(
        jnp.where(served_by[:, None, :, None], per_group_sum[:, :, None, :], 0.0), axis=0
    )
    return finished.astype(jnp.bfloat16)


def solution(mesh):
    req_count, kv_count = mesh.devices.shape
    halves = kv_count // BEAMS
    split = Mesh(
        mesh.devices.reshape(req_count, BEAMS // 2, halves, 2), ("req",) + KV
    )
    mesh = split
    ROWS = ("req",) + KV
    in_specs = (
        P(None, ROWS, None),
        P(),
        P(),
        P(),
        P(ROWS, None),
        P(ROWS, None, None),
        P(),
        P(),
        P(),
        P(),
        P(),
        P(None, KV),
        P(None, KV),
        P(KV, None),
    )
    out_specs = P(None, ROWS, None)
    return jax.shard_map(
        on_device, mesh=mesh, in_specs=in_specs, out_specs=out_specs, check_vma=False
    )
```

```python
import jax
import jax.numpy as jnp
from jax import lax
from jax.sharding import Mesh, PartitionSpec as P
from jax.experimental import pallas as pl
from jax.experimental.pallas import tpu as pltpu

WINDOW = 1024
PAGE = 128
BEAMS = 8


EPSILON = 1e-06
KV = ("y", "zhi", "zlo")
HALF = ("y", "zlo")
NEGATIVE = -1e30


def member_of(beam_index, half_index, halves):
    return beam_index % 2 + 2 * half_index + 2 * halves * (beam_index // 2)


def rms_round(values, gain):
    wide = values.astype(jnp.float32)
    mean_square = jnp.mean(wide * wide, axis=-1, keepdims=True)
    return (wide * lax.rsqrt(mean_square + EPSILON) * gain).astype(jnp.bfloat16)


def rank_within(labels, offsets):
    earlier = (labels[None, :] == labels[:, None]) & (offsets[None, :] < offsets[:, None])
    return jnp.sum(earlier.astype(jnp.int32), axis=1)


def follow(index, table):
    picks = index[:, None, :] == jnp.arange(BEAMS, dtype=jnp.int32)[None, :, None]
    return jnp.sum(jnp.where(picks, table[None, :, :], 0), axis=1)


def pick_rows(index, table):
    picks = index[:, None, :] == jnp.arange(BEAMS, dtype=jnp.int32)[None, :, None]
    return jnp.sum(jnp.where(picks[..., None], table[None, :, :, :], 0), axis=1).astype(table.dtype)


def attend_kernel(bounds_ref, used_ref, q_ref, kv_ref, new_ref, pick_ref, out_ref):
    r = pl.program_id(0)
    steps = q_ref.shape[1]
    head_dim = q_ref.shape[3]
    scale = head_dim ** (-0.5)
    keys = kv_ref[0, :, :head_dim]
    values = kv_ref[0, :, head_dim:]
    pos = lax.broadcasted_iota(jnp.int32, (1, kv_ref.shape[1]), 1)
    contract = (((1,), (1,)), ((), ()))
    for t in range(steps):

        @pl.when(used_ref[r * steps + t] != 0)
        def _(t=t):
            lo = bounds_ref[(r * steps + t) * 2]
            hi = bounds_ref[(r * steps + t) * 2 + 1]
            query = q_ref[0, t]
            scores = lax.dot_general(query, keys, contract, preferred_element_type=jnp.float32) * scale
            allowed = (pos > lo) & (pos < hi)
            scores = jnp.where(allowed, scores, NEGATIVE)
            high_c = jnp.max(scores, axis=1, keepdims=True)
            weights = jnp.exp(scores - high_c).astype(jnp.bfloat16)
            total_c = jnp.sum(weights.astype(jnp.float32), axis=1, keepdims=True)
            sum_c = jnp.dot(weights, values, preferred_element_type=jnp.float32)
            entries = new_ref[0, t]
            fresh = lax.dot_general(
                query, entries[:, :head_dim], contract, preferred_element_type=jnp.float32
            ) * scale
            fresh = jnp.where(pick_ref[t] > 0, fresh, NEGATIVE)
            high_n = jnp.max(fresh, axis=1, keepdims=True)
            fresh_w = jnp.exp(fresh - high_n).astype(jnp.bfloat16)
            total_n = jnp.sum(fresh_w.astype(jnp.float32), axis=1, keepdims=True)
            sum_n = jnp.dot(fresh_w, entries[:, head_dim:], preferred_element_type=jnp.float32)
            highest = jnp.maximum(high_c, high_n)
            scale_c = jnp.exp(high_c - highest)
            scale_n = jnp.exp(high_n - highest)
            totals = total_c * scale_c + total_n * scale_n
            weighted = sum_c * scale_c + sum_n * scale_n
            out_ref[0, t] = (weighted / totals).astype(out_ref.dtype)

        @pl.when(used_ref[r * steps + t] == 0)
        def _(t=t):
            out_ref[0, t] = jnp.zeros(out_ref.shape[2:], out_ref.dtype)


def attend(bounds, used, queries, pages, entries, pick):
    rows, steps, count, head_dim = queries.shape
    span = pages.shape[1]
    flops = 4 * rows * steps * count * (span + entries.shape[2]) * head_dim
    return pl.pallas_call(
        attend_kernel,
        grid_spec=pltpu.PrefetchScalarGridSpec(
            num_scalar_prefetch=2,
            grid=(rows,),
            in_specs=[
                pl.BlockSpec((1, steps, count, head_dim), lambda r, b, u: (r, 0, 0, 0)),
                pl.BlockSpec((1, span, pages.shape[2]), lambda r, b, u: (r, 0, 0)),
                pl.BlockSpec((1,) + entries.shape[1:], lambda r, b, u: (r, 0, 0, 0)),
                pl.BlockSpec(pick.shape, lambda r, b, u: (0, 0, 0)),
            ],
            out_specs=pl.BlockSpec((1, steps, count, head_dim), lambda r, b, u: (r, 0, 0, 0)),
        ),
        out_shape=jax.ShapeDtypeStruct(queries.shape, jnp.bfloat16),
        cost_estimate=pl.CostEstimate(
            flops=flops,
            transcendentals=rows * steps * count * span,
            bytes_accessed=pages.size * 2 + queries.size * 4 + entries.size * 2,
        ),
    )(bounds, used, queries, pages, entries, pick)


def on_device(
    x_steps,
    lengths,
    perm,
    parents,
    table,
    pool,
    norm_attn,
    w_query,
    w_keyval,
    w_out,
    norm_mlp,
    w_gate,
    w_up,
    w_down,
):
    steps, rows, width = x_steps.shape
    head_dim = pool.shape[2] // 2
    heads = w_query.shape[1] // head_dim
    qwidth = heads * head_dim
    span = table.shape[1] * pool.shape[1]
    req_count = lax.axis_size("req")
    kv_count = lax.axis_size(KV)
    group = lax.axis_index("req")
    halves = lax.axis_size("zhi")
    half = lax.axis_index("zhi")
    beam = lax.axis_index("y") * 2 + lax.axis_index("zlo")
    member = member_of(beam, half, halves)
    per_group = halves * rows
    group_rows = kv_count * rows
    quota = rows // req_count

    offsets = jnp.arange(rows, dtype=jnp.int32)
    slot_ids = group * per_group + half * rows + offsets
    placed = lax.dynamic_slice_in_dim(perm.reshape(req_count, per_group), half * rows, rows, 1)
    serving = lax.dynamic_index_in_dim(placed, group, 0, keepdims=False)
    target = jnp.sum(
        jnp.where(placed == slot_ids[None, :], jnp.arange(req_count, dtype=jnp.int32)[:, None], 0),
        axis=0,
    )
    anchor = serving // per_group
    send_slot = jnp.sum(
        jnp.where(target[None, :] == offsets[:, None], offsets[None, :], 0), axis=1
    )
    outgoing = jnp.take(x_steps, send_slot, axis=1).reshape(steps, req_count, quota, width)
    arrived = lax.all_to_all(outgoing, "req", split_axis=1, concat_axis=1, tiled=True).reshape(
        steps, rows, width
    )
    slot_req = perm.reshape(req_count, halves, rows) // (halves * rows)
    mine_req = slot_req[:, half, :][group]
    offset_of = jnp.sum(
        jnp.where(mine_req[None, :] == offsets[:, None], offsets[None, :], 0), axis=1
    )
    inputs = arrived

    normed = rms_round(inputs.reshape(steps * rows, width), norm_attn)
    query = jnp.dot(normed, w_query, preferred_element_type=jnp.float32).astype(jnp.bfloat16)
    fresh = jnp.dot(normed, w_keyval, preferred_element_type=jnp.float32).astype(jnp.bfloat16)
    packed = jnp.concatenate([query, fresh], axis=-1).reshape(steps, rows, qwidth + 2 * head_dim)
    mine = lax.all_to_all(
        jnp.broadcast_to(packed[None], (BEAMS,) + packed.shape), HALF, 0, 0, tiled=True
    )
    queries = mine[..., :qwidth].reshape(BEAMS, steps, rows, heads, head_dim)
    entries = mine[..., qwidth:]

    family = lax.dynamic_slice_in_dim(parents, group * group_rows, group_rows, 1).reshape(
        (steps, BEAMS // 2, halves, 2, rows)
    )
    family = lax.dynamic_index_in_dim(family, half, 2, keepdims=False).reshape(steps, BEAMS, rows)
    family = family[:, :, offset_of]
    own = jnp.broadcast_to(jnp.arange(BEAMS, dtype=jnp.int32)[:, None], (BEAMS, rows))
    cache_beam = own
    sources = []
    cache_beams = []
    listed = []
    for step_index in range(steps):
        cache_beam = follow(family[step_index], cache_beam)
        sources = [follow(family[step_index], source) for source in sources] + [own]
        cache_beams.append(cache_beam)
        picked = [pick_rows(source, entries[:, s]) for s, source in enumerate(sources)]
        picked += [jnp.zeros_like(picked[0])] * (steps - 1 - step_index)
        listed.append(jnp.stack(picked))
    held = jnp.stack(cache_beams, axis=1) == beam
    listed = jnp.stack(listed)

    length = lengths[serving[offset_of]]
    first_page = jnp.maximum(length - WINDOW + 1, 0) // PAGE
    device = group * kv_count + member
    pages = pool[table[offset_of] - device * pool.shape[0]].reshape(rows, span, 2 * head_dim)
    scale = head_dim ** (-0.5)
    step_ids = jnp.arange(steps, dtype=jnp.int32)
    base = first_page * PAGE
    lo = length[:, None] + step_ids[None, :] - WINDOW - base[:, None]
    hi = jnp.broadcast_to((length - base)[:, None], (rows, steps))
    bounds = jnp.stack([lo, hi], axis=-1).reshape(rows * steps * 2)
    by_row = jnp.transpose(queries, (2, 1, 0, 3, 4)).reshape(rows, steps, BEAMS * heads, head_dim)
    entries_by_row = jnp.transpose(listed, (3, 0, 1, 2, 4)).reshape(
        rows, steps, steps * BEAMS, 2 * head_dim
    )
    row_beam = jnp.arange(BEAMS * heads, dtype=jnp.int32) // heads
    column = jnp.arange(steps * BEAMS, dtype=jnp.int32)
    pick = (
        (column[None, None, :] % BEAMS == row_beam[None, :, None])
        & (column[None, None, :] // BEAMS <= step_ids[:, None, None])
    ).astype(jnp.float32)
    used = jnp.any(held, axis=0).T.astype(jnp.int32).reshape(rows * steps)
    attended = attend(bounds, used, by_row, pages, entries_by_row, pick)
    attended = jnp.transpose(attended.reshape(rows, steps, BEAMS, qwidth), (2, 1, 0, 3))
    attended = jnp.where(held[..., None], attended, jnp.zeros_like(attended))

    received = lax.all_to_all(attended, HALF, split_axis=0, concat_axis=0, tiled=True)
    attended_own = jnp.sum(received.astype(jnp.float32), axis=0).astype(jnp.bfloat16)

    current = inputs.reshape(steps * rows, width)
    residual = (
        current.astype(jnp.float32)
        + jnp.dot(attended_own.reshape(steps * rows, qwidth), w_out, preferred_element_type=jnp.float32)
    ).astype(jnp.bfloat16)
    by_req = jnp.swapaxes(residual.reshape(steps, rows, width), 0, 1).reshape(rows * steps, width)
    mlp_own = rms_round(by_req, norm_mlp)
    mlp_in = lax.all_to_all(
        jnp.broadcast_to(mlp_own[None], (kv_count,) + mlp_own.shape), KV, 0, 0, tiled=True
    ).reshape(kv_count * rows * steps, width)
    gate = jnp.dot(mlp_in, w_gate, preferred_element_type=jnp.float32)
    upward = jnp.dot(mlp_in, w_up, preferred_element_type=jnp.float32)
    hidden = (jax.nn.gelu(gate, approximate=True) * upward).astype(jnp.bfloat16)
    own_row = jnp.arange(kv_count * rows * steps, dtype=jnp.int32)
    select = (
        (own_row[:, None] // (rows * steps) == member)
        & (own_row[:, None] % (rows * steps) == jnp.arange(rows * steps, dtype=jnp.int32)[None, :])
    ).astype(jnp.bfloat16)
    terms = jnp.dot(
        jnp.concatenate([hidden, select], axis=1),
        jnp.concatenate([w_down, by_req], axis=0),
        preferred_element_type=jnp.float32,
    ).astype(jnp.bfloat16)

    leaving = terms
    arrived_sums = lax.all_to_all(leaving, KV + ("req",), 0, 0, tiled=True).reshape(
        kv_count, req_count, steps, width
    )
    per_group_sum = jnp.sum(arrived_sums.astype(jnp.float32), axis=0)
    served_by = slot_req[:, half, :] == group
    finished = jnp.sum(
        jnp.where(served_by[:, None, :, None], per_group_sum[:, :, None, :], 0.0), axis=0
    )
    return finished.astype(jnp.bfloat16)


def solution(mesh):
    req_count, kv_count = mesh.devices.shape
    halves = kv_count // BEAMS
    split = Mesh(
        mesh.devices.reshape(req_count, BEAMS // 2, halves, 2), ("req",) + KV
    )
    mesh = split
    ROWS = ("req",) + KV
    in_specs = (
        P(None, ROWS, None),
        P(),
        P(),
        P(),
        P(ROWS, None),
        P(ROWS, None, None),
        P(),
        P(),
        P(),
        P(),
        P(),
        P(None, KV),
        P(None, KV),
        P(KV, None),
    )
    out_specs = P(None, ROWS, None)
    return jax.shard_map(
        on_device, mesh=mesh, in_specs=in_specs, out_specs=out_specs, check_vma=False
    )
```

```python
import jax
import jax.numpy as jnp
from jax import lax
from jax.sharding import Mesh, PartitionSpec as P
from jax.experimental import pallas as pl
from jax.experimental.pallas import tpu as pltpu

WINDOW = 1024
PAGE = 128
BEAMS = 8


EPSILON = 1e-06
KV = ("y", "zhi", "zlo")
HALF = ("y", "zlo")
NEGATIVE = -1e30


def member_of(beam_index, half_index, halves):
    return beam_index % 2 + 2 * half_index + 2 * halves * (beam_index // 2)


def rms_round(values, gain):
    wide = values.astype(jnp.float32)
    mean_square = jnp.mean(wide * wide, axis=-1, keepdims=True)
    return (wide * lax.rsqrt(mean_square + EPSILON) * gain).astype(jnp.bfloat16)


def rank_within(labels, offsets):
    earlier = (labels[None, :] == labels[:, None]) & (offsets[None, :] < offsets[:, None])
    return jnp.sum(earlier.astype(jnp.int32), axis=1)


def follow(index, table):
    picks = index[:, None, :] == jnp.arange(BEAMS, dtype=jnp.int32)[None, :, None]
    return jnp.sum(jnp.where(picks, table[None, :, :], 0), axis=1)


def pick_rows(index, table):
    picks = index[:, None, :] == jnp.arange(BEAMS, dtype=jnp.int32)[None, :, None]
    return jnp.sum(jnp.where(picks[..., None], table[None, :, :, :], 0), axis=1).astype(table.dtype)


def attend_kernel(bounds_ref, used_ref, q_ref, kv_ref, new_ref, pick_ref, out_ref):
    r = pl.program_id(0)
    steps = q_ref.shape[1]
    head_dim = q_ref.shape[3]
    scale = head_dim ** (-0.5)
    keys = kv_ref[0, :, :head_dim]
    values = jnp.concatenate(
        [kv_ref[0, :, head_dim:], jnp.ones((kv_ref.shape[1], head_dim), kv_ref.dtype)], axis=1
    )
    pos = lax.broadcasted_iota(jnp.int32, (1, kv_ref.shape[1]), 1)
    contract = (((1,), (1,)), ((), ()))
    for t in range(steps):

        @pl.when(used_ref[r * steps + t] != 0)
        def _(t=t):
            lo = bounds_ref[(r * steps + t) * 2]
            hi = bounds_ref[(r * steps + t) * 2 + 1]
            query = q_ref[0, t]
            scores = lax.dot_general(query, keys, contract, preferred_element_type=jnp.float32) * scale
            allowed = (pos > lo) & (pos < hi)
            scores = jnp.where(allowed, scores, NEGATIVE)
            high_c = jnp.max(scores, axis=1, keepdims=True)
            weights = jnp.exp(scores - high_c).astype(jnp.bfloat16)
            both = jnp.dot(weights, values, preferred_element_type=jnp.float32)
            sum_c = both[:, :head_dim]
            total_c = both[:, head_dim : head_dim + 1]
            entries = new_ref[0, t]
            fresh = lax.dot_general(
                query, entries[:, :head_dim], contract, preferred_element_type=jnp.float32
            ) * scale
            fresh = jnp.where(pick_ref[t] > 0, fresh, NEGATIVE)
            high_n = jnp.max(fresh, axis=1, keepdims=True)
            fresh_w = jnp.exp(fresh - high_n).astype(jnp.bfloat16)
            total_n = jnp.sum(fresh_w.astype(jnp.float32), axis=1, keepdims=True)
            sum_n = jnp.dot(fresh_w, entries[:, head_dim:], preferred_element_type=jnp.float32)
            highest = jnp.maximum(high_c, high_n)
            scale_c = jnp.exp(high_c - highest)
            scale_n = jnp.exp(high_n - highest)
            totals = total_c * scale_c + total_n * scale_n
            weighted = sum_c * scale_c + sum_n * scale_n
            out_ref[0, t] = (weighted / totals).astype(out_ref.dtype)

        @pl.when(used_ref[r * steps + t] == 0)
        def _(t=t):
            out_ref[0, t] = jnp.zeros(out_ref.shape[2:], out_ref.dtype)


def attend(bounds, used, queries, pages, entries, pick):
    rows, steps, count, head_dim = queries.shape
    span = pages.shape[1]
    flops = 4 * rows * steps * count * (span + entries.shape[2]) * head_dim
    return pl.pallas_call(
        attend_kernel,
        grid_spec=pltpu.PrefetchScalarGridSpec(
            num_scalar_prefetch=2,
            grid=(rows,),
            in_specs=[
                pl.BlockSpec((1, steps, count, head_dim), lambda r, b, u: (r, 0, 0, 0)),
                pl.BlockSpec((1, span, pages.shape[2]), lambda r, b, u: (r, 0, 0)),
                pl.BlockSpec((1,) + entries.shape[1:], lambda r, b, u: (r, 0, 0, 0)),
                pl.BlockSpec(pick.shape, lambda r, b, u: (0, 0, 0)),
            ],
            out_specs=pl.BlockSpec((1, steps, count, head_dim), lambda r, b, u: (r, 0, 0, 0)),
        ),
        out_shape=jax.ShapeDtypeStruct(queries.shape, jnp.bfloat16),
        cost_estimate=pl.CostEstimate(
            flops=flops,
            transcendentals=rows * steps * count * span,
            bytes_accessed=pages.size * 2 + queries.size * 4 + entries.size * 2,
        ),
    )(bounds, used, queries, pages, entries, pick)


def on_device(
    x_steps,
    lengths,
    perm,
    parents,
    table,
    pool,
    norm_attn,
    w_query,
    w_keyval,
    w_out,
    norm_mlp,
    w_gate,
    w_up,
    w_down,
):
    steps, rows, width = x_steps.shape
    head_dim = pool.shape[2] // 2
    heads = w_query.shape[1] // head_dim
    qwidth = heads * head_dim
    span = table.shape[1] * pool.shape[1]
    req_count = lax.axis_size("req")
    kv_count = lax.axis_size(KV)
    group = lax.axis_index("req")
    halves = lax.axis_size("zhi")
    half = lax.axis_index("zhi")
    beam = lax.axis_index("y") * 2 + lax.axis_index("zlo")
    member = member_of(beam, half, halves)
    per_group = halves * rows
    group_rows = kv_count * rows
    quota = rows // req_count

    offsets = jnp.arange(rows, dtype=jnp.int32)
    slot_ids = group * per_group + half * rows + offsets
    placed = lax.dynamic_slice_in_dim(perm.reshape(req_count, per_group), half * rows, rows, 1)
    serving = lax.dynamic_index_in_dim(placed, group, 0, keepdims=False)
    target = jnp.sum(
        jnp.where(placed == slot_ids[None, :], jnp.arange(req_count, dtype=jnp.int32)[:, None], 0),
        axis=0,
    )
    anchor = serving // per_group
    send_slot = jnp.sum(
        jnp.where(target[None, :] == offsets[:, None], offsets[None, :], 0), axis=1
    )
    outgoing = jnp.take(x_steps, send_slot, axis=1).reshape(steps, req_count, quota, width)
    arrived = lax.all_to_all(outgoing, "req", split_axis=1, concat_axis=1, tiled=True).reshape(
        steps, rows, width
    )
    slot_req = perm.reshape(req_count, halves, rows) // (halves * rows)
    mine_req = slot_req[:, half, :][group]
    offset_of = jnp.sum(
        jnp.where(mine_req[None, :] == offsets[:, None], offsets[None, :], 0), axis=1
    )
    inputs = arrived

    normed = rms_round(inputs.reshape(steps * rows, width), norm_attn)
    query = jnp.dot(normed, w_query, preferred_element_type=jnp.float32).astype(jnp.bfloat16)
    fresh = jnp.dot(normed, w_keyval, preferred_element_type=jnp.float32).astype(jnp.bfloat16)
    packed = jnp.concatenate([query, fresh], axis=-1).reshape(steps, rows, qwidth + 2 * head_dim)
    mine = lax.all_to_all(
        jnp.broadcast_to(packed[None], (BEAMS,) + packed.shape), HALF, 0, 0, tiled=True
    )
    queries = mine[..., :qwidth].reshape(BEAMS, steps, rows, heads, head_dim)
    entries = mine[..., qwidth:]

    family = lax.dynamic_slice_in_dim(parents, group * group_rows, group_rows, 1).reshape(
        (steps, BEAMS // 2, halves, 2, rows)
    )
    family = lax.dynamic_index_in_dim(family, half, 2, keepdims=False).reshape(steps, BEAMS, rows)
    family = family[:, :, offset_of]
    own = jnp.broadcast_to(jnp.arange(BEAMS, dtype=jnp.int32)[:, None], (BEAMS, rows))
    cache_beam = own
    sources = []
    cache_beams = []
    listed = []
    for step_index in range(steps):
        cache_beam = follow(family[step_index], cache_beam)
        sources = [follow(family[step_index], source) for source in sources] + [own]
        cache_beams.append(cache_beam)
        picked = [pick_rows(source, entries[:, s]) for s, source in enumerate(sources)]
        picked += [jnp.zeros_like(picked[0])] * (steps - 1 - step_index)
        listed.append(jnp.stack(picked))
    held = jnp.stack(cache_beams, axis=1) == beam
    listed = jnp.stack(listed)

    length = lengths[serving[offset_of]]
    first_page = jnp.maximum(length - WINDOW + 1, 0) // PAGE
    device = group * kv_count + member
    pages = pool[table[offset_of] - device * pool.shape[0]].reshape(rows, span, 2 * head_dim)
    scale = head_dim ** (-0.5)
    step_ids = jnp.arange(steps, dtype=jnp.int32)
    base = first_page * PAGE
    lo = length[:, None] + step_ids[None, :] - WINDOW - base[:, None]
    hi = jnp.broadcast_to((length - base)[:, None], (rows, steps))
    bounds = jnp.stack([lo, hi], axis=-1).reshape(rows * steps * 2)
    by_row = jnp.transpose(queries, (2, 1, 0, 3, 4)).reshape(rows, steps, BEAMS * heads, head_dim)
    entries_by_row = jnp.transpose(listed, (3, 0, 1, 2, 4)).reshape(
        rows, steps, steps * BEAMS, 2 * head_dim
    )
    row_beam = jnp.arange(BEAMS * heads, dtype=jnp.int32) // heads
    column = jnp.arange(steps * BEAMS, dtype=jnp.int32)
    pick = (
        (column[None, None, :] % BEAMS == row_beam[None, :, None])
        & (column[None, None, :] // BEAMS <= step_ids[:, None, None])
    ).astype(jnp.float32)
    used = jnp.any(held, axis=0).T.astype(jnp.int32).reshape(rows * steps)
    attended = attend(bounds, used, by_row, pages, entries_by_row, pick)
    attended = jnp.transpose(attended.reshape(rows, steps, BEAMS, qwidth), (2, 1, 0, 3))
    attended = jnp.where(held[..., None], attended, jnp.zeros_like(attended))

    received = lax.all_to_all(attended, HALF, split_axis=0, concat_axis=0, tiled=True)
    attended_own = jnp.sum(received.astype(jnp.float32), axis=0).astype(jnp.bfloat16)

    current = inputs.reshape(steps * rows, width)
    residual = (
        current.astype(jnp.float32)
        + jnp.dot(attended_own.reshape(steps * rows, qwidth), w_out, preferred_element_type=jnp.float32)
    ).astype(jnp.bfloat16)
    by_req = jnp.swapaxes(residual.reshape(steps, rows, width), 0, 1).reshape(rows * steps, width)
    mlp_own = rms_round(by_req, norm_mlp)
    mlp_in = lax.all_to_all(
        jnp.broadcast_to(mlp_own[None], (kv_count,) + mlp_own.shape), KV, 0, 0, tiled=True
    ).reshape(kv_count * rows * steps, width)
    gate = jnp.dot(mlp_in, w_gate, preferred_element_type=jnp.float32)
    upward = jnp.dot(mlp_in, w_up, preferred_element_type=jnp.float32)
    hidden = (jax.nn.gelu(gate, approximate=True) * upward).astype(jnp.bfloat16)
    own_row = jnp.arange(kv_count * rows * steps, dtype=jnp.int32)
    select = (
        (own_row[:, None] // (rows * steps) == member)
        & (own_row[:, None] % (rows * steps) == jnp.arange(rows * steps, dtype=jnp.int32)[None, :])
    ).astype(jnp.bfloat16)
    terms = jnp.dot(
        jnp.concatenate([hidden, select], axis=1),
        jnp.concatenate([w_down, by_req], axis=0),
        preferred_element_type=jnp.float32,
    ).astype(jnp.bfloat16)

    leaving = terms
    arrived_sums = lax.all_to_all(leaving, KV + ("req",), 0, 0, tiled=True).reshape(
        kv_count, req_count, steps, width
    )
    per_group_sum = jnp.sum(arrived_sums.astype(jnp.float32), axis=0)
    served_by = slot_req[:, half, :] == group
    finished = jnp.sum(
        jnp.where(served_by[:, None, :, None], per_group_sum[:, :, None, :], 0.0), axis=0
    )
    return finished.astype(jnp.bfloat16)


def solution(mesh):
    req_count, kv_count = mesh.devices.shape
    halves = kv_count // BEAMS
    split = Mesh(
        mesh.devices.reshape(req_count, BEAMS // 2, halves, 2), ("req",) + KV
    )
    mesh = split
    ROWS = ("req",) + KV
    in_specs = (
        P(None, ROWS, None),
        P(),
        P(),
        P(),
        P(ROWS, None),
        P(ROWS, None, None),
        P(),
        P(),
        P(),
        P(),
        P(),
        P(None, KV),
        P(None, KV),
        P(KV, None),
    )
    out_specs = P(None, ROWS, None)
    return jax.shard_map(
        on_device, mesh=mesh, in_specs=in_specs, out_specs=out_specs, check_vma=False
    )
```

```python
import jax
import jax.numpy as jnp
from jax import lax
from jax.sharding import Mesh, PartitionSpec as P
from jax.experimental import pallas as pl
from jax.experimental.pallas import tpu as pltpu

WINDOW = 1024
PAGE = 128
BEAMS = 8


EPSILON = 1e-06
KV = ("y", "zhi", "zlo")
HALF = ("y", "zlo")
NEGATIVE = -1e30


def member_of(beam_index, half_index, halves):
    return beam_index % 2 + 2 * half_index + 2 * halves * (beam_index // 2)


def rms_round(values, gain):
    wide = values.astype(jnp.float32)
    mean_square = jnp.mean(wide * wide, axis=-1, keepdims=True)
    return (wide * lax.rsqrt(mean_square + EPSILON) * gain).astype(jnp.bfloat16)


def rank_within(labels, offsets):
    earlier = (labels[None, :] == labels[:, None]) & (offsets[None, :] < offsets[:, None])
    return jnp.sum(earlier.astype(jnp.int32), axis=1)


def follow(index, table):
    picks = index[:, None, :] == jnp.arange(BEAMS, dtype=jnp.int32)[None, :, None]
    return jnp.sum(jnp.where(picks, table[None, :, :], 0), axis=1)


def pick_rows(index, table):
    picks = index[:, None, :] == jnp.arange(BEAMS, dtype=jnp.int32)[None, :, None]
    return jnp.sum(jnp.where(picks[..., None], table[None, :, :, :], 0), axis=1).astype(table.dtype)


def attend_kernel(bounds_ref, used_ref, q_ref, kv_ref, new_ref, pick_ref, out_ref):
    r = pl.program_id(0)
    steps = q_ref.shape[1]
    head_dim = q_ref.shape[3]
    scale = head_dim ** (-0.5)
    keys = kv_ref[0, :, :head_dim]
    values = kv_ref[0, :, head_dim:]
    pos = lax.broadcasted_iota(jnp.int32, (1, kv_ref.shape[1]), 1)
    contract = (((1,), (1,)), ((), ()))
    for t in range(steps):

        @pl.when(used_ref[r * steps + t] != 0)
        def _(t=t):
            lo = bounds_ref[(r * steps + t) * 2]
            hi = bounds_ref[(r * steps + t) * 2 + 1]
            query = q_ref[0, t]
            scores = lax.dot_general(query, keys, contract, preferred_element_type=jnp.float32) * scale
            allowed = (pos > lo) & (pos < hi)
            scores = jnp.where(allowed, scores, NEGATIVE)
            high_c = jnp.max(scores, axis=1, keepdims=True)
            weights = jnp.exp(scores - high_c).astype(jnp.bfloat16)
            total_c = jnp.sum(weights.astype(jnp.float32), axis=1, keepdims=True)
            sum_c = jnp.dot(weights, values, preferred_element_type=jnp.float32)
            entries = new_ref[0, t]
            fresh = lax.dot_general(
                query, entries[:, :head_dim], contract, preferred_element_type=jnp.float32
            ) * scale
            fresh = jnp.where(pick_ref[t] > 0, fresh, NEGATIVE)
            high_n = jnp.max(fresh, axis=1, keepdims=True)
            fresh_w = jnp.exp(fresh - high_n).astype(jnp.bfloat16)
            total_n = jnp.sum(fresh_w.astype(jnp.float32), axis=1, keepdims=True)
            sum_n = jnp.dot(fresh_w, entries[:, head_dim:], preferred_element_type=jnp.float32)
            highest = jnp.maximum(high_c, high_n)
            scale_c = jnp.exp(high_c - highest)
            scale_n = jnp.exp(high_n - highest)
            totals = total_c * scale_c + total_n * scale_n
            weighted = sum_c * scale_c + sum_n * scale_n
            attended = weighted / totals
            for h in range(out_ref.shape[3] // head_dim):
                out_ref[0, t, :, h * head_dim : (h + 1) * head_dim] = attended[
                    h * out_ref.shape[2] : (h + 1) * out_ref.shape[2]
                ].astype(out_ref.dtype)

        @pl.when(used_ref[r * steps + t] == 0)
        def _(t=t):
            out_ref[0, t] = jnp.zeros(out_ref.shape[2:], out_ref.dtype)


def attend(bounds, used, queries, pages, entries, pick):
    rows, steps, count, head_dim = queries.shape
    out_rows = BEAMS
    out_width = count // BEAMS * head_dim
    span = pages.shape[1]
    flops = 4 * rows * steps * count * (span + entries.shape[2]) * head_dim
    return pl.pallas_call(
        attend_kernel,
        grid_spec=pltpu.PrefetchScalarGridSpec(
            num_scalar_prefetch=2,
            grid=(rows,),
            in_specs=[
                pl.BlockSpec((1, steps, count, head_dim), lambda r, b, u: (r, 0, 0, 0)),
                pl.BlockSpec((1, span, pages.shape[2]), lambda r, b, u: (r, 0, 0)),
                pl.BlockSpec((1,) + entries.shape[1:], lambda r, b, u: (r, 0, 0, 0)),
                pl.BlockSpec(pick.shape, lambda r, b, u: (0, 0, 0)),
            ],
            out_specs=pl.BlockSpec((1, steps, out_rows, out_width), lambda r, b, u: (r, 0, 0, 0)),
        ),
        out_shape=jax.ShapeDtypeStruct((rows, steps, out_rows, out_width), jnp.bfloat16),
        cost_estimate=pl.CostEstimate(
            flops=flops,
            transcendentals=rows * steps * count * span,
            bytes_accessed=pages.size * 2 + queries.size * 4 + entries.size * 2,
        ),
    )(bounds, used, queries, pages, entries, pick)


def on_device(
    x_steps,
    lengths,
    perm,
    parents,
    table,
    pool,
    norm_attn,
    w_query,
    w_keyval,
    w_out,
    norm_mlp,
    w_gate,
    w_up,
    w_down,
):
    steps, rows, width = x_steps.shape
    head_dim = pool.shape[2] // 2
    heads = w_query.shape[1] // head_dim
    qwidth = heads * head_dim
    span = table.shape[1] * pool.shape[1]
    req_count = lax.axis_size("req")
    kv_count = lax.axis_size(KV)
    group = lax.axis_index("req")
    halves = lax.axis_size("zhi")
    half = lax.axis_index("zhi")
    beam = lax.axis_index("y") * 2 + lax.axis_index("zlo")
    member = member_of(beam, half, halves)
    per_group = halves * rows
    group_rows = kv_count * rows
    quota = rows // req_count

    offsets = jnp.arange(rows, dtype=jnp.int32)
    slot_ids = group * per_group + half * rows + offsets
    placed = lax.dynamic_slice_in_dim(perm.reshape(req_count, per_group), half * rows, rows, 1)
    serving = lax.dynamic_index_in_dim(placed, group, 0, keepdims=False)
    target = jnp.sum(
        jnp.where(placed == slot_ids[None, :], jnp.arange(req_count, dtype=jnp.int32)[:, None], 0),
        axis=0,
    )
    anchor = serving // per_group
    send_slot = jnp.sum(
        jnp.where(target[None, :] == offsets[:, None], offsets[None, :], 0), axis=1
    )
    outgoing = jnp.take(x_steps, send_slot, axis=1).reshape(steps, req_count, quota, width)
    arrived = lax.all_to_all(outgoing, "req", split_axis=1, concat_axis=1, tiled=True).reshape(
        steps, rows, width
    )
    slot_req = perm.reshape(req_count, halves, rows) // (halves * rows)
    mine_req = slot_req[:, half, :][group]
    offset_of = jnp.sum(
        jnp.where(mine_req[None, :] == offsets[:, None], offsets[None, :], 0), axis=1
    )
    inputs = arrived

    normed = rms_round(inputs.reshape(steps * rows, width), norm_attn)
    query = jnp.dot(normed, w_query, preferred_element_type=jnp.float32).astype(jnp.bfloat16)
    fresh = jnp.dot(normed, w_keyval, preferred_element_type=jnp.float32).astype(jnp.bfloat16)
    packed = jnp.concatenate([query, fresh], axis=-1).reshape(steps, rows, qwidth + 2 * head_dim)
    mine = lax.all_to_all(
        jnp.broadcast_to(packed[None], (BEAMS,) + packed.shape), HALF, 0, 0, tiled=True
    )
    queries = mine[..., :qwidth].reshape(BEAMS, steps, rows, heads, head_dim)
    entries = mine[..., qwidth:]

    family = lax.dynamic_slice_in_dim(parents, group * group_rows, group_rows, 1).reshape(
        (steps, BEAMS // 2, halves, 2, rows)
    )
    family = lax.dynamic_index_in_dim(family, half, 2, keepdims=False).reshape(steps, BEAMS, rows)
    family = family[:, :, offset_of]
    own = jnp.broadcast_to(jnp.arange(BEAMS, dtype=jnp.int32)[:, None], (BEAMS, rows))
    cache_beam = own
    sources = []
    cache_beams = []
    listed = []
    for step_index in range(steps):
        cache_beam = follow(family[step_index], cache_beam)
        sources = [follow(family[step_index], source) for source in sources] + [own]
        cache_beams.append(cache_beam)
        picked = [pick_rows(source, entries[:, s]) for s, source in enumerate(sources)]
        picked += [jnp.zeros_like(picked[0])] * (steps - 1 - step_index)
        listed.append(jnp.stack(picked))
    held = jnp.stack(cache_beams, axis=1) == beam
    listed = jnp.stack(listed)

    length = lengths[serving[offset_of]]
    first_page = jnp.maximum(length - WINDOW + 1, 0) // PAGE
    device = group * kv_count + member
    pages = pool[table[offset_of] - device * pool.shape[0]].reshape(rows, span, 2 * head_dim)
    scale = head_dim ** (-0.5)
    step_ids = jnp.arange(steps, dtype=jnp.int32)
    base = first_page * PAGE
    lo = length[:, None] + step_ids[None, :] - WINDOW - base[:, None]
    hi = jnp.broadcast_to((length - base)[:, None], (rows, steps))
    bounds = jnp.stack([lo, hi], axis=-1).reshape(rows * steps * 2)
    by_row = jnp.transpose(queries, (2, 1, 3, 0, 4)).reshape(rows, steps, heads * BEAMS, head_dim)
    entries_by_row = jnp.transpose(listed, (3, 0, 1, 2, 4)).reshape(
        rows, steps, steps * BEAMS, 2 * head_dim
    )
    row_beam = jnp.arange(BEAMS * heads, dtype=jnp.int32) % BEAMS
    column = jnp.arange(steps * BEAMS, dtype=jnp.int32)
    pick = (
        (column[None, None, :] % BEAMS == row_beam[None, :, None])
        & (column[None, None, :] // BEAMS <= step_ids[:, None, None])
    ).astype(jnp.float32)
    used = jnp.any(held, axis=0).T.astype(jnp.int32).reshape(rows * steps)
    attended = attend(bounds, used, by_row, pages, entries_by_row, pick)
    attended = jnp.transpose(attended, (2, 1, 0, 3))
    attended = jnp.where(held[..., None], attended, jnp.zeros_like(attended))

    received = lax.all_to_all(attended, HALF, split_axis=0, concat_axis=0, tiled=True)
    attended_own = jnp.sum(received.astype(jnp.float32), axis=0).astype(jnp.bfloat16)

    current = inputs.reshape(steps * rows, width)
    residual = (
        current.astype(jnp.float32)
        + jnp.dot(attended_own.reshape(steps * rows, qwidth), w_out, preferred_element_type=jnp.float32)
    ).astype(jnp.bfloat16)
    by_req = jnp.swapaxes(residual.reshape(steps, rows, width), 0, 1).reshape(rows * steps, width)
    mlp_own = rms_round(by_req, norm_mlp)
    mlp_in = lax.all_to_all(
        jnp.broadcast_to(mlp_own[None], (kv_count,) + mlp_own.shape), KV, 0, 0, tiled=True
    ).reshape(kv_count * rows * steps, width)
    gate = jnp.dot(mlp_in, w_gate, preferred_element_type=jnp.float32)
    upward = jnp.dot(mlp_in, w_up, preferred_element_type=jnp.float32)
    hidden = (jax.nn.gelu(gate, approximate=True) * upward).astype(jnp.bfloat16)
    own_row = jnp.arange(kv_count * rows * steps, dtype=jnp.int32)
    select = (
        (own_row[:, None] // (rows * steps) == member)
        & (own_row[:, None] % (rows * steps) == jnp.arange(rows * steps, dtype=jnp.int32)[None, :])
    ).astype(jnp.bfloat16)
    terms = jnp.dot(
        jnp.concatenate([hidden, select], axis=1),
        jnp.concatenate([w_down, by_req], axis=0),
        preferred_element_type=jnp.float32,
    ).astype(jnp.bfloat16)

    leaving = terms
    arrived_sums = lax.all_to_all(leaving, KV + ("req",), 0, 0, tiled=True).reshape(
        kv_count, req_count, steps, width
    )
    per_group_sum = jnp.sum(arrived_sums.astype(jnp.float32), axis=0)
    served_by = slot_req[:, half, :] == group
    finished = jnp.sum(
        jnp.where(served_by[:, None, :, None], per_group_sum[:, :, None, :], 0.0), axis=0
    )
    return finished.astype(jnp.bfloat16)


def solution(mesh):
    req_count, kv_count = mesh.devices.shape
    halves = kv_count // BEAMS
    split = Mesh(
        mesh.devices.reshape(req_count, BEAMS // 2, halves, 2), ("req",) + KV
    )
    mesh = split
    ROWS = ("req",) + KV
    in_specs = (
        P(None, ROWS, None),
        P(),
        P(),
        P(),
        P(ROWS, None),
        P(ROWS, None, None),
        P(),
        P(),
        P(),
        P(),
        P(),
        P(None, KV),
        P(None, KV),
        P(KV, None),
    )
    out_specs = P(None, ROWS, None)
    return jax.shard_map(
        on_device, mesh=mesh, in_specs=in_specs, out_specs=out_specs, check_vma=False
    )
```

```python
import jax
import jax.numpy as jnp
from jax import lax
from jax.sharding import Mesh, PartitionSpec as P
from jax.experimental import pallas as pl
from jax.experimental.pallas import tpu as pltpu

WINDOW = 1024
PAGE = 128
BEAMS = 8


EPSILON = 1e-06
KV = ("y", "zhi", "zlo")
HALF = ("y", "zlo")
NEGATIVE = -1e30


def member_of(beam_index, half_index, halves):
    return beam_index % 2 + 2 * half_index + 2 * halves * (beam_index // 2)


def rms_round(values, gain):
    wide = values.astype(jnp.float32)
    mean_square = jnp.mean(wide * wide, axis=-1, keepdims=True)
    return (wide * lax.rsqrt(mean_square + EPSILON) * gain).astype(jnp.bfloat16)


def rank_within(labels, offsets):
    earlier = (labels[None, :] == labels[:, None]) & (offsets[None, :] < offsets[:, None])
    return jnp.sum(earlier.astype(jnp.int32), axis=1)


def follow(index, table):
    picks = index[:, None, :] == jnp.arange(BEAMS, dtype=jnp.int32)[None, :, None]
    return jnp.sum(jnp.where(picks, table[None, :, :], 0), axis=1)


def pick_rows(index, table):
    picks = index[:, None, :] == jnp.arange(BEAMS, dtype=jnp.int32)[None, :, None]
    return jnp.sum(jnp.where(picks[..., None], table[None, :, :, :], 0), axis=1).astype(table.dtype)


def attend_kernel(bounds_ref, used_ref, q_ref, kv_ref, new_ref, pick_ref, held_ref, out_ref):
    r = pl.program_id(0)
    steps = q_ref.shape[1]
    head_dim = q_ref.shape[3]
    scale = head_dim ** (-0.5)
    keys = kv_ref[0, :, :head_dim]
    values = kv_ref[0, :, head_dim:]
    pos = lax.broadcasted_iota(jnp.int32, (1, kv_ref.shape[1]), 1)
    contract = (((1,), (1,)), ((), ()))
    for t in range(steps):

        @pl.when(used_ref[r * steps + t] != 0)
        def _(t=t):
            lo = bounds_ref[(r * steps + t) * 2]
            hi = bounds_ref[(r * steps + t) * 2 + 1]
            query = q_ref[0, t]
            scores = lax.dot_general(query, keys, contract, preferred_element_type=jnp.float32) * scale
            allowed = (pos > lo) & (pos < hi)
            scores = jnp.where(allowed, scores, NEGATIVE)
            high_c = jnp.max(scores, axis=1, keepdims=True)
            weights = jnp.exp(scores - high_c).astype(jnp.bfloat16)
            total_c = jnp.sum(weights.astype(jnp.float32), axis=1, keepdims=True)
            sum_c = jnp.dot(weights, values, preferred_element_type=jnp.float32)
            entries = new_ref[0, t]
            fresh = lax.dot_general(
                query, entries[:, :head_dim], contract, preferred_element_type=jnp.float32
            ) * scale
            fresh = jnp.where(pick_ref[t] > 0, fresh, NEGATIVE)
            high_n = jnp.max(fresh, axis=1, keepdims=True)
            fresh_w = jnp.exp(fresh - high_n).astype(jnp.bfloat16)
            total_n = jnp.sum(fresh_w.astype(jnp.float32), axis=1, keepdims=True)
            sum_n = jnp.dot(fresh_w, entries[:, head_dim:], preferred_element_type=jnp.float32)
            highest = jnp.maximum(high_c, high_n)
            scale_c = jnp.exp(high_c - highest)
            scale_n = jnp.exp(high_n - highest)
            totals = total_c * scale_c + total_n * scale_n
            weighted = sum_c * scale_c + sum_n * scale_n
            attended = weighted / totals
            kept = held_ref[0, t] > 0
            for h in range(out_ref.shape[3] // head_dim):
                part = attended[h * out_ref.shape[2] : (h + 1) * out_ref.shape[2]]
                out_ref[0, t, :, h * head_dim : (h + 1) * head_dim] = jnp.where(
                    kept, part, 0.0
                ).astype(out_ref.dtype)

        @pl.when(used_ref[r * steps + t] == 0)
        def _(t=t):
            out_ref[0, t] = jnp.zeros(out_ref.shape[2:], out_ref.dtype)


def attend(bounds, used, queries, pages, entries, pick, held):
    rows, steps, count, head_dim = queries.shape
    out_rows = BEAMS
    out_width = count // BEAMS * head_dim
    span = pages.shape[1]
    flops = 4 * rows * steps * count * (span + entries.shape[2]) * head_dim
    return pl.pallas_call(
        attend_kernel,
        grid_spec=pltpu.PrefetchScalarGridSpec(
            num_scalar_prefetch=2,
            grid=(rows,),
            in_specs=[
                pl.BlockSpec((1, steps, count, head_dim), lambda r, b, u: (r, 0, 0, 0)),
                pl.BlockSpec((1, span, pages.shape[2]), lambda r, b, u: (r, 0, 0)),
                pl.BlockSpec((1,) + entries.shape[1:], lambda r, b, u: (r, 0, 0, 0)),
                pl.BlockSpec(pick.shape, lambda r, b, u: (0, 0, 0)),
                pl.BlockSpec((1,) + held.shape[1:], lambda r, b, u: (r, 0, 0, 0)),
            ],
            out_specs=pl.BlockSpec((1, steps, out_rows, out_width), lambda r, b, u: (r, 0, 0, 0)),
        ),
        out_shape=jax.ShapeDtypeStruct((rows, steps, out_rows, out_width), jnp.bfloat16),
        cost_estimate=pl.CostEstimate(
            flops=flops,
            transcendentals=rows * steps * count * span,
            bytes_accessed=pages.size * 2 + queries.size * 4 + entries.size * 2,
        ),
    )(bounds, used, queries, pages, entries, pick, held)


def on_device(
    x_steps,
    lengths,
    perm,
    parents,
    table,
    pool,
    norm_attn,
    w_query,
    w_keyval,
    w_out,
    norm_mlp,
    w_gate,
    w_up,
    w_down,
):
    steps, rows, width = x_steps.shape
    head_dim = pool.shape[2] // 2
    heads = w_query.shape[1] // head_dim
    qwidth = heads * head_dim
    span = table.shape[1] * pool.shape[1]
    req_count = lax.axis_size("req")
    kv_count = lax.axis_size(KV)
    group = lax.axis_index("req")
    halves = lax.axis_size("zhi")
    half = lax.axis_index("zhi")
    beam = lax.axis_index("y") * 2 + lax.axis_index("zlo")
    member = member_of(beam, half, halves)
    per_group = halves * rows
    group_rows = kv_count * rows
    quota = rows // req_count

    offsets = jnp.arange(rows, dtype=jnp.int32)
    slot_ids = group * per_group + half * rows + offsets
    placed = lax.dynamic_slice_in_dim(perm.reshape(req_count, per_group), half * rows, rows, 1)
    serving = lax.dynamic_index_in_dim(placed, group, 0, keepdims=False)
    target = jnp.sum(
        jnp.where(placed == slot_ids[None, :], jnp.arange(req_count, dtype=jnp.int32)[:, None], 0),
        axis=0,
    )
    anchor = serving // per_group
    send_slot = jnp.sum(
        jnp.where(target[None, :] == offsets[:, None], offsets[None, :], 0), axis=1
    )
    outgoing = jnp.take(x_steps, send_slot, axis=1).reshape(steps, req_count, quota, width)
    arrived = lax.all_to_all(outgoing, "req", split_axis=1, concat_axis=1, tiled=True).reshape(
        steps, rows, width
    )
    slot_req = perm.reshape(req_count, halves, rows) // (halves * rows)
    mine_req = slot_req[:, half, :][group]
    offset_of = jnp.sum(
        jnp.where(mine_req[None, :] == offsets[:, None], offsets[None, :], 0), axis=1
    )
    inputs = arrived

    normed = rms_round(inputs.reshape(steps * rows, width), norm_attn)
    query = jnp.dot(normed, w_query, preferred_element_type=jnp.float32).astype(jnp.bfloat16)
    fresh = jnp.dot(normed, w_keyval, preferred_element_type=jnp.float32).astype(jnp.bfloat16)
    packed = jnp.concatenate([query, fresh], axis=-1).reshape(steps, rows, qwidth + 2 * head_dim)
    mine = lax.all_to_all(
        jnp.broadcast_to(packed[None], (BEAMS,) + packed.shape), HALF, 0, 0, tiled=True
    )
    queries = mine[..., :qwidth].reshape(BEAMS, steps, rows, heads, head_dim)
    entries = mine[..., qwidth:]

    family = lax.dynamic_slice_in_dim(parents, group * group_rows, group_rows, 1).reshape(
        (steps, BEAMS // 2, halves, 2, rows)
    )
    family = lax.dynamic_index_in_dim(family, half, 2, keepdims=False).reshape(steps, BEAMS, rows)
    family = family[:, :, offset_of]
    own = jnp.broadcast_to(jnp.arange(BEAMS, dtype=jnp.int32)[:, None], (BEAMS, rows))
    cache_beam = own
    sources = []
    cache_beams = []
    listed = []
    for step_index in range(steps):
        cache_beam = follow(family[step_index], cache_beam)
        sources = [follow(family[step_index], source) for source in sources] + [own]
        cache_beams.append(cache_beam)
        picked = [pick_rows(source, entries[:, s]) for s, source in enumerate(sources)]
        picked += [jnp.zeros_like(picked[0])] * (steps - 1 - step_index)
        listed.append(jnp.stack(picked))
    held = jnp.stack(cache_beams, axis=1) == beam
    listed = jnp.stack(listed)

    length = lengths[serving[offset_of]]
    first_page = jnp.maximum(length - WINDOW + 1, 0) // PAGE
    device = group * kv_count + member
    pages = pool[table[offset_of] - device * pool.shape[0]].reshape(rows, span, 2 * head_dim)
    scale = head_dim ** (-0.5)
    step_ids = jnp.arange(steps, dtype=jnp.int32)
    base = first_page * PAGE
    lo = length[:, None] + step_ids[None, :] - WINDOW - base[:, None]
    hi = jnp.broadcast_to((length - base)[:, None], (rows, steps))
    bounds = jnp.stack([lo, hi], axis=-1).reshape(rows * steps * 2)
    by_row = jnp.transpose(queries, (2, 1, 3, 0, 4)).reshape(rows, steps, heads * BEAMS, head_dim)
    entries_by_row = jnp.transpose(listed, (3, 0, 1, 2, 4)).reshape(
        rows, steps, steps * BEAMS, 2 * head_dim
    )
    row_beam = jnp.arange(BEAMS * heads, dtype=jnp.int32) % BEAMS
    column = jnp.arange(steps * BEAMS, dtype=jnp.int32)
    pick = (
        (column[None, None, :] % BEAMS == row_beam[None, :, None])
        & (column[None, None, :] // BEAMS <= step_ids[:, None, None])
    ).astype(jnp.float32)
    used = jnp.any(held, axis=0).T.astype(jnp.int32).reshape(rows * steps)
    held_by_row = jnp.transpose(held, (2, 1, 0)).astype(jnp.float32)[..., None]
    attended = attend(bounds, used, by_row, pages, entries_by_row, pick, held_by_row)

    received = lax.all_to_all(attended, HALF, split_axis=2, concat_axis=2, tiled=True)
    attended_own = jnp.swapaxes(
        jnp.sum(received.astype(jnp.float32), axis=2).astype(jnp.bfloat16), 0, 1
    )

    current = inputs.reshape(steps * rows, width)
    residual = (
        current.astype(jnp.float32)
        + jnp.dot(attended_own.reshape(steps * rows, qwidth), w_out, preferred_element_type=jnp.float32)
    ).astype(jnp.bfloat16)
    by_req = jnp.swapaxes(residual.reshape(steps, rows, width), 0, 1).reshape(rows * steps, width)
    mlp_own = rms_round(by_req, norm_mlp)
    mlp_in = lax.all_to_all(
        jnp.broadcast_to(mlp_own[None], (kv_count,) + mlp_own.shape), KV, 0, 0, tiled=True
    ).reshape(kv_count * rows * steps, width)
    gate = jnp.dot(mlp_in, w_gate, preferred_element_type=jnp.float32)
    upward = jnp.dot(mlp_in, w_up, preferred_element_type=jnp.float32)
    hidden = (jax.nn.gelu(gate, approximate=True) * upward).astype(jnp.bfloat16)
    own_row = jnp.arange(kv_count * rows * steps, dtype=jnp.int32)
    select = (
        (own_row[:, None] // (rows * steps) == member)
        & (own_row[:, None] % (rows * steps) == jnp.arange(rows * steps, dtype=jnp.int32)[None, :])
    ).astype(jnp.bfloat16)
    terms = jnp.dot(
        jnp.concatenate([hidden, select], axis=1),
        jnp.concatenate([w_down, by_req], axis=0),
        preferred_element_type=jnp.float32,
    ).astype(jnp.bfloat16)

    leaving = terms
    arrived_sums = lax.all_to_all(leaving, KV + ("req",), 0, 0, tiled=True).reshape(
        kv_count, req_count, steps, width
    )
    per_group_sum = jnp.sum(arrived_sums.astype(jnp.float32), axis=0)
    served_by = slot_req[:, half, :] == group
    finished = jnp.sum(
        jnp.where(served_by[:, None, :, None], per_group_sum[:, :, None, :], 0.0), axis=0
    )
    return finished.astype(jnp.bfloat16)


def solution(mesh):
    req_count, kv_count = mesh.devices.shape
    halves = kv_count // BEAMS
    split = Mesh(
        mesh.devices.reshape(req_count, BEAMS // 2, halves, 2), ("req",) + KV
    )
    mesh = split
    ROWS = ("req",) + KV
    in_specs = (
        P(None, ROWS, None),
        P(),
        P(),
        P(),
        P(ROWS, None),
        P(ROWS, None, None),
        P(),
        P(),
        P(),
        P(),
        P(),
        P(None, KV),
        P(None, KV),
        P(KV, None),
    )
    out_specs = P(None, ROWS, None)
    return jax.shard_map(
        on_device, mesh=mesh, in_specs=in_specs, out_specs=out_specs, check_vma=False
    )
```

```python
import jax
import jax.numpy as jnp
from jax import lax
from jax.sharding import Mesh, PartitionSpec as P
from jax.experimental import pallas as pl
from jax.experimental.pallas import tpu as pltpu

WINDOW = 1024
PAGE = 128
BEAMS = 8


EPSILON = 1e-06
KV = ("y", "zhi", "zlo")
HALF = ("y", "zlo")
NEGATIVE = -1e30


def member_of(beam_index, half_index, halves):
    return beam_index % 2 + 2 * half_index + 2 * halves * (beam_index // 2)


def rms_round(values, gain):
    wide = values.astype(jnp.float32)
    mean_square = jnp.mean(wide * wide, axis=-1, keepdims=True)
    return (wide * lax.rsqrt(mean_square + EPSILON) * gain).astype(jnp.bfloat16)


def rank_within(labels, offsets):
    earlier = (labels[None, :] == labels[:, None]) & (offsets[None, :] < offsets[:, None])
    return jnp.sum(earlier.astype(jnp.int32), axis=1)


def follow(index, table):
    picks = index[:, None, :] == jnp.arange(BEAMS, dtype=jnp.int32)[None, :, None]
    return jnp.sum(jnp.where(picks, table[None, :, :], 0), axis=1)


def pick_by_row(index, table):
    picks = index.T[:, :, None] == jnp.arange(BEAMS, dtype=jnp.int32)[None, None, :]
    rows_first = jnp.swapaxes(table, 0, 1)
    return jnp.sum(
        jnp.where(picks[..., None], rows_first[:, None, :, :], 0), axis=2
    ).astype(table.dtype)


def pick_rows(index, table):
    picks = index[:, None, :] == jnp.arange(BEAMS, dtype=jnp.int32)[None, :, None]
    return jnp.sum(jnp.where(picks[..., None], table[None, :, :, :], 0), axis=1).astype(table.dtype)


def attend_kernel(bounds_ref, used_ref, q_ref, kv_ref, new_ref, pick_ref, out_ref):
    r = pl.program_id(0)
    steps = q_ref.shape[1]
    head_dim = q_ref.shape[3]
    scale = head_dim ** (-0.5)
    keys = kv_ref[0, :, :head_dim]
    values = kv_ref[0, :, head_dim:]
    pos = lax.broadcasted_iota(jnp.int32, (1, kv_ref.shape[1]), 1)
    contract = (((1,), (1,)), ((), ()))
    for t in range(steps):

        @pl.when(used_ref[r * steps + t] != 0)
        def _(t=t):
            lo = bounds_ref[(r * steps + t) * 2]
            hi = bounds_ref[(r * steps + t) * 2 + 1]
            query = q_ref[0, t]
            scores = lax.dot_general(query, keys, contract, preferred_element_type=jnp.float32) * scale
            allowed = (pos > lo) & (pos < hi)
            scores = jnp.where(allowed, scores, NEGATIVE)
            high_c = jnp.max(scores, axis=1, keepdims=True)
            weights = jnp.exp(scores - high_c).astype(jnp.bfloat16)
            total_c = jnp.sum(weights.astype(jnp.float32), axis=1, keepdims=True)
            sum_c = jnp.dot(weights, values, preferred_element_type=jnp.float32)
            entries = new_ref[0, t]
            fresh = lax.dot_general(
                query, entries[:, :head_dim], contract, preferred_element_type=jnp.float32
            ) * scale
            fresh = jnp.where(pick_ref[t] > 0, fresh, NEGATIVE)
            high_n = jnp.max(fresh, axis=1, keepdims=True)
            fresh_w = jnp.exp(fresh - high_n).astype(jnp.bfloat16)
            total_n = jnp.sum(fresh_w.astype(jnp.float32), axis=1, keepdims=True)
            sum_n = jnp.dot(fresh_w, entries[:, head_dim:], preferred_element_type=jnp.float32)
            highest = jnp.maximum(high_c, high_n)
            scale_c = jnp.exp(high_c - highest)
            scale_n = jnp.exp(high_n - highest)
            totals = total_c * scale_c + total_n * scale_n
            weighted = sum_c * scale_c + sum_n * scale_n
            attended = weighted / totals
            for h in range(out_ref.shape[3] // head_dim):
                out_ref[0, t, :, h * head_dim : (h + 1) * head_dim] = attended[
                    h * out_ref.shape[2] : (h + 1) * out_ref.shape[2]
                ].astype(out_ref.dtype)

        @pl.when(used_ref[r * steps + t] == 0)
        def _(t=t):
            out_ref[0, t] = jnp.zeros(out_ref.shape[2:], out_ref.dtype)


def attend(bounds, used, queries, pages, entries, pick):
    rows, steps, count, head_dim = queries.shape
    out_rows = BEAMS
    out_width = count // BEAMS * head_dim
    span = pages.shape[1]
    flops = 4 * rows * steps * count * (span + entries.shape[2]) * head_dim
    return pl.pallas_call(
        attend_kernel,
        grid_spec=pltpu.PrefetchScalarGridSpec(
            num_scalar_prefetch=2,
            grid=(rows,),
            in_specs=[
                pl.BlockSpec((1, steps, count, head_dim), lambda r, b, u: (r, 0, 0, 0)),
                pl.BlockSpec((1, span, pages.shape[2]), lambda r, b, u: (r, 0, 0)),
                pl.BlockSpec((1,) + entries.shape[1:], lambda r, b, u: (r, 0, 0, 0)),
                pl.BlockSpec(pick.shape, lambda r, b, u: (0, 0, 0)),
            ],
            out_specs=pl.BlockSpec((1, steps, out_rows, out_width), lambda r, b, u: (r, 0, 0, 0)),
        ),
        out_shape=jax.ShapeDtypeStruct((rows, steps, out_rows, out_width), jnp.bfloat16),
        cost_estimate=pl.CostEstimate(
            flops=flops,
            transcendentals=rows * steps * count * span,
            bytes_accessed=pages.size * 2 + queries.size * 4 + entries.size * 2,
        ),
    )(bounds, used, queries, pages, entries, pick)


def on_device(
    x_steps,
    lengths,
    perm,
    parents,
    table,
    pool,
    norm_attn,
    w_query,
    w_keyval,
    w_out,
    norm_mlp,
    w_gate,
    w_up,
    w_down,
):
    steps, rows, width = x_steps.shape
    head_dim = pool.shape[2] // 2
    heads = w_query.shape[1] // head_dim
    qwidth = heads * head_dim
    span = table.shape[1] * pool.shape[1]
    req_count = lax.axis_size("req")
    kv_count = lax.axis_size(KV)
    group = lax.axis_index("req")
    halves = lax.axis_size("zhi")
    half = lax.axis_index("zhi")
    beam = lax.axis_index("y") * 2 + lax.axis_index("zlo")
    member = member_of(beam, half, halves)
    per_group = halves * rows
    group_rows = kv_count * rows
    quota = rows // req_count

    offsets = jnp.arange(rows, dtype=jnp.int32)
    slot_ids = group * per_group + half * rows + offsets
    placed = lax.dynamic_slice_in_dim(perm.reshape(req_count, per_group), half * rows, rows, 1)
    serving = lax.dynamic_index_in_dim(placed, group, 0, keepdims=False)
    target = jnp.sum(
        jnp.where(placed == slot_ids[None, :], jnp.arange(req_count, dtype=jnp.int32)[:, None], 0),
        axis=0,
    )
    anchor = serving // per_group
    send_slot = jnp.sum(
        jnp.where(target[None, :] == offsets[:, None], offsets[None, :], 0), axis=1
    )
    outgoing = jnp.take(x_steps, send_slot, axis=1).reshape(steps, req_count, quota, width)
    arrived = lax.all_to_all(outgoing, "req", split_axis=1, concat_axis=1, tiled=True).reshape(
        steps, rows, width
    )
    slot_req = perm.reshape(req_count, halves, rows) // (halves * rows)
    mine_req = slot_req[:, half, :][group]
    offset_of = jnp.sum(
        jnp.where(mine_req[None, :] == offsets[:, None], offsets[None, :], 0), axis=1
    )
    inputs = arrived

    normed = rms_round(inputs.reshape(steps * rows, width), norm_attn)
    query = jnp.dot(normed, w_query, preferred_element_type=jnp.float32).astype(jnp.bfloat16)
    fresh = jnp.dot(normed, w_keyval, preferred_element_type=jnp.float32).astype(jnp.bfloat16)
    packed = jnp.concatenate([query, fresh], axis=-1).reshape(steps, rows, qwidth + 2 * head_dim)
    mine = lax.all_to_all(
        jnp.broadcast_to(packed[None], (BEAMS,) + packed.shape), HALF, 0, 0, tiled=True
    )
    queries = mine[..., :qwidth].reshape(BEAMS, steps, rows, heads, head_dim)
    entries = mine[..., qwidth:]

    family = lax.dynamic_slice_in_dim(parents, group * group_rows, group_rows, 1).reshape(
        (steps, BEAMS // 2, halves, 2, rows)
    )
    family = lax.dynamic_index_in_dim(family, half, 2, keepdims=False).reshape(steps, BEAMS, rows)
    family = family[:, :, offset_of]
    own = jnp.broadcast_to(jnp.arange(BEAMS, dtype=jnp.int32)[:, None], (BEAMS, rows))
    cache_beam = own
    sources = []
    cache_beams = []
    listed = []
    for step_index in range(steps):
        cache_beam = follow(family[step_index], cache_beam)
        sources = [follow(family[step_index], source) for source in sources] + [own]
        cache_beams.append(cache_beam)
        picked = [pick_by_row(source, entries[:, s]) for s, source in enumerate(sources)]
        picked += [jnp.zeros_like(picked[0])] * (steps - 1 - step_index)
        listed.append(jnp.stack(picked, axis=1))
    held = jnp.stack(cache_beams, axis=1) == beam
    listed = jnp.stack(listed, axis=1)

    length = lengths[serving[offset_of]]
    first_page = jnp.maximum(length - WINDOW + 1, 0) // PAGE
    device = group * kv_count + member
    pages = pool[table[offset_of] - device * pool.shape[0]].reshape(rows, span, 2 * head_dim)
    scale = head_dim ** (-0.5)
    step_ids = jnp.arange(steps, dtype=jnp.int32)
    base = first_page * PAGE
    lo = length[:, None] + step_ids[None, :] - WINDOW - base[:, None]
    hi = jnp.broadcast_to((length - base)[:, None], (rows, steps))
    bounds = jnp.stack([lo, hi], axis=-1).reshape(rows * steps * 2)
    by_row = jnp.transpose(queries, (2, 1, 3, 0, 4)).reshape(rows, steps, heads * BEAMS, head_dim)
    entries_by_row = listed.reshape(rows, steps, steps * BEAMS, 2 * head_dim)
    row_beam = jnp.arange(BEAMS * heads, dtype=jnp.int32) % BEAMS
    column = jnp.arange(steps * BEAMS, dtype=jnp.int32)
    pick = (
        (column[None, None, :] % BEAMS == row_beam[None, :, None])
        & (column[None, None, :] // BEAMS <= step_ids[:, None, None])
    ).astype(jnp.float32)
    used = jnp.any(held, axis=0).T.astype(jnp.int32).reshape(rows * steps)
    attended = attend(bounds, used, by_row, pages, entries_by_row, pick)
    attended = jnp.transpose(attended, (2, 1, 0, 3))
    attended = jnp.where(held[..., None], attended, jnp.zeros_like(attended))

    received = lax.all_to_all(attended, HALF, split_axis=0, concat_axis=0, tiled=True)
    attended_own = jnp.sum(received.astype(jnp.float32), axis=0).astype(jnp.bfloat16)

    current = inputs.reshape(steps * rows, width)
    residual = (
        current.astype(jnp.float32)
        + jnp.dot(attended_own.reshape(steps * rows, qwidth), w_out, preferred_element_type=jnp.float32)
    ).astype(jnp.bfloat16)
    by_req = jnp.swapaxes(residual.reshape(steps, rows, width), 0, 1).reshape(rows * steps, width)
    mlp_own = rms_round(by_req, norm_mlp)
    mlp_in = lax.all_to_all(
        jnp.broadcast_to(mlp_own[None], (kv_count,) + mlp_own.shape), KV, 0, 0, tiled=True
    ).reshape(kv_count * rows * steps, width)
    gate = jnp.dot(mlp_in, w_gate, preferred_element_type=jnp.float32)
    upward = jnp.dot(mlp_in, w_up, preferred_element_type=jnp.float32)
    hidden = (jax.nn.gelu(gate, approximate=True) * upward).astype(jnp.bfloat16)
    own_row = jnp.arange(kv_count * rows * steps, dtype=jnp.int32)
    select = (
        (own_row[:, None] // (rows * steps) == member)
        & (own_row[:, None] % (rows * steps) == jnp.arange(rows * steps, dtype=jnp.int32)[None, :])
    ).astype(jnp.bfloat16)
    terms = jnp.dot(
        jnp.concatenate([hidden, select], axis=1),
        jnp.concatenate([w_down, by_req], axis=0),
        preferred_element_type=jnp.float32,
    ).astype(jnp.bfloat16)

    leaving = terms
    arrived_sums = lax.all_to_all(leaving, KV + ("req",), 0, 0, tiled=True).reshape(
        kv_count, req_count, steps, width
    )
    per_group_sum = jnp.sum(arrived_sums.astype(jnp.float32), axis=0)
    served_by = slot_req[:, half, :] == group
    finished = jnp.sum(
        jnp.where(served_by[:, None, :, None], per_group_sum[:, :, None, :], 0.0), axis=0
    )
    return finished.astype(jnp.bfloat16)


def solution(mesh):
    req_count, kv_count = mesh.devices.shape
    halves = kv_count // BEAMS
    split = Mesh(
        mesh.devices.reshape(req_count, BEAMS // 2, halves, 2), ("req",) + KV
    )
    mesh = split
    ROWS = ("req",) + KV
    in_specs = (
        P(None, ROWS, None),
        P(),
        P(),
        P(),
        P(ROWS, None),
        P(ROWS, None, None),
        P(),
        P(),
        P(),
        P(),
        P(),
        P(None, KV),
        P(None, KV),
        P(KV, None),
    )
    out_specs = P(None, ROWS, None)
    return jax.shard_map(
        on_device, mesh=mesh, in_specs=in_specs, out_specs=out_specs, check_vma=False
    )
```

```python
import jax
import jax.numpy as jnp
from jax import lax
from jax.sharding import Mesh, PartitionSpec as P
from jax.experimental import pallas as pl
from jax.experimental.pallas import tpu as pltpu

WINDOW = 1024
PAGE = 128
BEAMS = 8


EPSILON = 1e-06
KV = ("y", "zhi", "zlo")
HALF = ("y", "zlo")
NEGATIVE = -1e30


def member_of(beam_index, half_index, halves):
    return beam_index % 2 + 2 * half_index + 2 * halves * (beam_index // 2)


def rms_round(values, gain):
    wide = values.astype(jnp.float32)
    mean_square = jnp.mean(wide * wide, axis=-1, keepdims=True)
    return (wide * lax.rsqrt(mean_square + EPSILON) * gain).astype(jnp.bfloat16)


def rank_within(labels, offsets):
    earlier = (labels[None, :] == labels[:, None]) & (offsets[None, :] < offsets[:, None])
    return jnp.sum(earlier.astype(jnp.int32), axis=1)


def follow(index, table):
    picks = index[:, None, :] == jnp.arange(BEAMS, dtype=jnp.int32)[None, :, None]
    return jnp.sum(jnp.where(picks, table[None, :, :], 0), axis=1)


def pick_by_row(index, table):
    picks = index.T[:, :, None] == jnp.arange(BEAMS, dtype=jnp.int32)[None, None, :]
    rows_first = jnp.swapaxes(table, 0, 1)
    return jnp.sum(
        jnp.where(picks[..., None], rows_first[:, None, :, :], 0), axis=2
    ).astype(table.dtype)


def pick_rows(index, table):
    picks = index[:, None, :] == jnp.arange(BEAMS, dtype=jnp.int32)[None, :, None]
    return jnp.sum(jnp.where(picks[..., None], table[None, :, :, :], 0), axis=1).astype(table.dtype)


def attend_kernel(bounds_ref, used_ref, q_ref, kv_ref, new_ref, pick_ref, out_ref):
    r = pl.program_id(0)
    steps = q_ref.shape[1]
    head_dim = q_ref.shape[3]
    scale = head_dim ** (-0.5)
    keys = kv_ref[0, :, :head_dim]
    values = kv_ref[0, :, head_dim:]
    pos = lax.broadcasted_iota(jnp.int32, (1, kv_ref.shape[1]), 1)
    contract = (((1,), (1,)), ((), ()))
    for t in range(steps):

        @pl.when(used_ref[r * steps + t] != 0)
        def _(t=t):
            lo = bounds_ref[(r * steps + t) * 2]
            hi = bounds_ref[(r * steps + t) * 2 + 1]
            query = q_ref[0, t]
            scores = lax.dot_general(query, keys, contract, preferred_element_type=jnp.float32) * scale
            allowed = (pos > lo) & (pos < hi)
            scores = jnp.where(allowed, scores, NEGATIVE)
            high_c = jnp.max(scores, axis=1, keepdims=True)
            weights = jnp.exp(scores - high_c).astype(jnp.bfloat16)
            total_c = jnp.sum(weights.astype(jnp.float32), axis=1, keepdims=True)
            sum_c = jnp.dot(weights, values, preferred_element_type=jnp.float32)
            entries = new_ref[0, t]
            fresh = lax.dot_general(
                query, entries[:, :head_dim], contract, preferred_element_type=jnp.float32
            ) * scale
            fresh = jnp.where(pick_ref[t] > 0, fresh, NEGATIVE)
            high_n = jnp.max(fresh, axis=1, keepdims=True)
            fresh_w = jnp.exp(fresh - high_n).astype(jnp.bfloat16)
            total_n = jnp.sum(fresh_w.astype(jnp.float32), axis=1, keepdims=True)
            sum_n = jnp.dot(fresh_w, entries[:, head_dim:], preferred_element_type=jnp.float32)
            highest = jnp.maximum(high_c, high_n)
            scale_c = jnp.exp(high_c - highest)
            scale_n = jnp.exp(high_n - highest)
            totals = total_c * scale_c + total_n * scale_n
            weighted = sum_c * scale_c + sum_n * scale_n
            attended = weighted / totals
            for h in range(out_ref.shape[3] // head_dim):
                out_ref[0, t, :, h * head_dim : (h + 1) * head_dim] = attended[
                    h * out_ref.shape[2] : (h + 1) * out_ref.shape[2]
                ].astype(out_ref.dtype)

        @pl.when(used_ref[r * steps + t] == 0)
        def _(t=t):
            out_ref[0, t] = jnp.zeros(out_ref.shape[2:], out_ref.dtype)


def attend(bounds, used, queries, pages, entries, pick):
    rows, steps, count, head_dim = queries.shape
    out_rows = BEAMS
    out_width = count // BEAMS * head_dim
    span = pages.shape[1]
    flops = 4 * rows * steps * count * (span + entries.shape[2]) * head_dim
    return pl.pallas_call(
        attend_kernel,
        grid_spec=pltpu.PrefetchScalarGridSpec(
            num_scalar_prefetch=2,
            grid=(rows,),
            in_specs=[
                pl.BlockSpec((1, steps, count, head_dim), lambda r, b, u: (r, 0, 0, 0)),
                pl.BlockSpec((1, span, pages.shape[2]), lambda r, b, u: (r, 0, 0)),
                pl.BlockSpec((1,) + entries.shape[1:], lambda r, b, u: (r, 0, 0, 0)),
                pl.BlockSpec(pick.shape, lambda r, b, u: (0, 0, 0)),
            ],
            out_specs=pl.BlockSpec((1, steps, out_rows, out_width), lambda r, b, u: (r, 0, 0, 0)),
        ),
        out_shape=jax.ShapeDtypeStruct((rows, steps, out_rows, out_width), jnp.bfloat16),
        cost_estimate=pl.CostEstimate(
            flops=flops,
            transcendentals=rows * steps * count * span,
            bytes_accessed=pages.size * 2 + queries.size * 4 + entries.size * 2,
        ),
    )(bounds, used, queries, pages, entries, pick)


def on_device(
    x_steps,
    lengths,
    perm,
    parents,
    table,
    pool,
    norm_attn,
    w_query,
    w_keyval,
    w_out,
    norm_mlp,
    w_gate,
    w_up,
    w_down,
):
    steps, rows, width = x_steps.shape
    head_dim = pool.shape[2] // 2
    heads = w_query.shape[1] // head_dim
    qwidth = heads * head_dim
    span = table.shape[1] * pool.shape[1]
    req_count = lax.axis_size("req")
    kv_count = lax.axis_size(KV)
    group = lax.axis_index("req")
    halves = lax.axis_size("zhi")
    half = lax.axis_index("zhi")
    beam = lax.axis_index("y") * 2 + lax.axis_index("zlo")
    member = member_of(beam, half, halves)
    per_group = halves * rows
    group_rows = kv_count * rows
    quota = rows // req_count

    offsets = jnp.arange(rows, dtype=jnp.int32)
    slot_ids = group * per_group + half * rows + offsets
    placed = lax.dynamic_slice_in_dim(perm.reshape(req_count, per_group), half * rows, rows, 1)
    serving = lax.dynamic_index_in_dim(placed, group, 0, keepdims=False)
    target = jnp.sum(
        jnp.where(placed == slot_ids[None, :], jnp.arange(req_count, dtype=jnp.int32)[:, None], 0),
        axis=0,
    )
    anchor = serving // per_group
    send_slot = jnp.sum(
        jnp.where(target[None, :] == offsets[:, None], offsets[None, :], 0), axis=1
    )
    outgoing = jnp.take(x_steps, send_slot, axis=1).reshape(steps, req_count, quota, width)
    arrived = lax.all_to_all(outgoing, "req", split_axis=1, concat_axis=1, tiled=True).reshape(
        steps, rows, width
    )
    slot_req = perm.reshape(req_count, halves, rows) // (halves * rows)
    mine_req = slot_req[:, half, :][group]
    offset_of = jnp.sum(
        jnp.where(mine_req[None, :] == offsets[:, None], offsets[None, :], 0), axis=1
    )
    inputs = arrived

    normed = rms_round(inputs.reshape(steps * rows, width), norm_attn)
    query = jnp.dot(normed, w_query, preferred_element_type=jnp.float32).astype(jnp.bfloat16)
    fresh = jnp.dot(normed, w_keyval, preferred_element_type=jnp.float32).astype(jnp.bfloat16)
    packed = jnp.concatenate([query, fresh], axis=-1).reshape(steps, rows, qwidth + 2 * head_dim)
    mine = lax.all_to_all(
        jnp.broadcast_to(packed[None], (BEAMS,) + packed.shape), HALF, 0, 0, tiled=True
    )
    queries = mine[..., :qwidth].reshape(BEAMS, steps, rows, heads, head_dim)
    entries = mine[..., qwidth:]

    family = lax.dynamic_slice_in_dim(parents, group * group_rows, group_rows, 1).reshape(
        (steps, BEAMS // 2, halves, 2, rows)
    )
    family = lax.dynamic_index_in_dim(family, half, 2, keepdims=False).reshape(steps, BEAMS, rows)
    family = family[:, :, offset_of]
    own = jnp.broadcast_to(jnp.arange(BEAMS, dtype=jnp.int32)[:, None], (BEAMS, rows))
    cache_beam = own
    sources = []
    cache_beams = []
    listed = []
    for step_index in range(steps):
        cache_beam = follow(family[step_index], cache_beam)
        sources = [follow(family[step_index], source) for source in sources] + [own]
        cache_beams.append(cache_beam)
        listed.append(jnp.stack(sources + [jnp.full_like(own, -1)] * (steps - 1 - step_index)))
    held = jnp.stack(cache_beams, axis=1) == beam
    source_of = jnp.transpose(jnp.stack(listed), (3, 0, 1, 2))
    chosen = source_of[..., None] == jnp.arange(BEAMS, dtype=jnp.int32)
    by_source = jnp.transpose(entries, (2, 1, 0, 3))
    listed = jnp.sum(
        jnp.where(chosen[..., None], by_source[:, None, :, None, :, :], 0), axis=4
    ).astype(entries.dtype)

    length = lengths[serving[offset_of]]
    first_page = jnp.maximum(length - WINDOW + 1, 0) // PAGE
    device = group * kv_count + member
    pages = pool[table[offset_of] - device * pool.shape[0]].reshape(rows, span, 2 * head_dim)
    scale = head_dim ** (-0.5)
    step_ids = jnp.arange(steps, dtype=jnp.int32)
    base = first_page * PAGE
    lo = length[:, None] + step_ids[None, :] - WINDOW - base[:, None]
    hi = jnp.broadcast_to((length - base)[:, None], (rows, steps))
    bounds = jnp.stack([lo, hi], axis=-1).reshape(rows * steps * 2)
    by_row = jnp.transpose(queries, (2, 1, 3, 0, 4)).reshape(rows, steps, heads * BEAMS, head_dim)
    entries_by_row = listed.reshape(rows, steps, steps * BEAMS, 2 * head_dim)
    row_beam = jnp.arange(BEAMS * heads, dtype=jnp.int32) % BEAMS
    column = jnp.arange(steps * BEAMS, dtype=jnp.int32)
    pick = (
        (column[None, None, :] % BEAMS == row_beam[None, :, None])
        & (column[None, None, :] // BEAMS <= step_ids[:, None, None])
    ).astype(jnp.float32)
    used = jnp.any(held, axis=0).T.astype(jnp.int32).reshape(rows * steps)
    attended = attend(bounds, used, by_row, pages, entries_by_row, pick)
    attended = jnp.transpose(attended, (2, 1, 0, 3))
    attended = jnp.where(held[..., None], attended, jnp.zeros_like(attended))

    received = lax.all_to_all(attended, HALF, split_axis=0, concat_axis=0, tiled=True)
    attended_own = jnp.sum(received.astype(jnp.float32), axis=0).astype(jnp.bfloat16)

    current = inputs.reshape(steps * rows, width)
    residual = (
        current.astype(jnp.float32)
        + jnp.dot(attended_own.reshape(steps * rows, qwidth), w_out, preferred_element_type=jnp.float32)
    ).astype(jnp.bfloat16)
    by_req = jnp.swapaxes(residual.reshape(steps, rows, width), 0, 1).reshape(rows * steps, width)
    mlp_own = rms_round(by_req, norm_mlp)
    mlp_in = lax.all_to_all(
        jnp.broadcast_to(mlp_own[None], (kv_count,) + mlp_own.shape), KV, 0, 0, tiled=True
    ).reshape(kv_count * rows * steps, width)
    gate = jnp.dot(mlp_in, w_gate, preferred_element_type=jnp.float32)
    upward = jnp.dot(mlp_in, w_up, preferred_element_type=jnp.float32)
    hidden = (jax.nn.gelu(gate, approximate=True) * upward).astype(jnp.bfloat16)
    own_row = jnp.arange(kv_count * rows * steps, dtype=jnp.int32)
    select = (
        (own_row[:, None] // (rows * steps) == member)
        & (own_row[:, None] % (rows * steps) == jnp.arange(rows * steps, dtype=jnp.int32)[None, :])
    ).astype(jnp.bfloat16)
    terms = jnp.dot(
        jnp.concatenate([hidden, select], axis=1),
        jnp.concatenate([w_down, by_req], axis=0),
        preferred_element_type=jnp.float32,
    ).astype(jnp.bfloat16)

    leaving = terms
    arrived_sums = lax.all_to_all(leaving, KV + ("req",), 0, 0, tiled=True).reshape(
        kv_count, req_count, steps, width
    )
    per_group_sum = jnp.sum(arrived_sums.astype(jnp.float32), axis=0)
    served_by = slot_req[:, half, :] == group
    finished = jnp.sum(
        jnp.where(served_by[:, None, :, None], per_group_sum[:, :, None, :], 0.0), axis=0
    )
    return finished.astype(jnp.bfloat16)


def solution(mesh):
    req_count, kv_count = mesh.devices.shape
    halves = kv_count // BEAMS
    split = Mesh(
        mesh.devices.reshape(req_count, BEAMS // 2, halves, 2), ("req",) + KV
    )
    mesh = split
    ROWS = ("req",) + KV
    in_specs = (
        P(None, ROWS, None),
        P(),
        P(),
        P(),
        P(ROWS, None),
        P(ROWS, None, None),
        P(),
        P(),
        P(),
        P(),
        P(),
        P(None, KV),
        P(None, KV),
        P(KV, None),
    )
    out_specs = P(None, ROWS, None)
    return jax.shard_map(
        on_device, mesh=mesh, in_specs=in_specs, out_specs=out_specs, check_vma=False
    )
```

```python
import jax
import jax.numpy as jnp
from jax import lax
from jax.sharding import Mesh, PartitionSpec as P
from jax.experimental import pallas as pl
from jax.experimental.pallas import tpu as pltpu

WINDOW = 1024
PAGE = 128
BEAMS = 8


EPSILON = 1e-06
KV = ("y", "zhi", "zlo")
HALF = ("y", "zlo")
NEGATIVE = -1e30


def member_of(beam_index, half_index, halves):
    return beam_index % 2 + 2 * half_index + 2 * halves * (beam_index // 2)


def rms_round(values, gain):
    wide = values.astype(jnp.float32)
    mean_square = jnp.mean(wide * wide, axis=-1, keepdims=True)
    return (wide * lax.rsqrt(mean_square + EPSILON) * gain).astype(jnp.bfloat16)


def rank_within(labels, offsets):
    earlier = (labels[None, :] == labels[:, None]) & (offsets[None, :] < offsets[:, None])
    return jnp.sum(earlier.astype(jnp.int32), axis=1)


def follow(index, table):
    picks = index[:, None, :] == jnp.arange(BEAMS, dtype=jnp.int32)[None, :, None]
    return jnp.sum(jnp.where(picks, table[None, :, :], 0), axis=1)


def pick_by_row(index, table):
    picks = index.T[:, :, None] == jnp.arange(BEAMS, dtype=jnp.int32)[None, None, :]
    rows_first = jnp.swapaxes(table, 0, 1)
    return jnp.sum(
        jnp.where(picks[..., None], rows_first[:, None, :, :], 0), axis=2
    ).astype(table.dtype)


def pick_rows(index, table):
    picks = index[:, None, :] == jnp.arange(BEAMS, dtype=jnp.int32)[None, :, None]
    return jnp.sum(jnp.where(picks[..., None], table[None, :, :, :], 0), axis=1).astype(table.dtype)


def attend_kernel(bounds_ref, used_ref, q_ref, kv_ref, new_ref, pick_ref, out_ref):
    r = pl.program_id(0)
    steps = q_ref.shape[1]
    head_dim = q_ref.shape[3]
    scale = head_dim ** (-0.5)
    keys = kv_ref[0, :, :head_dim]
    values = kv_ref[0, :, head_dim:]
    pos = lax.broadcasted_iota(jnp.int32, (1, kv_ref.shape[1]), 1)
    contract = (((1,), (1,)), ((), ()))
    for t in range(steps):

        @pl.when(used_ref[r * steps + t] != 0)
        def _(t=t):
            lo = bounds_ref[(r * steps + t) * 2]
            hi = bounds_ref[(r * steps + t) * 2 + 1]
            query = q_ref[0, t]
            scores = lax.dot_general(query, keys, contract, preferred_element_type=jnp.float32) * scale
            allowed = (pos > lo) & (pos < hi)
            scores = jnp.where(allowed, scores, NEGATIVE)
            high_c = jnp.max(scores, axis=1, keepdims=True)
            weights = jnp.exp(scores - high_c).astype(jnp.bfloat16)
            total_c = jnp.sum(weights.astype(jnp.float32), axis=1, keepdims=True)
            sum_c = jnp.dot(weights, values, preferred_element_type=jnp.float32)
            entries = new_ref[0, t]
            fresh = lax.dot_general(
                query, entries[:, :head_dim], contract, preferred_element_type=jnp.float32
            ) * scale
            fresh = jnp.where(pick_ref[t] > 0, fresh, NEGATIVE)
            high_n = jnp.max(fresh, axis=1, keepdims=True)
            fresh_w = jnp.exp(fresh - high_n).astype(jnp.bfloat16)
            total_n = jnp.sum(fresh_w.astype(jnp.float32), axis=1, keepdims=True)
            sum_n = jnp.dot(fresh_w, entries[:, head_dim:], preferred_element_type=jnp.float32)
            highest = jnp.maximum(high_c, high_n)
            scale_c = jnp.exp(high_c - highest)
            scale_n = jnp.exp(high_n - highest)
            totals = total_c * scale_c + total_n * scale_n
            weighted = sum_c * scale_c + sum_n * scale_n
            attended = weighted / totals
            for h in range(out_ref.shape[3] // head_dim):
                out_ref[0, t, :, h * head_dim : (h + 1) * head_dim] = attended[
                    h * out_ref.shape[2] : (h + 1) * out_ref.shape[2]
                ].astype(out_ref.dtype)

        @pl.when(used_ref[r * steps + t] == 0)
        def _(t=t):
            out_ref[0, t] = jnp.zeros(out_ref.shape[2:], out_ref.dtype)


def attend(bounds, used, queries, pages, entries, pick):
    rows, steps, count, head_dim = queries.shape
    out_rows = BEAMS
    out_width = count // BEAMS * head_dim
    span = pages.shape[1]
    flops = 4 * rows * steps * count * (span + entries.shape[2]) * head_dim
    return pl.pallas_call(
        attend_kernel,
        grid_spec=pltpu.PrefetchScalarGridSpec(
            num_scalar_prefetch=2,
            grid=(rows,),
            in_specs=[
                pl.BlockSpec((1, steps, count, head_dim), lambda r, b, u: (r, 0, 0, 0)),
                pl.BlockSpec((1, span, pages.shape[2]), lambda r, b, u: (r, 0, 0)),
                pl.BlockSpec((1,) + entries.shape[1:], lambda r, b, u: (r, 0, 0, 0)),
                pl.BlockSpec(pick.shape, lambda r, b, u: (0, 0, 0)),
            ],
            out_specs=pl.BlockSpec((1, steps, out_rows, out_width), lambda r, b, u: (r, 0, 0, 0)),
        ),
        out_shape=jax.ShapeDtypeStruct((rows, steps, out_rows, out_width), jnp.bfloat16),
        cost_estimate=pl.CostEstimate(
            flops=flops,
            transcendentals=rows * steps * count * span,
            bytes_accessed=pages.size * 2 + queries.size * 4 + entries.size * 2,
        ),
    )(bounds, used, queries, pages, entries, pick)


def on_device(
    x_steps,
    lengths,
    perm,
    parents,
    table,
    pool,
    norm_attn,
    w_query,
    w_keyval,
    w_out,
    norm_mlp,
    w_gate,
    w_up,
    w_down,
):
    steps, rows, width = x_steps.shape
    head_dim = pool.shape[2] // 2
    heads = w_query.shape[1] // head_dim
    qwidth = heads * head_dim
    span = table.shape[1] * pool.shape[1]
    req_count = lax.axis_size("req")
    kv_count = lax.axis_size(KV)
    group = lax.axis_index("req")
    halves = lax.axis_size("zhi")
    half = lax.axis_index("zhi")
    beam = lax.axis_index("y") * 2 + lax.axis_index("zlo")
    member = member_of(beam, half, halves)
    per_group = halves * rows
    group_rows = kv_count * rows
    quota = rows // req_count

    offsets = jnp.arange(rows, dtype=jnp.int32)
    slot_ids = group * per_group + half * rows + offsets
    placed = lax.dynamic_slice_in_dim(perm.reshape(req_count, per_group), half * rows, rows, 1)
    serving = lax.dynamic_index_in_dim(placed, group, 0, keepdims=False)
    target = jnp.sum(
        jnp.where(placed == slot_ids[None, :], jnp.arange(req_count, dtype=jnp.int32)[:, None], 0),
        axis=0,
    )
    anchor = serving // per_group
    send_slot = jnp.sum(
        jnp.where(target[None, :] == offsets[:, None], offsets[None, :], 0), axis=1
    )
    outgoing = jnp.take(x_steps, send_slot, axis=1).reshape(steps, req_count, quota, width)
    arrived = lax.all_to_all(outgoing, "req", split_axis=1, concat_axis=1, tiled=True).reshape(
        steps, rows, width
    )
    slot_req = perm.reshape(req_count, halves, rows) // (halves * rows)
    mine_req = slot_req[:, half, :][group]
    offset_of = jnp.sum(
        jnp.where(mine_req[None, :] == offsets[:, None], offsets[None, :], 0), axis=1
    )
    inputs = arrived

    normed = rms_round(inputs.reshape(steps * rows, width), norm_attn)
    query = jnp.dot(normed, w_query, preferred_element_type=jnp.float32).astype(jnp.bfloat16)
    fresh = jnp.dot(normed, w_keyval, preferred_element_type=jnp.float32).astype(jnp.bfloat16)
    packed = jnp.concatenate([query, fresh], axis=-1).reshape(steps, rows, qwidth + 2 * head_dim)
    mine = lax.all_to_all(
        jnp.broadcast_to(packed[None], (BEAMS,) + packed.shape), HALF, 0, 0, tiled=True
    )
    queries = mine[..., :qwidth].reshape(BEAMS, steps, rows, heads, head_dim)
    entries = mine[..., qwidth:]

    family = lax.dynamic_slice_in_dim(parents, group * group_rows, group_rows, 1).reshape(
        (steps, BEAMS // 2, halves, 2, rows)
    )
    family = lax.dynamic_index_in_dim(family, half, 2, keepdims=False).reshape(steps, BEAMS, rows)
    family = family[:, :, offset_of]
    own = jnp.broadcast_to(jnp.arange(BEAMS, dtype=jnp.int32)[:, None], (BEAMS, rows))
    cache_beam = own
    sources = []
    cache_beams = []
    listed = []
    for step_index in range(steps):
        cache_beam = follow(family[step_index], cache_beam)
        sources = [follow(family[step_index], source) for source in sources] + [own]
        cache_beams.append(cache_beam)
        picked = [pick_by_row(source, entries[:, s]) for s, source in enumerate(sources)]
        picked += [jnp.zeros_like(picked[0])] * (steps - 1 - step_index)
        listed.append(jnp.stack(picked, axis=1))
    held = jnp.stack(cache_beams, axis=1) == beam
    listed = jnp.stack(listed, axis=1)

    length = lengths[serving[offset_of]]
    first_page = jnp.maximum(length - WINDOW + 1, 0) // PAGE
    device = group * kv_count + member
    pages = pool[table[offset_of] - device * pool.shape[0]].reshape(rows, span, 2 * head_dim)
    scale = head_dim ** (-0.5)
    step_ids = jnp.arange(steps, dtype=jnp.int32)
    base = first_page * PAGE
    lo = length[:, None] + step_ids[None, :] - WINDOW - base[:, None]
    hi = jnp.broadcast_to((length - base)[:, None], (rows, steps))
    bounds = jnp.stack([lo, hi], axis=-1).reshape(rows * steps * 2)
    by_row = jnp.transpose(queries, (2, 1, 3, 0, 4)).reshape(rows, steps, heads * BEAMS, head_dim)
    entries_by_row = listed.reshape(rows, steps, steps * BEAMS, 2 * head_dim)
    row_beam = jnp.arange(BEAMS * heads, dtype=jnp.int32) % BEAMS
    column = jnp.arange(steps * BEAMS, dtype=jnp.int32)
    pick = (
        (column[None, None, :] % BEAMS == row_beam[None, :, None])
        & (column[None, None, :] // BEAMS <= step_ids[:, None, None])
    ).astype(jnp.float32)
    used = jnp.any(held, axis=0).T.astype(jnp.int32).reshape(rows * steps)
    attended = attend(bounds, used, by_row, pages, entries_by_row, pick)
    attended = jnp.transpose(attended, (2, 1, 0, 3))

    received = lax.all_to_all(attended, HALF, split_axis=0, concat_axis=0, tiled=True)
    own_cache = lax.dynamic_index_in_dim(jnp.stack(cache_beams), beam, 1, keepdims=False)
    from_holder = own_cache[None] == jnp.arange(BEAMS, dtype=jnp.int32)[:, None, None]
    attended_own = jnp.sum(
        jnp.where(from_holder[..., None], received.astype(jnp.float32), 0.0), axis=0
    ).astype(jnp.bfloat16)

    current = inputs.reshape(steps * rows, width)
    residual = (
        current.astype(jnp.float32)
        + jnp.dot(attended_own.reshape(steps * rows, qwidth), w_out, preferred_element_type=jnp.float32)
    ).astype(jnp.bfloat16)
    by_req = jnp.swapaxes(residual.reshape(steps, rows, width), 0, 1).reshape(rows * steps, width)
    mlp_own = rms_round(by_req, norm_mlp)
    mlp_in = lax.all_to_all(
        jnp.broadcast_to(mlp_own[None], (kv_count,) + mlp_own.shape), KV, 0, 0, tiled=True
    ).reshape(kv_count * rows * steps, width)
    gate = jnp.dot(mlp_in, w_gate, preferred_element_type=jnp.float32)
    upward = jnp.dot(mlp_in, w_up, preferred_element_type=jnp.float32)
    hidden = (jax.nn.gelu(gate, approximate=True) * upward).astype(jnp.bfloat16)
    own_row = jnp.arange(kv_count * rows * steps, dtype=jnp.int32)
    select = (
        (own_row[:, None] // (rows * steps) == member)
        & (own_row[:, None] % (rows * steps) == jnp.arange(rows * steps, dtype=jnp.int32)[None, :])
    ).astype(jnp.bfloat16)
    terms = jnp.dot(
        jnp.concatenate([hidden, select], axis=1),
        jnp.concatenate([w_down, by_req], axis=0),
        preferred_element_type=jnp.float32,
    ).astype(jnp.bfloat16)

    leaving = terms
    arrived_sums = lax.all_to_all(leaving, KV + ("req",), 0, 0, tiled=True).reshape(
        kv_count, req_count, steps, width
    )
    per_group_sum = jnp.sum(arrived_sums.astype(jnp.float32), axis=0)
    served_by = slot_req[:, half, :] == group
    finished = jnp.sum(
        jnp.where(served_by[:, None, :, None], per_group_sum[:, :, None, :], 0.0), axis=0
    )
    return finished.astype(jnp.bfloat16)


def solution(mesh):
    req_count, kv_count = mesh.devices.shape
    halves = kv_count // BEAMS
    split = Mesh(
        mesh.devices.reshape(req_count, BEAMS // 2, halves, 2), ("req",) + KV
    )
    mesh = split
    ROWS = ("req",) + KV
    in_specs = (
        P(None, ROWS, None),
        P(),
        P(),
        P(),
        P(ROWS, None),
        P(ROWS, None, None),
        P(),
        P(),
        P(),
        P(),
        P(),
        P(None, KV),
        P(None, KV),
        P(KV, None),
    )
    out_specs = P(None, ROWS, None)
    return jax.shard_map(
        on_device, mesh=mesh, in_specs=in_specs, out_specs=out_specs, check_vma=False
    )
```
